32 devices in a mesh: dp: 2 (over core), ctx: 16 (over z, y, x).
Axes of the slice: x: 2, y: 2, z: 4, core: 2. Of those that a mesh axis runs over, the one named last changes fastest.
Arguments:
- tokens: bfloat16 [8192, 2880], P(('dp', 'ctx')), parts along dimension 0, may hold values from -6 to 6
- positions: int32 [8192], P(('dp', 'ctx')), parts along dimension 0, may hold values from 0 to 4223, as said below
- norm_gain: float32 [2880], replicated, may hold values from 0.5 to 1.5
- qkv_weight: bfloat16 [2880, 2560], P(None, 'ctx'), may hold values from -4 to 4
- qkv_bias: float32 [2560], replicated, may hold values from -3 to 3
- sinks: float32 [32], replicated, may hold values from 0 to 4
- earlier_keys: bfloat16 [256, 256], P('dp'), parts along dimension 0, may hold values from -6 to 6
- earlier_values: bfloat16 [256, 256], P('dp'), parts along dimension 0, may hold values from -6 to 6
Outputs:
- attended: bfloat16 [8192, 2048], P(('dp', 'ctx')), parts along dimension 0
The draws below stay inside these ranges and needn't reach their ends.
There are 2 independent parts, one for each index of `dp`. The reference program is written for one: setup_inputs(seed, part) draws one part's arguments, and reference() takes and returns one part's arrays. A program takes and returns all parts, laid end to end along the dimension named above; an argument that names none is the same for every part. Nothing has to cross between parts.
Inputs may be any that keep to these rules, and one draw needn't show every extreme that they name: Within each document positions rise by one from token to token and restart at 0 where the next document begins; the first token of the span continues a document of the previous span and has position 128 or more, so that the previous span's last 128 tokens belong to it; at least one document begins inside the span, and the token just before the first such start has position 4223.
All inputs are finite; a program needn't handle non-finite values.
Results may differ from the reference program's by a relative error of at most 0.0074.
Values may be sent and summed in bfloat16 or wider, within the bound.
No kernel may reach another device: no remote copies, remote signals or barrier semaphores. Data moves between devices by JAX's collectives and lax.ppermute only.
A program may use at most 64 MiB of HBM per device.

```python
import jax
import jax.numpy as jnp
from jax import lax

D = 2880
QUERY_HEADS = 32
KEY_VALUE_HEADS = 4
HEAD_SIZE = 64
WINDOW_TOKENS = 128
TOKENS = 4096
NCOL = 2560


def draw_positions(key, part):
    key_starts = jax.random.fold_in(key, 11)
    key_forced = jax.random.fold_in(key, 12)
    index = jnp.arange(TOKENS, dtype=jnp.int32)
    starts = jax.random.randint(key_starts, (TOKENS,), 0, 2048) == 0
    forced = jax.random.randint(key_forced, (), WINDOW_TOKENS, TOKENS)
    starts = (starts | (index == forced)) & (index > 0)
    first_start = jnp.min(jnp.where(starts, index, TOKENS))
    carried = TOKENS + WINDOW_TOKENS - first_start
    latest = lax.cummax(jnp.where(starts, index, -1), axis=0)
    return jnp.where(latest >= 0, index - latest, index + carried).astype(jnp.int32)


def draw_qkv_weight(key, part):
    weight = jax.random.truncated_normal(key, -6.0, 6.0, (D, NCOL), jnp.float32) * D ** (-0.5)
    return weight.astype(jnp.bfloat16)


def block_levels(rng, shape, cuts, low, high):
    level = 1.0
    for dim, parts in cuts:
        heights = jax.random.uniform(jax.random.fold_in(jax.random.fold_in(rng, 6), dim), (parts,), jnp.float32, low / len(cuts), high / len(cuts))
        level = level * jnp.repeat(jnp.exp(heights), shape[dim] // parts).reshape((-1,) + (1,) * (len(shape) - 1 - dim))
    return level


def gaussian(rng, dims, width, reach, pieces=(), kind=jnp.bfloat16):
    factor_of = block_levels(rng, dims, pieces, -0.22, 0.18) if pieces else 1.0
    result = jax.random.normal(rng, dims, jnp.float32) * width * factor_of
    return jnp.minimum(jnp.maximum(result, -reach), reach).astype(kind)


def setup_inputs(seed: int = 0, part: int = 0) -> dict:
    splits = jax.random.split(jax.random.key(seed), 9)
    part_splits = jax.random.split(jax.random.fold_in(splits[8], part), 9)
    tokens = gaussian(part_splits[0], (TOKENS, D), 1.0, 6.0, ((0, 16),))
    positions = draw_positions(jax.random.fold_in(jax.random.fold_in(splits[8], part), 71), part)
    norm_gain = jnp.clip(1.0 + 0.1 * jax.random.normal(splits[2], (D,), jnp.float32), 0.5, 1.5)
    qkv_weight = draw_qkv_weight(jax.random.fold_in(splits[8], 71), part)
    qkv_bias = gaussian(splits[4], (NCOL,), 0.5, 3.0, (), jnp.float32)
    sinks = jnp.clip(jax.random.uniform(splits[5], (QUERY_HEADS,), jnp.float32, 0.0, 4.0), 0.0, 4.0)
    earlier_keys = gaussian(part_splits[6], (WINDOW_TOKENS, KEY_VALUE_HEADS * HEAD_SIZE), 1.0, 6.0)
    earlier_values = gaussian(part_splits[7], (WINDOW_TOKENS, KEY_VALUE_HEADS * HEAD_SIZE), 1.0, 6.0)
    return dict(tokens=tokens, positions=positions, norm_gain=norm_gain, qkv_weight=qkv_weight, qkv_bias=qkv_bias, sinks=sinks, earlier_keys=earlier_keys, earlier_values=earlier_values)


def apply_rotation(heads, positions):
    half = heads.shape[-1] // 2
    freq = 150000.0 ** (-(jnp.arange(half, dtype=jnp.float32) * 2.0 / heads.shape[-1]))
    angle = positions.astype(jnp.float32)[:, None] * freq[None, :]
    cosine = jnp.cos(angle)[:, None, :]
    sine = jnp.sin(angle)[:, None, :]
    first = heads[..., :half]
    second = heads[..., half:]
    return jnp.concatenate([first * cosine - second * sine, second * cosine + first * sine], axis=-1)

def attend_head(query_rows, key_rows, value_rows, sink_row, visible):
    scores = jnp.einsum('nrgd,nkd->ngrk', query_rows.astype(jnp.float32), key_rows.astype(jnp.float32)) * HEAD_SIZE ** (-0.5)
    scores = jnp.where(visible[:, None], scores, -1e+30)
    top = jnp.maximum(lax.optimization_barrier(jnp.max(scores, axis=-1)), sink_row[None, :, None])
    expo = jnp.exp(scores - top[..., None])
    total = lax.optimization_barrier(jnp.sum(expo, axis=-1)) + jnp.exp(sink_row[None, :, None] - top)
    probs = (expo / total[..., None]).astype(jnp.bfloat16)
    out = jnp.einsum('ngrk,nkd->nrgd', probs.astype(jnp.float32), value_rows.astype(jnp.float32))
    return out.astype(jnp.bfloat16)

def reference(tokens, positions, norm_gain, qkv_weight, qkv_bias, sinks, earlier_keys, earlier_values):
    token_rows = TOKENS
    query_group = QUERY_HEADS // KEY_VALUE_HEADS
    query_length = QUERY_HEADS * HEAD_SIZE
    key_length = KEY_VALUE_HEADS * HEAD_SIZE
    flat = tokens.astype(jnp.float32)
    scale = lax.rsqrt(lax.optimization_barrier(jnp.mean(flat * flat, axis=-1, keepdims=True)) + 1e-05)
    normed = (flat * scale * norm_gain[None, :]).astype(jnp.bfloat16)
    combined_output = jnp.dot(normed, qkv_weight, preferred_element_type=jnp.float32) + qkv_bias[None, :]
    query_rows = apply_rotation(combined_output[:, :query_length].reshape(token_rows, QUERY_HEADS, HEAD_SIZE), positions).astype(jnp.bfloat16)
    key_rows = apply_rotation(combined_output[:, query_length:query_length + key_length].reshape(token_rows, KEY_VALUE_HEADS, HEAD_SIZE), positions).astype(jnp.bfloat16)
    value_rows = combined_output[:, query_length + key_length:].astype(jnp.bfloat16).reshape(token_rows, KEY_VALUE_HEADS, HEAD_SIZE)
    joined_keys = jnp.concatenate([earlier_keys.reshape(WINDOW_TOKENS, KEY_VALUE_HEADS, HEAD_SIZE), key_rows], axis=0)
    joined_values = jnp.concatenate([earlier_values.reshape(WINDOW_TOKENS, KEY_VALUE_HEADS, HEAD_SIZE), value_rows], axis=0)
    block_count = token_rows // WINDOW_TOKENS
    window_keys = jnp.concatenate([joined_keys[:token_rows].reshape(block_count, WINDOW_TOKENS, KEY_VALUE_HEADS, HEAD_SIZE), joined_keys[WINDOW_TOKENS:].reshape(block_count, WINDOW_TOKENS, KEY_VALUE_HEADS, HEAD_SIZE)], axis=1)
    window_values = jnp.concatenate([joined_values[:token_rows].reshape(block_count, WINDOW_TOKENS, KEY_VALUE_HEADS, HEAD_SIZE), joined_values[WINDOW_TOKENS:].reshape(block_count, WINDOW_TOKENS, KEY_VALUE_HEADS, HEAD_SIZE)], axis=1)
    query_blocks = query_rows.reshape(block_count, WINDOW_TOKENS, KEY_VALUE_HEADS, query_group, HEAD_SIZE)
    limit = jnp.minimum(positions, WINDOW_TOKENS - 1).reshape(block_count, WINDOW_TOKENS)
    rel = jnp.arange(WINDOW_TOKENS, dtype=jnp.int32)[:, None] - jnp.arange(2 * WINDOW_TOKENS, dtype=jnp.int32)[None, :] + WINDOW_TOKENS
    visible = (rel >= 0)[None] & (rel[None] <= limit[:, :, None])
    sink_tokens = sinks.reshape(KEY_VALUE_HEADS, query_group)

    def one_head(items):
        return attend_head(items[0], items[1], items[2], items[3], visible)
    out = lax.map(one_head, (jnp.moveaxis(query_blocks, 2, 0), jnp.moveaxis(window_keys, 2, 0), jnp.moveaxis(window_values, 2, 0), sink_tokens))
    return jnp.moveaxis(out, 0, 2).reshape(token_rows, query_length)
```

```python
import jax
import jax.numpy as jnp
from jax import lax
from jax.sharding import PartitionSpec as P

QUERY_HEADS = 32
KEY_VALUE_HEADS = 4
HEAD_SIZE = 64
WINDOW_TOKENS = 128


def shifted(value, axis, steps):
    count = lax.axis_size(axis)
    leading, last = (max(0, -steps), min(count, count - steps))
    return lax.ppermute(value, axis, [(source, source + steps) for source in range(leading, last)])


def apply_rotation(heads, positions):
    half = heads.shape[-1] // 2
    freq = 150000.0 ** (-(jnp.arange(half, dtype=jnp.float32) * 2.0 / heads.shape[-1]))
    angle = positions.astype(jnp.float32)[:, None] * freq[None, :]
    cosine = jnp.cos(angle)[:, None, :]
    sine = jnp.sin(angle)[:, None, :]
    first = heads[..., :half]
    second = heads[..., half:]
    return jnp.concatenate(
        [first * cosine - second * sine, second * cosine + first * sine], axis=-1
    )


def attend_head(query_rows, key_rows, value_rows, sink_row, visible):
    scores = jnp.einsum(
        "nrgd,nkd->ngrk", query_rows, key_rows, preferred_element_type=jnp.float32
    ) * HEAD_SIZE ** (-0.5)
    scores = jnp.where(visible[:, None], scores, -1e30)
    top = jnp.maximum(jnp.max(scores, axis=-1), sink_row[None, :, None])
    expo = jnp.exp(scores - top[..., None])
    total = jnp.sum(expo, axis=-1) + jnp.exp(sink_row[None, :, None] - top)
    probs = (expo / total[..., None]).astype(jnp.bfloat16)
    out = jnp.einsum("ngrk,nkd->nrgd", probs, value_rows, preferred_element_type=jnp.float32)
    return out.astype(jnp.bfloat16)


def send_rim(window_output, token_rows):
    return shifted(window_output[:, token_rows - WINDOW_TOKENS :], "ctx", 1)


def split_mixed(combined_output, positions, token_rows, query_length, key_length):
    key_rows = apply_rotation(
        combined_output[:, query_length : query_length + key_length].reshape(
            token_rows, KEY_VALUE_HEADS, HEAD_SIZE
        ),
        positions,
    ).astype(jnp.bfloat16)
    value_rows = combined_output[:, query_length + key_length :].astype(jnp.bfloat16)
    window_output = jnp.stack([key_rows.reshape(token_rows, key_length), value_rows])
    received = send_rim(window_output, token_rows)
    query_rows = apply_rotation(
        combined_output[:, :query_length].reshape(token_rows, QUERY_HEADS, HEAD_SIZE), positions
    ).astype(jnp.bfloat16)
    return (window_output, received, query_rows)


def gather_weight(qkv_weight):
    pairs = lax.axis_size("dp")
    columns = qkv_weight.shape[1]
    if columns % pairs:
        return lax.all_gather(qkv_weight, "ctx", axis=1, tiled=True)
    piece = columns // pairs
    own = lax.dynamic_slice_in_dim(qkv_weight, lax.axis_index("dp") * piece, piece, axis=1)
    return lax.all_gather(own, ("ctx", "dp"), axis=1, tiled=True)


def on_device(
    tokens, positions, norm_gain, qkv_weight, qkv_bias, sinks, earlier_keys, earlier_values
):
    token_rows = tokens.shape[0]
    query_group = QUERY_HEADS // KEY_VALUE_HEADS
    query_length = QUERY_HEADS * HEAD_SIZE
    key_length = KEY_VALUE_HEADS * HEAD_SIZE
    flat = tokens.astype(jnp.float32)
    scale = lax.rsqrt(jnp.mean(flat * flat, axis=-1, keepdims=True) + 1e-05)
    normed = (flat * scale * norm_gain[None, :]).astype(jnp.bfloat16)
    combined_output = jnp.dot(
        normed, gather_weight(qkv_weight), preferred_element_type=jnp.float32
    )
    combined_output = combined_output + qkv_bias[None, :]
    window_output, received, query_rows = split_mixed(
        combined_output, positions, token_rows, query_length, key_length
    )
    prior = jnp.stack([earlier_keys, earlier_values])
    border_tokens = jnp.where(lax.axis_index("ctx") == 0, prior, received)
    padded_rows = jnp.concatenate([border_tokens, window_output], axis=1).reshape(
        2, WINDOW_TOKENS + token_rows, KEY_VALUE_HEADS, HEAD_SIZE
    )
    joined_keys = padded_rows[0]
    joined_values = padded_rows[1]
    limit = jnp.minimum(positions, WINDOW_TOKENS - 1)
    sink_tokens = sinks.reshape(KEY_VALUE_HEADS, query_group)
    rel = (
        jnp.arange(token_rows, dtype=jnp.int32)[:, None]
        - jnp.arange(WINDOW_TOKENS + token_rows, dtype=jnp.int32)[None, :]
        + WINDOW_TOKENS
    )
    visible = ((rel >= 0) & (rel <= limit[:, None]))[None]
    query_blocks = query_rows.reshape(1, token_rows, KEY_VALUE_HEADS, query_group, HEAD_SIZE)
    window_keys = joined_keys[None]
    window_values = joined_values[None]

    def one_head(items):
        return attend_head(items[0], items[1], items[2], items[3], visible)

    out = lax.map(
        one_head,
        (
            jnp.moveaxis(query_blocks, 2, 0),
            jnp.moveaxis(window_keys, 2, 0),
            jnp.moveaxis(window_values, 2, 0),
            sink_tokens,
        ),
    )
    return jnp.moveaxis(out, 0, 2).reshape(token_rows, query_length)


def solution(mesh):
    placed = (
        P(("dp", "ctx"), None),
        P(("dp", "ctx")),
        P(),
        P(None, "ctx"),
        P(),
        P(),
        P("dp", None),
        P("dp", None),
    )
    return jax.shard_map(
        on_device, mesh=mesh, in_specs=placed, out_specs=P(("dp", "ctx"), None), check_vma=False
    )
```

```python
import jax
import jax.numpy as jnp
from jax import lax
from jax.sharding import PartitionSpec as P

QUERY_HEADS = 32
KEY_VALUE_HEADS = 4
HEAD_SIZE = 64
WINDOW_TOKENS = 128


def shifted(value, axis, steps):
    count = lax.axis_size(axis)
    leading, last = (max(0, -steps), min(count, count - steps))
    return lax.ppermute(value, axis, [(source, source + steps) for source in range(leading, last)])


def apply_rotation(heads, positions):
    half = heads.shape[-1] // 2
    freq = 150000.0 ** (-(jnp.arange(half, dtype=jnp.float32) * 2.0 / heads.shape[-1]))
    angle = positions.astype(jnp.float32)[:, None] * freq[None, :]
    cosine = jnp.cos(angle)[:, None, :]
    sine = jnp.sin(angle)[:, None, :]
    first = heads[..., :half]
    second = heads[..., half:]
    return jnp.concatenate(
        [first * cosine - second * sine, second * cosine + first * sine], axis=-1
    )


def attend_head(query_rows, key_rows, value_rows, sink_row, visible):
    scores = jnp.einsum(
        "nrgd,nkd->ngrk", query_rows, key_rows, preferred_element_type=jnp.float32
    ) * HEAD_SIZE ** (-0.5)
    scores = jnp.where(visible[:, None], scores, -1e30)
    top = jnp.maximum(jnp.max(scores, axis=-1), sink_row[None, :, None])
    expo = jnp.exp(scores - top[..., None])
    total = jnp.sum(expo, axis=-1) + jnp.exp(sink_row[None, :, None] - top)
    probs = (expo / total[..., None]).astype(jnp.bfloat16)
    out = jnp.einsum("ngrk,nkd->nrgd", probs, value_rows, preferred_element_type=jnp.float32)
    return out.astype(jnp.bfloat16)


def send_rim(window_output, token_rows):
    return shifted(window_output[:, token_rows - WINDOW_TOKENS :], "ctx", 1)


def split_mixed(combined_output, positions, token_rows, query_length, key_length):
    key_rows = apply_rotation(
        combined_output[:, query_length : query_length + key_length].reshape(
            token_rows, KEY_VALUE_HEADS, HEAD_SIZE
        ),
        positions,
    ).astype(jnp.bfloat16)
    value_rows = combined_output[:, query_length + key_length :].astype(jnp.bfloat16)
    window_output = jnp.stack([key_rows.reshape(token_rows, key_length), value_rows])
    received = send_rim(window_output, token_rows)
    query_rows = apply_rotation(
        combined_output[:, :query_length].reshape(token_rows, QUERY_HEADS, HEAD_SIZE), positions
    ).astype(jnp.bfloat16)
    return (window_output, received, query_rows)


def gather_weight(qkv_weight):
    pairs = lax.axis_size("dp")
    columns = qkv_weight.shape[1]
    if columns % pairs:
        return lax.all_gather(qkv_weight.T, "ctx", axis=0, tiled=True)
    piece = columns // pairs
    own = lax.dynamic_slice_in_dim(qkv_weight, lax.axis_index("dp") * piece, piece, axis=1)
    return lax.all_gather(own.T, ("ctx", "dp"), axis=0, tiled=True)


def on_device(
    tokens, positions, norm_gain, qkv_weight, qkv_bias, sinks, earlier_keys, earlier_values
):
    token_rows = tokens.shape[0]
    query_group = QUERY_HEADS // KEY_VALUE_HEADS
    query_length = QUERY_HEADS * HEAD_SIZE
    key_length = KEY_VALUE_HEADS * HEAD_SIZE
    flat = tokens.astype(jnp.float32)
    scale = lax.rsqrt(jnp.mean(flat * flat, axis=-1, keepdims=True) + 1e-05)
    normed = (flat * scale * norm_gain[None, :]).astype(jnp.bfloat16)
    combined_output = lax.dot_general(
        normed,
        gather_weight(qkv_weight),
        (((1,), (1,)), ((), ())),
        preferred_element_type=jnp.float32,
    )
    combined_output = combined_output + qkv_bias[None, :]
    window_output, received, query_rows = split_mixed(
        combined_output, positions, token_rows, query_length, key_length
    )
    prior = jnp.stack([earlier_keys, earlier_values])
    border_tokens = jnp.where(lax.axis_index("ctx") == 0, prior, received)
    padded_rows = jnp.concatenate([border_tokens, window_output], axis=1).reshape(
        2, WINDOW_TOKENS + token_rows, KEY_VALUE_HEADS, HEAD_SIZE
    )
    joined_keys = padded_rows[0]
    joined_values = padded_rows[1]
    limit = jnp.minimum(positions, WINDOW_TOKENS - 1)
    sink_tokens = sinks.reshape(KEY_VALUE_HEADS, query_group)
    rel = (
        jnp.arange(token_rows, dtype=jnp.int32)[:, None]
        - jnp.arange(WINDOW_TOKENS + token_rows, dtype=jnp.int32)[None, :]
        + WINDOW_TOKENS
    )
    visible = ((rel >= 0) & (rel <= limit[:, None]))[None]
    query_blocks = query_rows.reshape(1, token_rows, KEY_VALUE_HEADS, query_group, HEAD_SIZE)
    window_keys = joined_keys[None]
    window_values = joined_values[None]

    def one_head(items):
        return attend_head(items[0], items[1], items[2], items[3], visible)

    out = lax.map(
        one_head,
        (
            jnp.moveaxis(query_blocks, 2, 0),
            jnp.moveaxis(window_keys, 2, 0),
            jnp.moveaxis(window_values, 2, 0),
            sink_tokens,
        ),
    )
    return jnp.moveaxis(out, 0, 2).reshape(token_rows, query_length)


def solution(mesh):
    placed = (
        P(("dp", "ctx"), None),
        P(("dp", "ctx")),
        P(),
        P(None, "ctx"),
        P(),
        P(),
        P("dp", None),
        P("dp", None),
    )
    return jax.shard_map(
        on_device, mesh=mesh, in_specs=placed, out_specs=P(("dp", "ctx"), None), check_vma=False
    )
```

```python
import jax
import jax.numpy as jnp
from jax import lax
from jax.sharding import PartitionSpec as P

QUERY_HEADS = 32
KEY_VALUE_HEADS = 4
HEAD_SIZE = 64
WINDOW_TOKENS = 128


def shifted(value, axis, steps):
    count = lax.axis_size(axis)
    leading, last = (max(0, -steps), min(count, count - steps))
    return lax.ppermute(value, axis, [(source, source + steps) for source in range(leading, last)])


def apply_rotation(heads, positions):
    half = heads.shape[-1] // 2
    freq = 150000.0 ** (-(jnp.arange(half, dtype=jnp.float32) * 2.0 / heads.shape[-1]))
    angle = positions.astype(jnp.float32)[:, None] * freq[None, :]
    cosine = jnp.cos(angle)[:, None, :]
    sine = jnp.sin(angle)[:, None, :]
    first = heads[..., :half]
    second = heads[..., half:]
    return jnp.concatenate(
        [first * cosine - second * sine, second * cosine + first * sine], axis=-1
    )


def attend_head(query_rows, key_rows, value_rows, sink_row, visible):
    scores = jnp.einsum(
        "nrgd,nkd->ngrk", query_rows, key_rows, preferred_element_type=jnp.float32
    ) * HEAD_SIZE ** (-0.5)
    scores = jnp.where(visible[:, None], scores, -1e30)
    top = jnp.maximum(jnp.max(scores, axis=-1), sink_row[None, :, None])
    expo = jnp.exp(scores - top[..., None])
    total = jnp.sum(expo, axis=-1) + jnp.exp(sink_row[None, :, None] - top)
    probs = (expo / total[..., None]).astype(jnp.bfloat16)
    out = jnp.einsum("ngrk,nkd->nrgd", probs, value_rows, preferred_element_type=jnp.float32)
    return out.astype(jnp.bfloat16)


def send_rim(window_output, token_rows):
    return shifted(window_output[:, token_rows - WINDOW_TOKENS :], "ctx", 1)


def split_mixed(combined_output, positions, token_rows, query_length, key_length):
    key_rows = apply_rotation(
        combined_output[:, query_length : query_length + key_length].reshape(
            token_rows, KEY_VALUE_HEADS, HEAD_SIZE
        ),
        positions,
    ).astype(jnp.bfloat16)
    value_rows = combined_output[:, query_length + key_length :].astype(jnp.bfloat16)
    window_output = jnp.stack([key_rows.reshape(token_rows, key_length), value_rows])
    received = send_rim(window_output, token_rows)
    query_rows = apply_rotation(
        combined_output[:, :query_length].reshape(token_rows, QUERY_HEADS, HEAD_SIZE), positions
    ).astype(jnp.bfloat16)
    return (window_output, received, query_rows)


def gather_weight(qkv_weight):
    pairs = lax.axis_size("dp")
    columns = qkv_weight.shape[1]
    if columns % pairs:
        return lax.all_gather(qkv_weight.T, "ctx", axis=0, tiled=True)
    piece = columns // pairs
    own = lax.dynamic_slice_in_dim(qkv_weight, lax.axis_index("dp") * piece, piece, axis=1)
    return lax.all_gather(own.T, ("ctx", "dp"), axis=0, tiled=True)


def on_device(
    tokens, positions, norm_gain, qkv_weight, qkv_bias, sinks, earlier_keys, earlier_values
):
    token_rows = tokens.shape[0]
    query_group = QUERY_HEADS // KEY_VALUE_HEADS
    query_length = QUERY_HEADS * HEAD_SIZE
    key_length = KEY_VALUE_HEADS * HEAD_SIZE
    flat = tokens.astype(jnp.float32)
    scale = lax.rsqrt(jnp.mean(flat * flat, axis=-1, keepdims=True) + 1e-05)
    normed = lax.optimization_barrier((flat * scale * norm_gain[None, :]).astype(jnp.bfloat16))
    combined_output = lax.dot_general(
        normed,
        gather_weight(qkv_weight),
        (((1,), (1,)), ((), ())),
        preferred_element_type=jnp.float32,
    )
    combined_output = combined_output + qkv_bias[None, :]
    window_output, received, query_rows = split_mixed(
        combined_output, positions, token_rows, query_length, key_length
    )
    prior = jnp.stack([earlier_keys, earlier_values])
    border_tokens = jnp.where(lax.axis_index("ctx") == 0, prior, received)
    padded_rows = jnp.concatenate([border_tokens, window_output], axis=1).reshape(
        2, WINDOW_TOKENS + token_rows, KEY_VALUE_HEADS, HEAD_SIZE
    )
    joined_keys = padded_rows[0]
    joined_values = padded_rows[1]
    limit = jnp.minimum(positions, WINDOW_TOKENS - 1)
    sink_tokens = sinks.reshape(KEY_VALUE_HEADS, query_group)
    rel = (
        jnp.arange(token_rows, dtype=jnp.int32)[:, None]
        - jnp.arange(WINDOW_TOKENS + token_rows, dtype=jnp.int32)[None, :]
        + WINDOW_TOKENS
    )
    visible = ((rel >= 0) & (rel <= limit[:, None]))[None]
    query_blocks = query_rows.reshape(1, token_rows, KEY_VALUE_HEADS, query_group, HEAD_SIZE)
    window_keys = joined_keys[None]
    window_values = joined_values[None]

    def one_head(items):
        return attend_head(items[0], items[1], items[2], items[3], visible)

    out = lax.map(
        one_head,
        (
            jnp.moveaxis(query_blocks, 2, 0),
            jnp.moveaxis(window_keys, 2, 0),
            jnp.moveaxis(window_values, 2, 0),
            sink_tokens,
        ),
    )
    return jnp.moveaxis(out, 0, 2).reshape(token_rows, query_length)


def solution(mesh):
    placed = (
        P(("dp", "ctx"), None),
        P(("dp", "ctx")),
        P(),
        P(None, "ctx"),
        P(),
        P(),
        P("dp", None),
        P("dp", None),
    )
    return jax.shard_map(
        on_device, mesh=mesh, in_specs=placed, out_specs=P(("dp", "ctx"), None), check_vma=False
    )
```

```python
import jax
import jax.numpy as jnp
from jax import lax
from jax.experimental import pallas as pl
from jax.experimental.pallas import tpu as pltpu
from jax.sharding import PartitionSpec as P

QUERY_HEADS = 32
KEY_VALUE_HEADS = 4
HEAD_SIZE = 64
WINDOW_TOKENS = 128


def shifted(value, axis, steps):
    count = lax.axis_size(axis)
    leading, last = (max(0, -steps), min(count, count - steps))
    return lax.ppermute(value, axis, [(source, source + steps) for source in range(leading, last)])


def apply_rotation(heads, positions):
    half = heads.shape[-1] // 2
    freq = 150000.0 ** (-(jnp.arange(half, dtype=jnp.float32) * 2.0 / heads.shape[-1]))
    angle = positions.astype(jnp.float32)[:, None] * freq[None, :]
    cosine = jnp.cos(angle)[:, None, :]
    sine = jnp.sin(angle)[:, None, :]
    first = heads[..., :half]
    second = heads[..., half:]
    return jnp.concatenate(
        [first * cosine - second * sine, second * cosine + first * sine], axis=-1
    )


def attend_head(query_rows, key_rows, value_rows, sink_row, visible):
    scores = jnp.einsum(
        "nrgd,nkd->ngrk", query_rows, key_rows, preferred_element_type=jnp.float32
    ) * HEAD_SIZE ** (-0.5)
    scores = jnp.where(visible[:, None], scores, -1e30)
    top = jnp.maximum(jnp.max(scores, axis=-1), sink_row[None, :, None])
    expo = jnp.exp(scores - top[..., None])
    total = jnp.sum(expo, axis=-1) + jnp.exp(sink_row[None, :, None] - top)
    probs = (expo / total[..., None]).astype(jnp.bfloat16)
    out = jnp.einsum("ngrk,nkd->nrgd", probs, value_rows, preferred_element_type=jnp.float32)
    return out.astype(jnp.bfloat16)


def attention_kernel(sinks_ref, limit_ref, cos_ref, sin_ref, q_ref, k_ref, v_ref, out_ref):
    group = pl.program_id(0)
    rows = q_ref.shape[0]
    query_group = q_ref.shape[1] // HEAD_SIZE
    half = HEAD_SIZE // 2
    lanes = cos_ref.shape[1]
    cosine = cos_ref[...]
    sine = sin_ref[...]
    lane = lax.broadcasted_iota(jnp.int32, (rows, lanes), 1)
    source = pltpu.roll(lane, half, 1)
    partner_lane = jnp.where(lane % HEAD_SIZE < half, lane + half, lane - half)
    take_first = source == partner_lane
    block = WINDOW_TOKENS
    query_index = lax.broadcasted_iota(jnp.int32, (block, 2 * block), 0)
    key_index = lax.broadcasted_iota(jnp.int32, (block, 2 * block), 1)
    rel = query_index - key_index + block
    visible = []
    for part in range(rows // block):
        limit = limit_ref[part * block : (part + 1) * block, :]
        visible.append((rel >= 0) & (rel <= limit))
    heads_per_chunk = lanes // HEAD_SIZE
    for chunk in range(q_ref.shape[1] // lanes):
        x = q_ref[:, chunk * lanes : (chunk + 1) * lanes]
        first = pltpu.roll(x, half, 1)
        second = pltpu.roll(x, lanes - half, 1)
        partner = jnp.where(take_first, first, second)
        rotated = (x * cosine + partner * sine).astype(jnp.bfloat16)
        for inner in range(heads_per_chunk):
            head = chunk * heads_per_chunk + inner
            sink = sinks_ref[group * query_group + head]
            query_head = rotated[:, inner * HEAD_SIZE : (inner + 1) * HEAD_SIZE]
            for part in range(rows // block):
                queries = query_head[part * block : (part + 1) * block]
                keys = k_ref[0, part * block : part * block + 2 * block, :]
                values = v_ref[0, part * block : part * block + 2 * block, :]
                scores = lax.dot_general(
                    queries, keys, (((1,), (1,)), ((), ())), preferred_element_type=jnp.float32
                ) * HEAD_SIZE ** (-0.5)
                scores = jnp.where(visible[part], scores, -1e30)
                top = jnp.maximum(jnp.max(scores, axis=1, keepdims=True), sink)
                expo = jnp.exp(scores - top)
                total = jnp.sum(expo, axis=1, keepdims=True) + jnp.exp(sink - top)
                probs = (expo / total).astype(jnp.bfloat16)
                out = jnp.dot(probs, values, preferred_element_type=jnp.float32)
                out_ref[part * block : (part + 1) * block, head * HEAD_SIZE : (head + 1) * HEAD_SIZE] = out.astype(
                    jnp.bfloat16
                )


def rotation_tables(positions, lanes):
    half = HEAD_SIZE // 2
    freq = 150000.0 ** (-(jnp.arange(half, dtype=jnp.float32) * 2.0 / HEAD_SIZE))
    angle = positions.astype(jnp.float32)[:, None] * freq[None, :]
    cosine = jnp.cos(angle)
    sine = jnp.sin(angle)
    repeats = lanes // HEAD_SIZE
    cos_table = jnp.tile(jnp.concatenate([cosine, cosine], axis=1), (1, repeats))
    sin_table = jnp.tile(jnp.concatenate([-sine, sine], axis=1), (1, repeats))
    return cos_table, sin_table


def attend(combined_output, joined_keys, joined_values, positions, sinks):
    token_rows = combined_output.shape[0]
    query_group = QUERY_HEADS // KEY_VALUE_HEADS
    group_width = query_group * HEAD_SIZE
    lanes = 128
    cos_table, sin_table = rotation_tables(positions, lanes)
    limit = jnp.minimum(positions, WINDOW_TOKENS - 1).astype(jnp.int32)[:, None]
    keys = jnp.moveaxis(joined_keys, 1, 0)
    values = jnp.moveaxis(joined_values, 1, 0)
    key_rows = keys.shape[1]
    return pl.pallas_call(
        attention_kernel,
        grid=(KEY_VALUE_HEADS,),
        in_specs=[
            pl.BlockSpec(memory_space=pltpu.SMEM),
            pl.BlockSpec((token_rows, 1), lambda g: (0, 0)),
            pl.BlockSpec((token_rows, lanes), lambda g: (0, 0)),
            pl.BlockSpec((token_rows, lanes), lambda g: (0, 0)),
            pl.BlockSpec((token_rows, group_width), lambda g: (0, g)),
            pl.BlockSpec((1, key_rows, HEAD_SIZE), lambda g: (g, 0, 0)),
            pl.BlockSpec((1, key_rows, HEAD_SIZE), lambda g: (g, 0, 0)),
        ],
        out_specs=pl.BlockSpec((token_rows, group_width), lambda g: (0, g)),
        out_shape=jax.ShapeDtypeStruct((token_rows, QUERY_HEADS * HEAD_SIZE), jnp.bfloat16),
    )(sinks, limit, cos_table, sin_table, combined_output, keys, values)


def send_rim(window_output, token_rows):
    return shifted(window_output[:, token_rows - WINDOW_TOKENS :], "ctx", 1)


def split_mixed(combined_output, positions, token_rows, query_length, key_length):
    key_rows = apply_rotation(
        combined_output[:, query_length : query_length + key_length].reshape(
            token_rows, KEY_VALUE_HEADS, HEAD_SIZE
        ),
        positions,
    ).astype(jnp.bfloat16)
    value_rows = combined_output[:, query_length + key_length :].astype(jnp.bfloat16)
    window_output = jnp.stack([key_rows.reshape(token_rows, key_length), value_rows])
    received = send_rim(window_output, token_rows)
    query_rows = apply_rotation(
        combined_output[:, :query_length].reshape(token_rows, QUERY_HEADS, HEAD_SIZE), positions
    ).astype(jnp.bfloat16)
    return (window_output, received, query_rows)


def gather_weight(qkv_weight):
    pairs = lax.axis_size("dp")
    columns = qkv_weight.shape[1]
    if columns % pairs:
        return lax.all_gather(qkv_weight.T, "ctx", axis=0, tiled=True)
    piece = columns // pairs
    own = lax.dynamic_slice_in_dim(qkv_weight, lax.axis_index("dp") * piece, piece, axis=1)
    return lax.all_gather(own.T, ("ctx", "dp"), axis=0, tiled=True)


def on_device(
    tokens, positions, norm_gain, qkv_weight, qkv_bias, sinks, earlier_keys, earlier_values
):
    token_rows = tokens.shape[0]
    query_group = QUERY_HEADS // KEY_VALUE_HEADS
    query_length = QUERY_HEADS * HEAD_SIZE
    key_length = KEY_VALUE_HEADS * HEAD_SIZE
    flat = tokens.astype(jnp.float32)
    scale = lax.rsqrt(jnp.mean(flat * flat, axis=-1, keepdims=True) + 1e-05)
    normed = lax.optimization_barrier((flat * scale * norm_gain[None, :]).astype(jnp.bfloat16))
    combined_output = lax.dot_general(
        normed,
        gather_weight(qkv_weight),
        (((1,), (1,)), ((), ())),
        preferred_element_type=jnp.float32,
    )
    combined_output = combined_output + qkv_bias[None, :]
    key_rows = apply_rotation(
        combined_output[:, query_length : query_length + key_length].reshape(
            token_rows, KEY_VALUE_HEADS, HEAD_SIZE
        ),
        positions,
    ).astype(jnp.bfloat16)
    value_rows = combined_output[:, query_length + key_length :].astype(jnp.bfloat16)
    window_output = jnp.stack([key_rows.reshape(token_rows, key_length), value_rows])
    received = send_rim(window_output, token_rows)
    prior = jnp.stack([earlier_keys, earlier_values])
    border_tokens = jnp.where(lax.axis_index("ctx") == 0, prior, received)
    padded_rows = jnp.concatenate([border_tokens, window_output], axis=1).reshape(
        2, WINDOW_TOKENS + token_rows, KEY_VALUE_HEADS, HEAD_SIZE
    )
    return attend(combined_output, padded_rows[0], padded_rows[1], positions, sinks)


def solution(mesh):
    placed = (
        P(("dp", "ctx"), None),
        P(("dp", "ctx")),
        P(),
        P(None, "ctx"),
        P(),
        P(),
        P("dp", None),
        P("dp", None),
    )
    return jax.shard_map(
        on_device, mesh=mesh, in_specs=placed, out_specs=P(("dp", "ctx"), None), check_vma=False
    )
```

```python
import jax
import jax.numpy as jnp
from jax import lax
from jax.experimental import pallas as pl
from jax.experimental.pallas import tpu as pltpu
from jax.sharding import PartitionSpec as P

QUERY_HEADS = 32
KEY_VALUE_HEADS = 4
HEAD_SIZE = 64
WINDOW_TOKENS = 128


def shifted(value, axis, steps):
    count = lax.axis_size(axis)
    leading, last = (max(0, -steps), min(count, count - steps))
    return lax.ppermute(value, axis, [(source, source + steps) for source in range(leading, last)])


def apply_rotation(heads, positions):
    half = heads.shape[-1] // 2
    freq = 150000.0 ** (-(jnp.arange(half, dtype=jnp.float32) * 2.0 / heads.shape[-1]))
    angle = positions.astype(jnp.float32)[:, None] * freq[None, :]
    cosine = jnp.cos(angle)[:, None, :]
    sine = jnp.sin(angle)[:, None, :]
    first = heads[..., :half]
    second = heads[..., half:]
    return jnp.concatenate(
        [first * cosine - second * sine, second * cosine + first * sine], axis=-1
    )


def attend_head(query_rows, key_rows, value_rows, sink_row, visible):
    scores = jnp.einsum(
        "nrgd,nkd->ngrk", query_rows, key_rows, preferred_element_type=jnp.float32
    ) * HEAD_SIZE ** (-0.5)
    scores = jnp.where(visible[:, None], scores, -1e30)
    top = jnp.maximum(jnp.max(scores, axis=-1), sink_row[None, :, None])
    expo = jnp.exp(scores - top[..., None])
    total = jnp.sum(expo, axis=-1) + jnp.exp(sink_row[None, :, None] - top)
    probs = (expo / total[..., None]).astype(jnp.bfloat16)
    out = jnp.einsum("ngrk,nkd->nrgd", probs, value_rows, preferred_element_type=jnp.float32)
    return out.astype(jnp.bfloat16)


def attention_kernel(sinks_ref, limit_ref, cos_ref, sin_ref, q_ref, k_ref, v_ref, out_ref):
    group = pl.program_id(0)
    rows = q_ref.shape[0]
    query_group = q_ref.shape[1] // HEAD_SIZE
    half = HEAD_SIZE // 2
    lanes = cos_ref.shape[1]
    cosine = cos_ref[...]
    sine = sin_ref[...]
    lane = lax.broadcasted_iota(jnp.int32, (rows, lanes), 1)
    source = pltpu.roll(lane, half, 1)
    partner_lane = jnp.where(lane % HEAD_SIZE < half, lane + half, lane - half)
    take_first = source == partner_lane
    block = WINDOW_TOKENS
    query_index = lax.broadcasted_iota(jnp.int32, (block, 2 * block), 0)
    key_index = lax.broadcasted_iota(jnp.int32, (block, 2 * block), 1)
    rel = query_index - key_index + block
    visible = []
    for part in range(rows // block):
        limit = limit_ref[part * block : (part + 1) * block, :]
        visible.append((rel >= 0) & (rel <= limit))
    heads_per_chunk = lanes // HEAD_SIZE
    for chunk in range(q_ref.shape[1] // lanes):
        x = q_ref[:, chunk * lanes : (chunk + 1) * lanes]
        first = pltpu.roll(x, half, 1)
        second = pltpu.roll(x, lanes - half, 1)
        partner = jnp.where(take_first, first, second)
        rotated = (x * cosine + partner * sine).astype(jnp.bfloat16)
        for inner in range(heads_per_chunk):
            head = chunk * heads_per_chunk + inner
            sink = sinks_ref[group * query_group + head]
            query_head = rotated[:, inner * HEAD_SIZE : (inner + 1) * HEAD_SIZE]
            for part in range(rows // block):
                queries = query_head[part * block : (part + 1) * block]
                keys = k_ref[0, part * block : part * block + 2 * block, :]
                values = v_ref[0, part * block : part * block + 2 * block, :]
                scores = lax.dot_general(
                    queries, keys, (((1,), (1,)), ((), ())), preferred_element_type=jnp.float32
                ) * HEAD_SIZE ** (-0.5)
                scores = jnp.where(visible[part], scores, -1e30)
                top = jnp.maximum(jnp.max(scores, axis=1, keepdims=True), sink)
                expo = jnp.exp(scores - top)
                total = jnp.sum(expo, axis=1, keepdims=True) + jnp.exp(sink - top)
                probs = (expo / total).astype(jnp.bfloat16)
                out = jnp.dot(probs, values, preferred_element_type=jnp.float32)
                out_ref[part * block : (part + 1) * block, head * HEAD_SIZE : (head + 1) * HEAD_SIZE] = out.astype(
                    jnp.bfloat16
                )


def rotation_tables(positions, lanes):
    half = HEAD_SIZE // 2
    freq = 150000.0 ** (-(jnp.arange(half, dtype=jnp.float32) * 2.0 / HEAD_SIZE))
    angle = positions.astype(jnp.float32)[:, None] * freq[None, :]
    cosine = jnp.cos(angle)
    sine = jnp.sin(angle)
    repeats = lanes // HEAD_SIZE
    cos_table = jnp.tile(jnp.concatenate([cosine, cosine], axis=1), (1, repeats))
    sin_table = jnp.tile(jnp.concatenate([-sine, sine], axis=1), (1, repeats))
    return cos_table, sin_table


def attend(combined_output, joined_keys, joined_values, tables, sinks):
    token_rows = combined_output.shape[0]
    query_group = QUERY_HEADS // KEY_VALUE_HEADS
    group_width = query_group * HEAD_SIZE
    cos_table, sin_table, limit = tables
    lanes = cos_table.shape[1]
    keys = jnp.moveaxis(joined_keys, 1, 0)
    values = jnp.moveaxis(joined_values, 1, 0)
    key_rows = keys.shape[1]
    return pl.pallas_call(
        attention_kernel,
        grid=(KEY_VALUE_HEADS,),
        in_specs=[
            pl.BlockSpec(memory_space=pltpu.SMEM),
            pl.BlockSpec((token_rows, 1), lambda g: (0, 0)),
            pl.BlockSpec((token_rows, lanes), lambda g: (0, 0)),
            pl.BlockSpec((token_rows, lanes), lambda g: (0, 0)),
            pl.BlockSpec((token_rows, group_width), lambda g: (0, g)),
            pl.BlockSpec((1, key_rows, HEAD_SIZE), lambda g: (g, 0, 0)),
            pl.BlockSpec((1, key_rows, HEAD_SIZE), lambda g: (g, 0, 0)),
        ],
        out_specs=pl.BlockSpec((token_rows, group_width), lambda g: (0, g)),
        out_shape=jax.ShapeDtypeStruct((token_rows, QUERY_HEADS * HEAD_SIZE), jnp.bfloat16),
    )(sinks, limit, cos_table, sin_table, combined_output, keys, values)


def send_rim(window_output, token_rows):
    return shifted(window_output[:, token_rows - WINDOW_TOKENS :], "ctx", 1)


def split_mixed(combined_output, positions, token_rows, query_length, key_length):
    key_rows = apply_rotation(
        combined_output[:, query_length : query_length + key_length].reshape(
            token_rows, KEY_VALUE_HEADS, HEAD_SIZE
        ),
        positions,
    ).astype(jnp.bfloat16)
    value_rows = combined_output[:, query_length + key_length :].astype(jnp.bfloat16)
    window_output = jnp.stack([key_rows.reshape(token_rows, key_length), value_rows])
    received = send_rim(window_output, token_rows)
    query_rows = apply_rotation(
        combined_output[:, :query_length].reshape(token_rows, QUERY_HEADS, HEAD_SIZE), positions
    ).astype(jnp.bfloat16)
    return (window_output, received, query_rows)


def gather_weight(qkv_weight):
    pairs = lax.axis_size("dp")
    columns = qkv_weight.shape[1]
    if columns % pairs:
        return lax.all_gather(qkv_weight.T, "ctx", axis=0, tiled=True)
    piece = columns // pairs
    own = lax.dynamic_slice_in_dim(qkv_weight, lax.axis_index("dp") * piece, piece, axis=1)
    return lax.all_gather(own.T, ("ctx", "dp"), axis=0, tiled=True)


def on_device(
    tokens, positions, norm_gain, qkv_weight, qkv_bias, sinks, earlier_keys, earlier_values
):
    token_rows = tokens.shape[0]
    query_group = QUERY_HEADS // KEY_VALUE_HEADS
    query_length = QUERY_HEADS * HEAD_SIZE
    key_length = KEY_VALUE_HEADS * HEAD_SIZE
    flat = tokens.astype(jnp.float32)
    scale = lax.rsqrt(jnp.mean(flat * flat, axis=-1, keepdims=True) + 1e-05)
    normed = (flat * scale * norm_gain[None, :]).astype(jnp.bfloat16)
    tables = rotation_tables(positions, 128) + (
        jnp.minimum(positions, WINDOW_TOKENS - 1).astype(jnp.int32)[:, None],
    )
    normed, tables = lax.optimization_barrier((normed, tables))
    combined_output = lax.dot_general(
        normed,
        gather_weight(qkv_weight),
        (((1,), (1,)), ((), ())),
        preferred_element_type=jnp.float32,
    )
    combined_output = combined_output + qkv_bias[None, :]
    key_rows = apply_rotation(
        combined_output[:, query_length : query_length + key_length].reshape(
            token_rows, KEY_VALUE_HEADS, HEAD_SIZE
        ),
        positions,
    ).astype(jnp.bfloat16)
    value_rows = combined_output[:, query_length + key_length :].astype(jnp.bfloat16)
    window_output = jnp.stack([key_rows.reshape(token_rows, key_length), value_rows])
    received = send_rim(window_output, token_rows)
    prior = jnp.stack([earlier_keys, earlier_values])
    border_tokens = jnp.where(lax.axis_index("ctx") == 0, prior, received)
    padded_rows = jnp.concatenate([border_tokens, window_output], axis=1).reshape(
        2, WINDOW_TOKENS + token_rows, KEY_VALUE_HEADS, HEAD_SIZE
    )
    return attend(combined_output, padded_rows[0], padded_rows[1], tables, sinks)


def solution(mesh):
    placed = (
        P(("dp", "ctx"), None),
        P(("dp", "ctx")),
        P(),
        P(None, "ctx"),
        P(),
        P(),
        P("dp", None),
        P("dp", None),
    )
    return jax.shard_map(
        on_device, mesh=mesh, in_specs=placed, out_specs=P(("dp", "ctx"), None), check_vma=False
    )
```

```python
import jax
import jax.numpy as jnp
from jax import lax
from jax.experimental import pallas as pl
from jax.experimental.pallas import tpu as pltpu
from jax.sharding import PartitionSpec as P

QUERY_HEADS = 32
KEY_VALUE_HEADS = 4
HEAD_SIZE = 64
WINDOW_TOKENS = 128


def shifted(value, axis, steps):
    count = lax.axis_size(axis)
    leading, last = (max(0, -steps), min(count, count - steps))
    return lax.ppermute(value, axis, [(source, source + steps) for source in range(leading, last)])


def apply_rotation(heads, positions):
    half = heads.shape[-1] // 2
    freq = 150000.0 ** (-(jnp.arange(half, dtype=jnp.float32) * 2.0 / heads.shape[-1]))
    angle = positions.astype(jnp.float32)[:, None] * freq[None, :]
    cosine = jnp.cos(angle)[:, None, :]
    sine = jnp.sin(angle)[:, None, :]
    first = heads[..., :half]
    second = heads[..., half:]
    return jnp.concatenate(
        [first * cosine - second * sine, second * cosine + first * sine], axis=-1
    )


def attend_head(query_rows, key_rows, value_rows, sink_row, visible):
    scores = jnp.einsum(
        "nrgd,nkd->ngrk", query_rows, key_rows, preferred_element_type=jnp.float32
    ) * HEAD_SIZE ** (-0.5)
    scores = jnp.where(visible[:, None], scores, -1e30)
    top = jnp.maximum(jnp.max(scores, axis=-1), sink_row[None, :, None])
    expo = jnp.exp(scores - top[..., None])
    total = jnp.sum(expo, axis=-1) + jnp.exp(sink_row[None, :, None] - top)
    probs = (expo / total[..., None]).astype(jnp.bfloat16)
    out = jnp.einsum("ngrk,nkd->nrgd", probs, value_rows, preferred_element_type=jnp.float32)
    return out.astype(jnp.bfloat16)


def attention_kernel(sinks_ref, limit_ref, cos_ref, sin_ref, q_ref, k_ref, v_ref, out_ref):
    group = pl.program_id(0)
    rows = q_ref.shape[0]
    query_group = q_ref.shape[1] // HEAD_SIZE
    half = HEAD_SIZE // 2
    lanes = cos_ref.shape[1]
    cosine = cos_ref[...]
    sine = sin_ref[...]
    lane = lax.broadcasted_iota(jnp.int32, (rows, lanes), 1)
    source = pltpu.roll(lane, half, 1)
    partner_lane = jnp.where(lane % HEAD_SIZE < half, lane + half, lane - half)
    take_first = source == partner_lane
    block = WINDOW_TOKENS
    query_index = lax.broadcasted_iota(jnp.int32, (block, 2 * block), 0)
    key_index = lax.broadcasted_iota(jnp.int32, (block, 2 * block), 1)
    rel = query_index - key_index + block
    visible = []
    for part in range(rows // block):
        limit = limit_ref[part * block : (part + 1) * block, :]
        visible.append((rel >= 0) & (rel <= limit))
    heads_per_chunk = lanes // HEAD_SIZE
    rotated_heads = []
    for chunk in range(q_ref.shape[1] // lanes):
        x = q_ref[:, chunk * lanes : (chunk + 1) * lanes]
        first = pltpu.roll(x, half, 1)
        second = pltpu.roll(x, lanes - half, 1)
        partner = jnp.where(take_first, first, second)
        rotated = (x * cosine + partner * sine).astype(jnp.bfloat16)
        for inner in range(heads_per_chunk):
            rotated_heads.append(rotated[:, inner * HEAD_SIZE : (inner + 1) * HEAD_SIZE])
    sink_rows = jnp.concatenate(
        [jnp.full((block, 1), sinks_ref[group * query_group + head], jnp.float32) for head in range(query_group)],
        axis=0,
    )
    for part in range(rows // block):
        queries = jnp.concatenate(
            [head_rows[part * block : (part + 1) * block] for head_rows in rotated_heads], axis=0
        )
        keys = k_ref[0, part * block : part * block + 2 * block, :]
        values = v_ref[0, part * block : part * block + 2 * block, :]
        scores = lax.dot_general(
            queries, keys, (((1,), (1,)), ((), ())), preferred_element_type=jnp.float32
        ) * HEAD_SIZE ** (-0.5)
        seen = jnp.concatenate([visible[part]] * query_group, axis=0)
        scores = jnp.where(seen, scores, -1e30)
        top = jnp.maximum(jnp.max(scores, axis=1, keepdims=True), sink_rows)
        expo = jnp.exp(scores - top)
        total = jnp.sum(expo, axis=1, keepdims=True) + jnp.exp(sink_rows - top)
        probs = (expo / total).astype(jnp.bfloat16)
        out = jnp.dot(probs, values, preferred_element_type=jnp.float32).astype(jnp.bfloat16)
        for head in range(query_group):
            out_ref[part * block : (part + 1) * block, head * HEAD_SIZE : (head + 1) * HEAD_SIZE] = out[
                head * block : (head + 1) * block
            ]


def rotation_tables(positions, lanes):
    half = HEAD_SIZE // 2
    freq = 150000.0 ** (-(jnp.arange(half, dtype=jnp.float32) * 2.0 / HEAD_SIZE))
    angle = positions.astype(jnp.float32)[:, None] * freq[None, :]
    cosine = jnp.cos(angle)
    sine = jnp.sin(angle)
    repeats = lanes // HEAD_SIZE
    cos_table = jnp.tile(jnp.concatenate([cosine, cosine], axis=1), (1, repeats))
    sin_table = jnp.tile(jnp.concatenate([-sine, sine], axis=1), (1, repeats))
    return cos_table, sin_table


def attend(combined_output, joined_keys, joined_values, tables, sinks):
    token_rows = combined_output.shape[0]
    query_group = QUERY_HEADS // KEY_VALUE_HEADS
    group_width = query_group * HEAD_SIZE
    cos_table, sin_table, limit = tables
    lanes = cos_table.shape[1]
    keys = jnp.moveaxis(joined_keys, 1, 0)
    values = jnp.moveaxis(joined_values, 1, 0)
    key_rows = keys.shape[1]
    return pl.pallas_call(
        attention_kernel,
        grid=(KEY_VALUE_HEADS,),
        in_specs=[
            pl.BlockSpec(memory_space=pltpu.SMEM),
            pl.BlockSpec((token_rows, 1), lambda g: (0, 0)),
            pl.BlockSpec((token_rows, lanes), lambda g: (0, 0)),
            pl.BlockSpec((token_rows, lanes), lambda g: (0, 0)),
            pl.BlockSpec((token_rows, group_width), lambda g: (0, g)),
            pl.BlockSpec((1, key_rows, HEAD_SIZE), lambda g: (g, 0, 0)),
            pl.BlockSpec((1, key_rows, HEAD_SIZE), lambda g: (g, 0, 0)),
        ],
        out_specs=pl.BlockSpec((token_rows, group_width), lambda g: (0, g)),
        out_shape=jax.ShapeDtypeStruct((token_rows, QUERY_HEADS * HEAD_SIZE), jnp.bfloat16),
    )(sinks, limit, cos_table, sin_table, combined_output, keys, values)


def send_rim(window_output, token_rows):
    return shifted(window_output[:, token_rows - WINDOW_TOKENS :], "ctx", 1)


def split_mixed(combined_output, positions, token_rows, query_length, key_length):
    key_rows = apply_rotation(
        combined_output[:, query_length : query_length + key_length].reshape(
            token_rows, KEY_VALUE_HEADS, HEAD_SIZE
        ),
        positions,
    ).astype(jnp.bfloat16)
    value_rows = combined_output[:, query_length + key_length :].astype(jnp.bfloat16)
    window_output = jnp.stack([key_rows.reshape(token_rows, key_length), value_rows])
    received = send_rim(window_output, token_rows)
    query_rows = apply_rotation(
        combined_output[:, :query_length].reshape(token_rows, QUERY_HEADS, HEAD_SIZE), positions
    ).astype(jnp.bfloat16)
    return (window_output, received, query_rows)


def gather_weight(qkv_weight):
    pairs = lax.axis_size("dp")
    columns = qkv_weight.shape[1]
    if columns % pairs:
        return lax.all_gather(qkv_weight.T, "ctx", axis=0, tiled=True)
    piece = columns // pairs
    own = lax.dynamic_slice_in_dim(qkv_weight, lax.axis_index("dp") * piece, piece, axis=1)
    return lax.all_gather(own.T, ("ctx", "dp"), axis=0, tiled=True)


def on_device(
    tokens, positions, norm_gain, qkv_weight, qkv_bias, sinks, earlier_keys, earlier_values
):
    token_rows = tokens.shape[0]
    query_group = QUERY_HEADS // KEY_VALUE_HEADS
    query_length = QUERY_HEADS * HEAD_SIZE
    key_length = KEY_VALUE_HEADS * HEAD_SIZE
    flat = tokens.astype(jnp.float32)
    scale = lax.rsqrt(jnp.mean(flat * flat, axis=-1, keepdims=True) + 1e-05)
    normed = (flat * scale * norm_gain[None, :]).astype(jnp.bfloat16)
    tables = rotation_tables(positions, 128) + (
        jnp.minimum(positions, WINDOW_TOKENS - 1).astype(jnp.int32)[:, None],
    )
    normed, tables = lax.optimization_barrier((normed, tables))
    combined_output = lax.dot_general(
        normed,
        gather_weight(qkv_weight),
        (((1,), (1,)), ((), ())),
        preferred_element_type=jnp.float32,
    )
    combined_output = combined_output + qkv_bias[None, :]
    key_rows = apply_rotation(
        combined_output[:, query_length : query_length + key_length].reshape(
            token_rows, KEY_VALUE_HEADS, HEAD_SIZE
        ),
        positions,
    ).astype(jnp.bfloat16)
    value_rows = combined_output[:, query_length + key_length :].astype(jnp.bfloat16)
    window_output = jnp.stack([key_rows.reshape(token_rows, key_length), value_rows])
    received = send_rim(window_output, token_rows)
    prior = jnp.stack([earlier_keys, earlier_values])
    border_tokens = jnp.where(lax.axis_index("ctx") == 0, prior, received)
    padded_rows = jnp.concatenate([border_tokens, window_output], axis=1).reshape(
        2, WINDOW_TOKENS + token_rows, KEY_VALUE_HEADS, HEAD_SIZE
    )
    return attend(combined_output, padded_rows[0], padded_rows[1], tables, sinks)


def solution(mesh):
    placed = (
        P(("dp", "ctx"), None),
        P(("dp", "ctx")),
        P(),
        P(None, "ctx"),
        P(),
        P(),
        P("dp", None),
        P("dp", None),
    )
    return jax.shard_map(
        on_device, mesh=mesh, in_specs=placed, out_specs=P(("dp", "ctx"), None), check_vma=False
    )
```

```python
import jax
import jax.numpy as jnp
from jax import lax
from jax.experimental import pallas as pl
from jax.experimental.pallas import tpu as pltpu
from jax.sharding import PartitionSpec as P

QUERY_HEADS = 32
KEY_VALUE_HEADS = 4
HEAD_SIZE = 64
WINDOW_TOKENS = 128


def shifted(value, axis, steps):
    count = lax.axis_size(axis)
    leading, last = (max(0, -steps), min(count, count - steps))
    return lax.ppermute(value, axis, [(source, source + steps) for source in range(leading, last)])


def apply_rotation(heads, positions):
    half = heads.shape[-1] // 2
    freq = 150000.0 ** (-(jnp.arange(half, dtype=jnp.float32) * 2.0 / heads.shape[-1]))
    angle = positions.astype(jnp.float32)[:, None] * freq[None, :]
    cosine = jnp.cos(angle)[:, None, :]
    sine = jnp.sin(angle)[:, None, :]
    first = heads[..., :half]
    second = heads[..., half:]
    return jnp.concatenate(
        [first * cosine - second * sine, second * cosine + first * sine], axis=-1
    )


def attend_head(query_rows, key_rows, value_rows, sink_row, visible):
    scores = jnp.einsum(
        "nrgd,nkd->ngrk", query_rows, key_rows, preferred_element_type=jnp.float32
    ) * HEAD_SIZE ** (-0.5)
    scores = jnp.where(visible[:, None], scores, -1e30)
    top = jnp.maximum(jnp.max(scores, axis=-1), sink_row[None, :, None])
    expo = jnp.exp(scores - top[..., None])
    total = jnp.sum(expo, axis=-1) + jnp.exp(sink_row[None, :, None] - top)
    probs = (expo / total[..., None]).astype(jnp.bfloat16)
    out = jnp.einsum("ngrk,nkd->nrgd", probs, value_rows, preferred_element_type=jnp.float32)
    return out.astype(jnp.bfloat16)


def attention_kernel(sinks_ref, limit_ref, cos_ref, sin_ref, q_ref, k_ref, v_ref, out_ref):
    group = pl.program_id(0)
    rows = q_ref.shape[0]
    query_group = q_ref.shape[1] // HEAD_SIZE
    half = HEAD_SIZE // 2
    lanes = cos_ref.shape[1]
    cosine = cos_ref[...]
    sine = sin_ref[...]
    lane = lax.broadcasted_iota(jnp.int32, (rows, lanes), 1)
    source = pltpu.roll(lane, half, 1)
    partner_lane = jnp.where(lane % HEAD_SIZE < half, lane + half, lane - half)
    take_first = source == partner_lane
    block = WINDOW_TOKENS
    query_index = lax.broadcasted_iota(jnp.int32, (block, 2 * block), 0)
    key_index = lax.broadcasted_iota(jnp.int32, (block, 2 * block), 1)
    rel = query_index - key_index + block
    visible = []
    for part in range(rows // block):
        limit = limit_ref[part * block : (part + 1) * block, :]
        visible.append((rel >= 0) & (rel <= limit))
    heads_per_chunk = lanes // HEAD_SIZE
    for chunk in range(q_ref.shape[1] // lanes):
        x = q_ref[:, chunk * lanes : (chunk + 1) * lanes]
        first = pltpu.roll(x, half, 1)
        second = pltpu.roll(x, lanes - half, 1)
        partner = jnp.where(take_first, first, second)
        rotated = ((x * cosine + partner * sine) * HEAD_SIZE ** (-0.5)).astype(jnp.bfloat16)
        for inner in range(heads_per_chunk):
            head = chunk * heads_per_chunk + inner
            sink = sinks_ref[group * query_group + head]
            query_head = rotated[:, inner * HEAD_SIZE : (inner + 1) * HEAD_SIZE]
            for part in range(rows // block):
                queries = query_head[part * block : (part + 1) * block]
                keys = k_ref[0, part * block : part * block + 2 * block, :]
                values = v_ref[0, part * block : part * block + 2 * block, :]
                scores = lax.dot_general(
                    queries, keys, (((1,), (1,)), ((), ())), preferred_element_type=jnp.float32
                )
                scores = jnp.where(visible[part], scores, -1e30)
                top = jnp.maximum(jnp.max(scores, axis=1, keepdims=True), sink)
                expo = jnp.exp(scores - top)
                total = jnp.sum(expo, axis=1, keepdims=True) + jnp.exp(sink - top)
                probs = (expo * (1.0 / total)).astype(jnp.bfloat16)
                out = jnp.dot(probs, values, preferred_element_type=jnp.float32)
                out_ref[part * block : (part + 1) * block, head * HEAD_SIZE : (head + 1) * HEAD_SIZE] = out.astype(
                    jnp.bfloat16
                )


def rotation_tables(positions, lanes):
    half = HEAD_SIZE // 2
    freq = 150000.0 ** (-(jnp.arange(half, dtype=jnp.float32) * 2.0 / HEAD_SIZE))
    angle = positions.astype(jnp.float32)[:, None] * freq[None, :]
    cosine = jnp.cos(angle)
    sine = jnp.sin(angle)
    repeats = lanes // HEAD_SIZE
    cos_table = jnp.tile(jnp.concatenate([cosine, cosine], axis=1), (1, repeats))
    sin_table = jnp.tile(jnp.concatenate([-sine, sine], axis=1), (1, repeats))
    return cos_table, sin_table


def attend(combined_output, joined_keys, joined_values, tables, sinks):
    token_rows = combined_output.shape[0]
    query_group = QUERY_HEADS // KEY_VALUE_HEADS
    group_width = query_group * HEAD_SIZE
    cos_table, sin_table, limit = tables
    lanes = cos_table.shape[1]
    keys = jnp.moveaxis(joined_keys, 1, 0)
    values = jnp.moveaxis(joined_values, 1, 0)
    key_rows = keys.shape[1]
    return pl.pallas_call(
        attention_kernel,
        grid=(KEY_VALUE_HEADS,),
        in_specs=[
            pl.BlockSpec(memory_space=pltpu.SMEM),
            pl.BlockSpec((token_rows, 1), lambda g: (0, 0)),
            pl.BlockSpec((token_rows, lanes), lambda g: (0, 0)),
            pl.BlockSpec((token_rows, lanes), lambda g: (0, 0)),
            pl.BlockSpec((token_rows, group_width), lambda g: (0, g)),
            pl.BlockSpec((1, key_rows, HEAD_SIZE), lambda g: (g, 0, 0)),
            pl.BlockSpec((1, key_rows, HEAD_SIZE), lambda g: (g, 0, 0)),
        ],
        out_specs=pl.BlockSpec((token_rows, group_width), lambda g: (0, g)),
        out_shape=jax.ShapeDtypeStruct((token_rows, QUERY_HEADS * HEAD_SIZE), jnp.bfloat16),
    )(sinks, limit, cos_table, sin_table, combined_output, keys, values)


def send_rim(window_output, token_rows):
    return shifted(window_output[:, token_rows - WINDOW_TOKENS :], "ctx", 1)


def split_mixed(combined_output, positions, token_rows, query_length, key_length):
    key_rows = apply_rotation(
        combined_output[:, query_length : query_length + key_length].reshape(
            token_rows, KEY_VALUE_HEADS, HEAD_SIZE
        ),
        positions,
    ).astype(jnp.bfloat16)
    value_rows = combined_output[:, query_length + key_length :].astype(jnp.bfloat16)
    window_output = jnp.stack([key_rows.reshape(token_rows, key_length), value_rows])
    received = send_rim(window_output, token_rows)
    query_rows = apply_rotation(
        combined_output[:, :query_length].reshape(token_rows, QUERY_HEADS, HEAD_SIZE), positions
    ).astype(jnp.bfloat16)
    return (window_output, received, query_rows)


def gather_weight(qkv_weight):
    pairs = lax.axis_size("dp")
    columns = qkv_weight.shape[1]
    if columns % pairs:
        return lax.all_gather(qkv_weight.T, "ctx", axis=0, tiled=True)
    piece = columns // pairs
    own = lax.dynamic_slice_in_dim(qkv_weight, lax.axis_index("dp") * piece, piece, axis=1)
    return lax.all_gather(own.T, ("ctx", "dp"), axis=0, tiled=True)


def on_device(
    tokens, positions, norm_gain, qkv_weight, qkv_bias, sinks, earlier_keys, earlier_values
):
    token_rows = tokens.shape[0]
    query_group = QUERY_HEADS // KEY_VALUE_HEADS
    query_length = QUERY_HEADS * HEAD_SIZE
    key_length = KEY_VALUE_HEADS * HEAD_SIZE
    flat = tokens.astype(jnp.float32)
    scale = lax.rsqrt(jnp.mean(flat * flat, axis=-1, keepdims=True) + 1e-05)
    normed = (flat * scale * norm_gain[None, :]).astype(jnp.bfloat16)
    tables = rotation_tables(positions, 128) + (
        jnp.minimum(positions, WINDOW_TOKENS - 1).astype(jnp.int32)[:, None],
    )
    normed, tables = lax.optimization_barrier((normed, tables))
    combined_output = lax.dot_general(
        normed,
        gather_weight(qkv_weight),
        (((1,), (1,)), ((), ())),
        preferred_element_type=jnp.float32,
    )
    combined_output = combined_output + qkv_bias[None, :]
    key_rows = apply_rotation(
        combined_output[:, query_length : query_length + key_length].reshape(
            token_rows, KEY_VALUE_HEADS, HEAD_SIZE
        ),
        positions,
    ).astype(jnp.bfloat16)
    value_rows = combined_output[:, query_length + key_length :].astype(jnp.bfloat16)
    window_output = jnp.stack([key_rows.reshape(token_rows, key_length), value_rows])
    received = send_rim(window_output, token_rows)
    prior = jnp.stack([earlier_keys, earlier_values])
    border_tokens = jnp.where(lax.axis_index("ctx") == 0, prior, received)
    padded_rows = jnp.concatenate([border_tokens, window_output], axis=1).reshape(
        2, WINDOW_TOKENS + token_rows, KEY_VALUE_HEADS, HEAD_SIZE
    )
    return attend(combined_output, padded_rows[0], padded_rows[1], tables, sinks)


def solution(mesh):
    placed = (
        P(("dp", "ctx"), None),
        P(("dp", "ctx")),
        P(),
        P(None, "ctx"),
        P(),
        P(),
        P("dp", None),
        P("dp", None),
    )
    return jax.shard_map(
        on_device, mesh=mesh, in_specs=placed, out_specs=P(("dp", "ctx"), None), check_vma=False
    )
```

```python
import jax
import jax.numpy as jnp
from jax import lax
from jax.experimental import pallas as pl
from jax.experimental.pallas import tpu as pltpu
from jax.sharding import PartitionSpec as P

QUERY_HEADS = 32
KEY_VALUE_HEADS = 4
HEAD_SIZE = 64
WINDOW_TOKENS = 128


def shifted(value, axis, steps):
    count = lax.axis_size(axis)
    leading, last = (max(0, -steps), min(count, count - steps))
    return lax.ppermute(value, axis, [(source, source + steps) for source in range(leading, last)])


def apply_rotation(heads, positions):
    half = heads.shape[-1] // 2
    freq = 150000.0 ** (-(jnp.arange(half, dtype=jnp.float32) * 2.0 / heads.shape[-1]))
    angle = positions.astype(jnp.float32)[:, None] * freq[None, :]
    cosine = jnp.cos(angle)[:, None, :]
    sine = jnp.sin(angle)[:, None, :]
    first = heads[..., :half]
    second = heads[..., half:]
    return jnp.concatenate(
        [first * cosine - second * sine, second * cosine + first * sine], axis=-1
    )


def attend_head(query_rows, key_rows, value_rows, sink_row, visible):
    scores = jnp.einsum(
        "nrgd,nkd->ngrk", query_rows, key_rows, preferred_element_type=jnp.float32
    ) * HEAD_SIZE ** (-0.5)
    scores = jnp.where(visible[:, None], scores, -1e30)
    top = jnp.maximum(jnp.max(scores, axis=-1), sink_row[None, :, None])
    expo = jnp.exp(scores - top[..., None])
    total = jnp.sum(expo, axis=-1) + jnp.exp(sink_row[None, :, None] - top)
    probs = (expo / total[..., None]).astype(jnp.bfloat16)
    out = jnp.einsum("ngrk,nkd->nrgd", probs, value_rows, preferred_element_type=jnp.float32)
    return out.astype(jnp.bfloat16)


def attention_kernel(sinks_ref, limit_ref, cos_ref, sin_ref, q_ref, k_ref, v_ref, out_ref):
    group = pl.program_id(0)
    rows = q_ref.shape[0]
    query_group = q_ref.shape[1] // HEAD_SIZE
    half = HEAD_SIZE // 2
    lanes = cos_ref.shape[1]
    cosine = cos_ref[...]
    sine = sin_ref[...]
    lane = lax.broadcasted_iota(jnp.int32, (rows, lanes), 1)
    source = pltpu.roll(lane, half, 1)
    partner_lane = jnp.where(lane % HEAD_SIZE < half, lane + half, lane - half)
    take_first = source == partner_lane
    block = WINDOW_TOKENS
    query_index = lax.broadcasted_iota(jnp.int32, (block, 2 * block), 0)
    key_index = lax.broadcasted_iota(jnp.int32, (block, 2 * block), 1)
    rel = query_index - key_index + block
    visible = []
    for part in range(rows // block):
        limit = limit_ref[part * block : (part + 1) * block, :]
        visible.append((rel >= 0) & (rel <= limit))
    heads_per_chunk = lanes // HEAD_SIZE
    for chunk in range(q_ref.shape[1] // lanes):
        x = q_ref[:, chunk * lanes : (chunk + 1) * lanes]
        first = pltpu.roll(x, half, 1)
        second = pltpu.roll(x, lanes - half, 1)
        partner = jnp.where(take_first, first, second)
        rotated = (x * cosine + partner * sine).astype(jnp.bfloat16)
        for inner in range(heads_per_chunk):
            head = chunk * heads_per_chunk + inner
            sink = sinks_ref[group * query_group + head]
            query_head = rotated[:, inner * HEAD_SIZE : (inner + 1) * HEAD_SIZE]
            for part in range(rows // block):
                queries = query_head[part * block : (part + 1) * block]
                keys = k_ref[0, part * block : part * block + 2 * block, :]
                values = v_ref[0, part * block : part * block + 2 * block, :]
                scores = lax.dot_general(
                    queries, keys, (((1,), (1,)), ((), ())), preferred_element_type=jnp.float32
                ) * HEAD_SIZE ** (-0.5)
                scores = jnp.where(visible[part], scores, -1e30)
                top = jnp.maximum(jnp.max(scores, axis=1, keepdims=True), sink)
                expo = jnp.exp(scores - top)
                total = jnp.sum(expo, axis=1, keepdims=True) + jnp.exp(sink - top)
                probs = (expo / total).astype(jnp.bfloat16)
                out = jnp.dot(probs, values, preferred_element_type=jnp.float32)
                out_ref[part * block : (part + 1) * block, head * HEAD_SIZE : (head + 1) * HEAD_SIZE] = out.astype(
                    jnp.bfloat16
                )


def rotation_tables(positions, lanes):
    half = HEAD_SIZE // 2
    freq = 150000.0 ** (-(jnp.arange(half, dtype=jnp.float32) * 2.0 / HEAD_SIZE))
    angle = positions.astype(jnp.float32)[:, None] * freq[None, :]
    cosine = jnp.cos(angle)
    sine = jnp.sin(angle)
    repeats = lanes // HEAD_SIZE
    cos_table = jnp.tile(jnp.concatenate([cosine, cosine], axis=1), (1, repeats))
    sin_table = jnp.tile(jnp.concatenate([-sine, sine], axis=1), (1, repeats))
    return cos_table, sin_table


def attend(combined_output, joined_keys, joined_values, tables, sinks):
    token_rows = combined_output.shape[0]
    query_group = QUERY_HEADS // KEY_VALUE_HEADS
    group_width = query_group * HEAD_SIZE
    cos_table, sin_table, limit = tables
    lanes = cos_table.shape[1]
    keys = jnp.moveaxis(joined_keys, 1, 0)
    values = jnp.moveaxis(joined_values, 1, 0)
    key_rows = keys.shape[1]
    return pl.pallas_call(
        attention_kernel,
        grid=(KEY_VALUE_HEADS,),
        in_specs=[
            pl.BlockSpec(memory_space=pltpu.SMEM),
            pl.BlockSpec((token_rows, 1), lambda g: (0, 0)),
            pl.BlockSpec((token_rows, lanes), lambda g: (0, 0)),
            pl.BlockSpec((token_rows, lanes), lambda g: (0, 0)),
            pl.BlockSpec((token_rows, group_width), lambda g: (0, g)),
            pl.BlockSpec((1, key_rows, HEAD_SIZE), lambda g: (g, 0, 0)),
            pl.BlockSpec((1, key_rows, HEAD_SIZE), lambda g: (g, 0, 0)),
        ],
        out_specs=pl.BlockSpec((token_rows, group_width), lambda g: (0, g)),
        out_shape=jax.ShapeDtypeStruct((token_rows, QUERY_HEADS * HEAD_SIZE), jnp.bfloat16),
    )(sinks, limit, cos_table, sin_table, combined_output, keys, values)


def send_rim(window_output, token_rows):
    return shifted(window_output[:, token_rows - WINDOW_TOKENS :], "ctx", 1)


def split_mixed(combined_output, positions, token_rows, query_length, key_length):
    key_rows = apply_rotation(
        combined_output[:, query_length : query_length + key_length].reshape(
            token_rows, KEY_VALUE_HEADS, HEAD_SIZE
        ),
        positions,
    ).astype(jnp.bfloat16)
    value_rows = combined_output[:, query_length + key_length :].astype(jnp.bfloat16)
    window_output = jnp.stack([key_rows.reshape(token_rows, key_length), value_rows])
    received = send_rim(window_output, token_rows)
    query_rows = apply_rotation(
        combined_output[:, :query_length].reshape(token_rows, QUERY_HEADS, HEAD_SIZE), positions
    ).astype(jnp.bfloat16)
    return (window_output, received, query_rows)


def gather_weight(qkv_weight):
    pairs = lax.axis_size("dp")
    columns = qkv_weight.shape[1]
    if columns % pairs:
        return lax.all_gather(qkv_weight.T, "ctx", axis=0, tiled=True)
    piece = columns // pairs
    own = lax.dynamic_slice_in_dim(qkv_weight, lax.axis_index("dp") * piece, piece, axis=1)
    flat = lax.all_gather(own.T.reshape(-1), ("ctx", "dp"), axis=0, tiled=True)
    return flat.reshape(columns * lax.axis_size("ctx"), qkv_weight.shape[0])


def on_device(
    tokens, positions, norm_gain, qkv_weight, qkv_bias, sinks, earlier_keys, earlier_values
):
    token_rows = tokens.shape[0]
    query_group = QUERY_HEADS // KEY_VALUE_HEADS
    query_length = QUERY_HEADS * HEAD_SIZE
    key_length = KEY_VALUE_HEADS * HEAD_SIZE
    flat = tokens.astype(jnp.float32)
    scale = lax.rsqrt(jnp.mean(flat * flat, axis=-1, keepdims=True) + 1e-05)
    normed = (flat * scale * norm_gain[None, :]).astype(jnp.bfloat16)
    tables = rotation_tables(positions, 128) + (
        jnp.minimum(positions, WINDOW_TOKENS - 1).astype(jnp.int32)[:, None],
    )
    normed, tables = lax.optimization_barrier((normed, tables))
    combined_output = lax.dot_general(
        normed,
        gather_weight(qkv_weight),
        (((1,), (1,)), ((), ())),
        preferred_element_type=jnp.float32,
    )
    combined_output = combined_output + qkv_bias[None, :]
    key_rows = apply_rotation(
        combined_output[:, query_length : query_length + key_length].reshape(
            token_rows, KEY_VALUE_HEADS, HEAD_SIZE
        ),
        positions,
    ).astype(jnp.bfloat16)
    value_rows = combined_output[:, query_length + key_length :].astype(jnp.bfloat16)
    window_output = jnp.stack([key_rows.reshape(token_rows, key_length), value_rows])
    received = send_rim(window_output, token_rows)
    prior = jnp.stack([earlier_keys, earlier_values])
    border_tokens = jnp.where(lax.axis_index("ctx") == 0, prior, received)
    padded_rows = jnp.concatenate([border_tokens, window_output], axis=1).reshape(
        2, WINDOW_TOKENS + token_rows, KEY_VALUE_HEADS, HEAD_SIZE
    )
    return attend(combined_output, padded_rows[0], padded_rows[1], tables, sinks)


def solution(mesh):
    placed = (
        P(("dp", "ctx"), None),
        P(("dp", "ctx")),
        P(),
        P(None, "ctx"),
        P(),
        P(),
        P("dp", None),
        P("dp", None),
    )
    return jax.shard_map(
        on_device, mesh=mesh, in_specs=placed, out_specs=P(("dp", "ctx"), None), check_vma=False
    )
```

```python
import jax
import jax.numpy as jnp
from jax import lax
from jax.experimental import pallas as pl
from jax.experimental.pallas import tpu as pltpu
from jax.sharding import PartitionSpec as P

QUERY_HEADS = 32
KEY_VALUE_HEADS = 4
HEAD_SIZE = 64
WINDOW_TOKENS = 128


def shifted(value, axis, steps):
    count = lax.axis_size(axis)
    leading, last = (max(0, -steps), min(count, count - steps))
    return lax.ppermute(value, axis, [(source, source + steps) for source in range(leading, last)])


def apply_rotation(heads, positions):
    half = heads.shape[-1] // 2
    freq = 150000.0 ** (-(jnp.arange(half, dtype=jnp.float32) * 2.0 / heads.shape[-1]))
    angle = positions.astype(jnp.float32)[:, None] * freq[None, :]
    cosine = jnp.cos(angle)[:, None, :]
    sine = jnp.sin(angle)[:, None, :]
    first = heads[..., :half]
    second = heads[..., half:]
    return jnp.concatenate(
        [first * cosine - second * sine, second * cosine + first * sine], axis=-1
    )


def attend_head(query_rows, key_rows, value_rows, sink_row, visible):
    scores = jnp.einsum(
        "nrgd,nkd->ngrk", query_rows, key_rows, preferred_element_type=jnp.float32
    ) * HEAD_SIZE ** (-0.5)
    scores = jnp.where(visible[:, None], scores, -1e30)
    top = jnp.maximum(jnp.max(scores, axis=-1), sink_row[None, :, None])
    expo = jnp.exp(scores - top[..., None])
    total = jnp.sum(expo, axis=-1) + jnp.exp(sink_row[None, :, None] - top)
    probs = (expo / total[..., None]).astype(jnp.bfloat16)
    out = jnp.einsum("ngrk,nkd->nrgd", probs, value_rows, preferred_element_type=jnp.float32)
    return out.astype(jnp.bfloat16)


def attention_kernel(sinks_ref, limit_ref, cos_ref, sin_ref, q_ref, k_ref, v_ref, out_ref):
    group = pl.program_id(0)
    rows = q_ref.shape[0]
    query_group = q_ref.shape[1] // HEAD_SIZE
    half = HEAD_SIZE // 2
    lanes = cos_ref.shape[1]
    cosine = cos_ref[...]
    sine = sin_ref[...]
    lane = lax.broadcasted_iota(jnp.int32, (rows, lanes), 1)
    source = pltpu.roll(lane, half, 1)
    partner_lane = jnp.where(lane % HEAD_SIZE < half, lane + half, lane - half)
    take_first = source == partner_lane
    block = WINDOW_TOKENS
    key_index = lax.broadcasted_iota(jnp.int32, (2 * block, block), 0)
    query_index = lax.broadcasted_iota(jnp.int32, (2 * block, block), 1)
    rel = query_index - key_index + block
    visible = []
    for part in range(rows // block):
        limit = limit_ref[part : part + 1, :]
        visible.append((rel >= 0) & (rel <= limit))
    heads_per_chunk = lanes // HEAD_SIZE
    for chunk in range(q_ref.shape[1] // lanes):
        x = q_ref[:, chunk * lanes : (chunk + 1) * lanes]
        first = pltpu.roll(x, half, 1)
        second = pltpu.roll(x, lanes - half, 1)
        partner = jnp.where(take_first, first, second)
        rotated = ((x * cosine + partner * sine) * HEAD_SIZE ** (-0.5)).astype(jnp.bfloat16)
        for inner in range(heads_per_chunk):
            head = chunk * heads_per_chunk + inner
            sink = sinks_ref[group * query_group + head]
            query_head = rotated[:, inner * HEAD_SIZE : (inner + 1) * HEAD_SIZE]
            for part in range(rows // block):
                queries = query_head[part * block : (part + 1) * block]
                keys = k_ref[0, part * block : part * block + 2 * block, :]
                values = v_ref[0, :, part * block : part * block + 2 * block]
                scores = lax.dot_general(
                    keys, queries, (((1,), (1,)), ((), ())), preferred_element_type=jnp.float32
                )
                scores = jnp.where(visible[part], scores, -1e30)
                top = jnp.maximum(jnp.max(scores, axis=0, keepdims=True), sink)
                expo = jnp.exp(scores - top)
                total = jnp.sum(expo, axis=0, keepdims=True) + jnp.exp(sink - top)
                probs = (expo * (1.0 / total)).astype(jnp.bfloat16)
                out = jnp.dot(values, probs, preferred_element_type=jnp.float32)
                out_ref[part * block : (part + 1) * block, head * HEAD_SIZE : (head + 1) * HEAD_SIZE] = out.T.astype(
                    jnp.bfloat16
                )


def rotation_tables(positions, lanes):
    half = HEAD_SIZE // 2
    freq = 150000.0 ** (-(jnp.arange(half, dtype=jnp.float32) * 2.0 / HEAD_SIZE))
    angle = positions.astype(jnp.float32)[:, None] * freq[None, :]
    cosine = jnp.cos(angle)
    sine = jnp.sin(angle)
    repeats = lanes // HEAD_SIZE
    cos_table = jnp.tile(jnp.concatenate([cosine, cosine], axis=1), (1, repeats))
    sin_table = jnp.tile(jnp.concatenate([-sine, sine], axis=1), (1, repeats))
    return cos_table, sin_table


def attend(combined_output, joined_keys, joined_values, tables, sinks):
    token_rows = combined_output.shape[0]
    query_group = QUERY_HEADS // KEY_VALUE_HEADS
    group_width = query_group * HEAD_SIZE
    cos_table, sin_table, limit = tables
    lanes = cos_table.shape[1]
    keys = jnp.moveaxis(joined_keys, 1, 0)
    values = jnp.transpose(joined_values, (1, 2, 0))
    key_rows = keys.shape[1]
    return pl.pallas_call(
        attention_kernel,
        grid=(KEY_VALUE_HEADS,),
        in_specs=[
            pl.BlockSpec(memory_space=pltpu.SMEM),
            pl.BlockSpec(limit.shape, lambda g: (0, 0)),
            pl.BlockSpec((token_rows, lanes), lambda g: (0, 0)),
            pl.BlockSpec((token_rows, lanes), lambda g: (0, 0)),
            pl.BlockSpec((token_rows, group_width), lambda g: (0, g)),
            pl.BlockSpec((1, key_rows, HEAD_SIZE), lambda g: (g, 0, 0)),
            pl.BlockSpec((1, HEAD_SIZE, key_rows), lambda g: (g, 0, 0)),
        ],
        out_specs=pl.BlockSpec((token_rows, group_width), lambda g: (0, g)),
        out_shape=jax.ShapeDtypeStruct((token_rows, QUERY_HEADS * HEAD_SIZE), jnp.bfloat16),
    )(sinks, limit, cos_table, sin_table, combined_output, keys, values)


def send_rim(window_output, token_rows):
    return shifted(window_output[:, token_rows - WINDOW_TOKENS :], "ctx", 1)


def split_mixed(combined_output, positions, token_rows, query_length, key_length):
    key_rows = apply_rotation(
        combined_output[:, query_length : query_length + key_length].reshape(
            token_rows, KEY_VALUE_HEADS, HEAD_SIZE
        ),
        positions,
    ).astype(jnp.bfloat16)
    value_rows = combined_output[:, query_length + key_length :].astype(jnp.bfloat16)
    window_output = jnp.stack([key_rows.reshape(token_rows, key_length), value_rows])
    received = send_rim(window_output, token_rows)
    query_rows = apply_rotation(
        combined_output[:, :query_length].reshape(token_rows, QUERY_HEADS, HEAD_SIZE), positions
    ).astype(jnp.bfloat16)
    return (window_output, received, query_rows)


def gather_weight(qkv_weight):
    pairs = lax.axis_size("dp")
    columns = qkv_weight.shape[1]
    if columns % pairs:
        return lax.all_gather(qkv_weight.T, "ctx", axis=0, tiled=True)
    piece = columns // pairs
    own = lax.dynamic_slice_in_dim(qkv_weight, lax.axis_index("dp") * piece, piece, axis=1)
    return lax.all_gather(own.T, ("ctx", "dp"), axis=0, tiled=True)


def on_device(
    tokens, positions, norm_gain, qkv_weight, qkv_bias, sinks, earlier_keys, earlier_values
):
    token_rows = tokens.shape[0]
    query_group = QUERY_HEADS // KEY_VALUE_HEADS
    query_length = QUERY_HEADS * HEAD_SIZE
    key_length = KEY_VALUE_HEADS * HEAD_SIZE
    flat = tokens.astype(jnp.float32)
    scale = lax.rsqrt(jnp.mean(flat * flat, axis=-1, keepdims=True) + 1e-05)
    normed = (flat * scale * norm_gain[None, :]).astype(jnp.bfloat16)
    tables = rotation_tables(positions, 128) + (
        jnp.minimum(positions, WINDOW_TOKENS - 1).astype(jnp.int32).reshape(-1, WINDOW_TOKENS),
    )
    normed, tables = lax.optimization_barrier((normed, tables))
    combined_output = lax.dot_general(
        normed,
        gather_weight(qkv_weight),
        (((1,), (1,)), ((), ())),
        preferred_element_type=jnp.float32,
    )
    combined_output = combined_output + qkv_bias[None, :]
    key_rows = apply_rotation(
        combined_output[:, query_length : query_length + key_length].reshape(
            token_rows, KEY_VALUE_HEADS, HEAD_SIZE
        ),
        positions,
    ).astype(jnp.bfloat16)
    value_rows = combined_output[:, query_length + key_length :].astype(jnp.bfloat16)
    window_output = jnp.stack([key_rows.reshape(token_rows, key_length), value_rows])
    received = send_rim(window_output, token_rows)
    prior = jnp.stack([earlier_keys, earlier_values])
    border_tokens = jnp.where(lax.axis_index("ctx") == 0, prior, received)
    padded_rows = jnp.concatenate([border_tokens, window_output], axis=1).reshape(
        2, WINDOW_TOKENS + token_rows, KEY_VALUE_HEADS, HEAD_SIZE
    )
    return attend(combined_output, padded_rows[0], padded_rows[1], tables, sinks)


def solution(mesh):
    placed = (
        P(("dp", "ctx"), None),
        P(("dp", "ctx")),
        P(),
        P(None, "ctx"),
        P(),
        P(),
        P("dp", None),
        P("dp", None),
    )
    return jax.shard_map(
        on_device, mesh=mesh, in_specs=placed, out_specs=P(("dp", "ctx"), None), check_vma=False
    )
```

```python
import jax
import jax.numpy as jnp
from jax import lax
from jax.experimental import pallas as pl
from jax.experimental.pallas import tpu as pltpu
from jax.sharding import PartitionSpec as P

QUERY_HEADS = 32
KEY_VALUE_HEADS = 4
HEAD_SIZE = 64
WINDOW_TOKENS = 128


def shifted(value, axis, steps):
    count = lax.axis_size(axis)
    leading, last = (max(0, -steps), min(count, count - steps))
    return lax.ppermute(value, axis, [(source, source + steps) for source in range(leading, last)])


def apply_rotation(heads, positions):
    half = heads.shape[-1] // 2
    freq = 150000.0 ** (-(jnp.arange(half, dtype=jnp.float32) * 2.0 / heads.shape[-1]))
    angle = positions.astype(jnp.float32)[:, None] * freq[None, :]
    cosine = jnp.cos(angle)[:, None, :]
    sine = jnp.sin(angle)[:, None, :]
    first = heads[..., :half]
    second = heads[..., half:]
    return jnp.concatenate(
        [first * cosine - second * sine, second * cosine + first * sine], axis=-1
    )


def attend_head(query_rows, key_rows, value_rows, sink_row, visible):
    scores = jnp.einsum(
        "nrgd,nkd->ngrk", query_rows, key_rows, preferred_element_type=jnp.float32
    ) * HEAD_SIZE ** (-0.5)
    scores = jnp.where(visible[:, None], scores, -1e30)
    top = jnp.maximum(jnp.max(scores, axis=-1), sink_row[None, :, None])
    expo = jnp.exp(scores - top[..., None])
    total = jnp.sum(expo, axis=-1) + jnp.exp(sink_row[None, :, None] - top)
    probs = (expo / total[..., None]).astype(jnp.bfloat16)
    out = jnp.einsum("ngrk,nkd->nrgd", probs, value_rows, preferred_element_type=jnp.float32)
    return out.astype(jnp.bfloat16)


def attention_kernel(sinks_ref, limit_ref, cos_ref, sin_ref, q_ref, k_ref, v_ref, out_ref):
    group = pl.program_id(0)
    rows = q_ref.shape[0]
    query_group = q_ref.shape[1] // HEAD_SIZE
    half = HEAD_SIZE // 2
    lanes = cos_ref.shape[1]
    cosine = cos_ref[...]
    sine = sin_ref[...]
    lane = lax.broadcasted_iota(jnp.int32, (rows, lanes), 1)
    source = pltpu.roll(lane, half, 1)
    partner_lane = jnp.where(lane % HEAD_SIZE < half, lane + half, lane - half)
    take_first = source == partner_lane
    block = WINDOW_TOKENS
    query_index = lax.broadcasted_iota(jnp.int32, (block, 2 * block), 0)
    key_index = lax.broadcasted_iota(jnp.int32, (block, 2 * block), 1)
    rel = query_index - key_index + block
    visible = []
    for part in range(rows // block):
        limit = limit_ref[part * block : (part + 1) * block, :]
        visible.append((rel >= 0) & (rel <= limit))
    heads_per_chunk = lanes // HEAD_SIZE
    for chunk in range(q_ref.shape[1] // lanes):
        x = q_ref[:, chunk * lanes : (chunk + 1) * lanes]
        first = pltpu.roll(x, half, 1)
        second = pltpu.roll(x, lanes - half, 1)
        partner = jnp.where(take_first, first, second)
        rotated = ((x * cosine + partner * sine) * HEAD_SIZE ** (-0.5)).astype(jnp.bfloat16)
        for inner in range(heads_per_chunk):
            head = chunk * heads_per_chunk + inner
            sink = sinks_ref[group * query_group + head]
            query_head = rotated[:, inner * HEAD_SIZE : (inner + 1) * HEAD_SIZE]
            for part in range(rows // block):
                queries = query_head[part * block : (part + 1) * block]
                keys = k_ref[0, part * block : part * block + 2 * block, :]
                values = v_ref[0, part * block : part * block + 2 * block, :]
                scores = lax.dot_general(
                    queries, keys, (((1,), (1,)), ((), ())), preferred_element_type=jnp.float32
                )
                scores = jnp.where(visible[part], scores, -1e30)
                top = jnp.maximum(jnp.max(scores, axis=1, keepdims=True), sink)
                expo = jnp.exp(scores - top)
                total = jnp.sum(expo, axis=1, keepdims=True) + jnp.exp(sink - top)
                probs = (expo * (1.0 / total)).astype(jnp.bfloat16)
                out = jnp.dot(probs, values, preferred_element_type=jnp.float32)
                out_ref[part * block : (part + 1) * block, head * HEAD_SIZE : (head + 1) * HEAD_SIZE] = out.astype(
                    jnp.bfloat16
                )


def rotation_tables(positions, lanes):
    half = HEAD_SIZE // 2
    freq = 150000.0 ** (-(jnp.arange(half, dtype=jnp.float32) * 2.0 / HEAD_SIZE))
    angle = positions.astype(jnp.float32)[:, None] * freq[None, :]
    cosine = jnp.cos(angle)
    sine = jnp.sin(angle)
    repeats = lanes // HEAD_SIZE
    cos_table = jnp.tile(jnp.concatenate([cosine, cosine], axis=1), (1, repeats))
    sin_table = jnp.tile(jnp.concatenate([-sine, sine], axis=1), (1, repeats))
    return cos_table, sin_table


def attend(combined_output, joined_keys, joined_values, tables, sinks):
    token_rows = combined_output.shape[0]
    query_group = QUERY_HEADS // KEY_VALUE_HEADS
    group_width = query_group * HEAD_SIZE
    cos_table, sin_table, limit = tables
    lanes = cos_table.shape[1]
    keys = jnp.moveaxis(joined_keys, 1, 0)
    values = jnp.moveaxis(joined_values, 1, 0)
    key_rows = keys.shape[1]
    return pl.pallas_call(
        attention_kernel,
        grid=(KEY_VALUE_HEADS,),
        in_specs=[
            pl.BlockSpec(memory_space=pltpu.SMEM),
            pl.BlockSpec((token_rows, 1), lambda g: (0, 0)),
            pl.BlockSpec((token_rows, lanes), lambda g: (0, 0)),
            pl.BlockSpec((token_rows, lanes), lambda g: (0, 0)),
            pl.BlockSpec((token_rows, group_width), lambda g: (0, g)),
            pl.BlockSpec((1, key_rows, HEAD_SIZE), lambda g: (g, 0, 0)),
            pl.BlockSpec((1, key_rows, HEAD_SIZE), lambda g: (g, 0, 0)),
        ],
        out_specs=pl.BlockSpec((token_rows, group_width), lambda g: (0, g)),
        out_shape=jax.ShapeDtypeStruct((token_rows, QUERY_HEADS * HEAD_SIZE), jnp.bfloat16),
    )(sinks, limit, cos_table, sin_table, combined_output, keys, values)


def send_rim(window_output, token_rows):
    return shifted(window_output[:, token_rows - WINDOW_TOKENS :], "ctx", 1)


def split_mixed(combined_output, positions, token_rows, query_length, key_length):
    key_rows = apply_rotation(
        combined_output[:, query_length : query_length + key_length].reshape(
            token_rows, KEY_VALUE_HEADS, HEAD_SIZE
        ),
        positions,
    ).astype(jnp.bfloat16)
    value_rows = combined_output[:, query_length + key_length :].astype(jnp.bfloat16)
    window_output = jnp.stack([key_rows.reshape(token_rows, key_length), value_rows])
    received = send_rim(window_output, token_rows)
    query_rows = apply_rotation(
        combined_output[:, :query_length].reshape(token_rows, QUERY_HEADS, HEAD_SIZE), positions
    ).astype(jnp.bfloat16)
    return (window_output, received, query_rows)


def gather_weight(qkv_weight):
    pairs = lax.axis_size("dp")
    columns = qkv_weight.shape[1]
    if columns % pairs:
        return lax.all_gather(qkv_weight.T, "ctx", axis=0, tiled=True)
    piece = columns // pairs
    own = lax.dynamic_slice_in_dim(qkv_weight, lax.axis_index("dp") * piece, piece, axis=1)
    return lax.all_gather(own.T, ("ctx", "dp"), axis=0, tiled=True)


def norm_rows(rows, norm_gain):
    flat = rows.astype(jnp.float32)
    scale = lax.rsqrt(jnp.mean(flat * flat, axis=-1, keepdims=True) + 1e-05)
    return (flat * scale * norm_gain[None, :]).astype(jnp.bfloat16)


def on_device(
    tokens, positions, norm_gain, qkv_weight, qkv_bias, sinks, earlier_keys, earlier_values
):
    token_rows = tokens.shape[0]
    query_group = QUERY_HEADS // KEY_VALUE_HEADS
    query_length = QUERY_HEADS * HEAD_SIZE
    key_length = KEY_VALUE_HEADS * HEAD_SIZE
    rim_tokens = shifted(tokens[token_rows - WINDOW_TOKENS :], "ctx", 1)
    rim_positions = shifted(positions[token_rows - WINDOW_TOKENS :], "ctx", 1)
    normed = norm_rows(tokens, norm_gain)
    rim_normed = norm_rows(rim_tokens, norm_gain)
    tables = rotation_tables(positions, 128) + (
        jnp.minimum(positions, WINDOW_TOKENS - 1).astype(jnp.int32)[:, None],
    )
    normed, rim_normed, tables = lax.optimization_barrier((normed, rim_normed, tables))
    weight_rows = gather_weight(qkv_weight)
    combined_output = lax.dot_general(
        normed, weight_rows, (((1,), (1,)), ((), ())), preferred_element_type=jnp.float32
    )
    combined_output = combined_output + qkv_bias[None, :]
    rim_output = lax.dot_general(
        rim_normed,
        weight_rows[query_length:],
        (((1,), (1,)), ((), ())),
        preferred_element_type=jnp.float32,
    )
    rim_output = rim_output + qkv_bias[None, query_length:]
    rim_keys = apply_rotation(
        rim_output[:, :key_length].reshape(WINDOW_TOKENS, KEY_VALUE_HEADS, HEAD_SIZE), rim_positions
    ).astype(jnp.bfloat16)
    rim_values = rim_output[:, key_length:].astype(jnp.bfloat16)
    computed_rim = jnp.stack([rim_keys.reshape(WINDOW_TOKENS, key_length), rim_values])
    key_rows = apply_rotation(
        combined_output[:, query_length : query_length + key_length].reshape(
            token_rows, KEY_VALUE_HEADS, HEAD_SIZE
        ),
        positions,
    ).astype(jnp.bfloat16)
    value_rows = combined_output[:, query_length + key_length :].astype(jnp.bfloat16)
    window_output = jnp.stack([key_rows.reshape(token_rows, key_length), value_rows])
    prior = jnp.stack([earlier_keys, earlier_values])
    border_tokens = jnp.where(lax.axis_index("ctx") == 0, prior, computed_rim)
    padded_rows = jnp.concatenate([border_tokens, window_output], axis=1).reshape(
        2, WINDOW_TOKENS + token_rows, KEY_VALUE_HEADS, HEAD_SIZE
    )
    return attend(combined_output, padded_rows[0], padded_rows[1], tables, sinks)


def solution(mesh):
    placed = (
        P(("dp", "ctx"), None),
        P(("dp", "ctx")),
        P(),
        P(None, "ctx"),
        P(),
        P(),
        P("dp", None),
        P("dp", None),
    )
    return jax.shard_map(
        on_device, mesh=mesh, in_specs=placed, out_specs=P(("dp", "ctx"), None), check_vma=False
    )
```

```python
import jax
import jax.numpy as jnp
from jax import lax
from jax.experimental import pallas as pl
from jax.experimental.pallas import tpu as pltpu
from jax.sharding import PartitionSpec as P

QUERY_HEADS = 32
KEY_VALUE_HEADS = 4
HEAD_SIZE = 64
WINDOW_TOKENS = 128


def shifted(value, axis, steps):
    count = lax.axis_size(axis)
    leading, last = (max(0, -steps), min(count, count - steps))
    return lax.ppermute(value, axis, [(source, source + steps) for source in range(leading, last)])


def apply_rotation(heads, positions):
    half = heads.shape[-1] // 2
    freq = 150000.0 ** (-(jnp.arange(half, dtype=jnp.float32) * 2.0 / heads.shape[-1]))
    angle = positions.astype(jnp.float32)[:, None] * freq[None, :]
    cosine = jnp.cos(angle)[:, None, :]
    sine = jnp.sin(angle)[:, None, :]
    first = heads[..., :half]
    second = heads[..., half:]
    return jnp.concatenate(
        [first * cosine - second * sine, second * cosine + first * sine], axis=-1
    )


def attend_head(query_rows, key_rows, value_rows, sink_row, visible):
    scores = jnp.einsum(
        "nrgd,nkd->ngrk", query_rows, key_rows, preferred_element_type=jnp.float32
    ) * HEAD_SIZE ** (-0.5)
    scores = jnp.where(visible[:, None], scores, -1e30)
    top = jnp.maximum(jnp.max(scores, axis=-1), sink_row[None, :, None])
    expo = jnp.exp(scores - top[..., None])
    total = jnp.sum(expo, axis=-1) + jnp.exp(sink_row[None, :, None] - top)
    probs = (expo / total[..., None]).astype(jnp.bfloat16)
    out = jnp.einsum("ngrk,nkd->nrgd", probs, value_rows, preferred_element_type=jnp.float32)
    return out.astype(jnp.bfloat16)


def attention_kernel(sinks_ref, limit_ref, cos_ref, sin_ref, q_ref, k_ref, v_ref, out_ref):
    group = pl.program_id(0)
    rows = q_ref.shape[0]
    query_group = q_ref.shape[1] // HEAD_SIZE
    half = HEAD_SIZE // 2
    lanes = cos_ref.shape[1]
    cosine = cos_ref[...]
    sine = sin_ref[...]
    lane = lax.broadcasted_iota(jnp.int32, (rows, lanes), 1)
    source = pltpu.roll(lane, half, 1)
    partner_lane = jnp.where(lane % HEAD_SIZE < half, lane + half, lane - half)
    take_first = source == partner_lane
    block = WINDOW_TOKENS
    query_index = lax.broadcasted_iota(jnp.int32, (block, 2 * block), 0)
    key_index = lax.broadcasted_iota(jnp.int32, (block, 2 * block), 1)
    rel = query_index - key_index + block
    visible = []
    for part in range(rows // block):
        limit = limit_ref[part * block : (part + 1) * block, :]
        visible.append((rel >= 0) & (rel <= limit))
    heads_per_chunk = lanes // HEAD_SIZE
    for chunk in range(q_ref.shape[1] // lanes):
        x = q_ref[:, chunk * lanes : (chunk + 1) * lanes]
        first = pltpu.roll(x, half, 1)
        second = pltpu.roll(x, lanes - half, 1)
        partner = jnp.where(take_first, first, second)
        rotated = ((x * cosine + partner * sine) * HEAD_SIZE ** (-0.5)).astype(jnp.bfloat16)
        for inner in range(heads_per_chunk):
            head = chunk * heads_per_chunk + inner
            sink = sinks_ref[group * query_group + head]
            query_head = rotated[:, inner * HEAD_SIZE : (inner + 1) * HEAD_SIZE]
            for part in range(rows // block):
                queries = query_head[part * block : (part + 1) * block]
                keys = k_ref[0, part * block : part * block + 2 * block, :]
                values = v_ref[0, part * block : part * block + 2 * block, :]
                scores = lax.dot_general(
                    queries, keys, (((1,), (1,)), ((), ())), preferred_element_type=jnp.float32
                )
                scores = jnp.where(visible[part], scores, -1e30)
                top = jnp.maximum(jnp.max(scores, axis=1, keepdims=True), sink)
                expo = jnp.exp(scores - top)
                total = jnp.sum(expo, axis=1, keepdims=True) + jnp.exp(sink - top)
                probs = (expo * (1.0 / total)).astype(jnp.bfloat16)
                out = jnp.dot(probs, values, preferred_element_type=jnp.float32)
                out_ref[part * block : (part + 1) * block, head * HEAD_SIZE : (head + 1) * HEAD_SIZE] = out.astype(
                    jnp.bfloat16
                )


def rotation_tables(positions, lanes):
    half = HEAD_SIZE // 2
    freq = 150000.0 ** (-(jnp.arange(half, dtype=jnp.float32) * 2.0 / HEAD_SIZE))
    angle = positions.astype(jnp.float32)[:, None] * freq[None, :]
    cosine = jnp.cos(angle)
    sine = jnp.sin(angle)
    repeats = lanes // HEAD_SIZE
    cos_table = jnp.tile(jnp.concatenate([cosine, cosine], axis=1), (1, repeats))
    sin_table = jnp.tile(jnp.concatenate([-sine, sine], axis=1), (1, repeats))
    return cos_table, sin_table


def attend(combined_output, joined_keys, joined_values, tables, sinks):
    token_rows = combined_output.shape[0]
    query_group = QUERY_HEADS // KEY_VALUE_HEADS
    group_width = query_group * HEAD_SIZE
    cos_table, sin_table, limit = tables
    lanes = cos_table.shape[1]
    keys = jnp.moveaxis(joined_keys, 1, 0)
    values = jnp.moveaxis(joined_values, 1, 0)
    key_rows = keys.shape[1]
    return pl.pallas_call(
        attention_kernel,
        grid=(KEY_VALUE_HEADS,),
        in_specs=[
            pl.BlockSpec(memory_space=pltpu.SMEM),
            pl.BlockSpec((token_rows, 1), lambda g: (0, 0)),
            pl.BlockSpec((token_rows, lanes), lambda g: (0, 0)),
            pl.BlockSpec((token_rows, lanes), lambda g: (0, 0)),
            pl.BlockSpec((token_rows, group_width), lambda g: (0, g)),
            pl.BlockSpec((1, key_rows, HEAD_SIZE), lambda g: (g, 0, 0)),
            pl.BlockSpec((1, key_rows, HEAD_SIZE), lambda g: (g, 0, 0)),
        ],
        out_specs=pl.BlockSpec((token_rows, group_width), lambda g: (0, g)),
        out_shape=jax.ShapeDtypeStruct((token_rows, QUERY_HEADS * HEAD_SIZE), jnp.bfloat16),
    )(sinks, limit, cos_table, sin_table, combined_output, keys, values)


def send_rim(window_output, token_rows):
    return shifted(window_output[:, token_rows - WINDOW_TOKENS :], "ctx", 1)


def split_mixed(combined_output, positions, token_rows, query_length, key_length):
    key_rows = apply_rotation(
        combined_output[:, query_length : query_length + key_length].reshape(
            token_rows, KEY_VALUE_HEADS, HEAD_SIZE
        ),
        positions,
    ).astype(jnp.bfloat16)
    value_rows = combined_output[:, query_length + key_length :].astype(jnp.bfloat16)
    window_output = jnp.stack([key_rows.reshape(token_rows, key_length), value_rows])
    received = send_rim(window_output, token_rows)
    query_rows = apply_rotation(
        combined_output[:, :query_length].reshape(token_rows, QUERY_HEADS, HEAD_SIZE), positions
    ).astype(jnp.bfloat16)
    return (window_output, received, query_rows)


def gather_weight(qkv_weight):
    pairs = lax.axis_size("dp")
    columns = qkv_weight.shape[1]
    if columns % pairs:
        return lax.all_gather(qkv_weight.T, "ctx", axis=0, tiled=True)
    piece = columns // pairs
    own = lax.dynamic_slice_in_dim(qkv_weight, lax.axis_index("dp") * piece, piece, axis=1)
    return lax.all_gather(own.T, ("ctx", "dp"), axis=0, tiled=True)


def on_device(
    tokens, positions, norm_gain, qkv_weight, qkv_bias, sinks, earlier_keys, earlier_values
):
    token_rows = tokens.shape[0]
    query_group = QUERY_HEADS // KEY_VALUE_HEADS
    query_length = QUERY_HEADS * HEAD_SIZE
    key_length = KEY_VALUE_HEADS * HEAD_SIZE
    flat = tokens.astype(jnp.float32)
    scale = lax.rsqrt(jnp.mean(flat * flat, axis=-1, keepdims=True) + 1e-05)
    normed = (flat * scale * norm_gain[None, :]).astype(jnp.bfloat16)
    tables = rotation_tables(positions, 128) + (
        jnp.minimum(positions, WINDOW_TOKENS - 1).astype(jnp.int32)[:, None],
    )
    normed, tables = lax.optimization_barrier((normed, tables))
    weight_rows = gather_weight(qkv_weight)
    key_value_output = lax.dot_general(
        normed,
        weight_rows[query_length:],
        (((1,), (1,)), ((), ())),
        preferred_element_type=jnp.float32,
    )
    key_value_output = key_value_output + qkv_bias[None, query_length:]
    key_rows = apply_rotation(
        key_value_output[:, :key_length].reshape(token_rows, KEY_VALUE_HEADS, HEAD_SIZE),
        positions,
    ).astype(jnp.bfloat16)
    value_rows = key_value_output[:, key_length:].astype(jnp.bfloat16)
    combined_output = lax.dot_general(
        normed,
        weight_rows[:query_length],
        (((1,), (1,)), ((), ())),
        preferred_element_type=jnp.float32,
    )
    combined_output = combined_output + qkv_bias[None, :query_length]
    window_output = jnp.stack([key_rows.reshape(token_rows, key_length), value_rows])
    received = send_rim(window_output, token_rows)
    prior = jnp.stack([earlier_keys, earlier_values])
    border_tokens = jnp.where(lax.axis_index("ctx") == 0, prior, received)
    padded_rows = jnp.concatenate([border_tokens, window_output], axis=1).reshape(
        2, WINDOW_TOKENS + token_rows, KEY_VALUE_HEADS, HEAD_SIZE
    )
    return attend(combined_output, padded_rows[0], padded_rows[1], tables, sinks)


def solution(mesh):
    placed = (
        P(("dp", "ctx"), None),
        P(("dp", "ctx")),
        P(),
        P(None, "ctx"),
        P(),
        P(),
        P("dp", None),
        P("dp", None),
    )
    return jax.shard_map(
        on_device, mesh=mesh, in_specs=placed, out_specs=P(("dp", "ctx"), None), check_vma=False
    )
```

```python
import jax
import jax.numpy as jnp
from jax import lax
from jax.experimental import pallas as pl
from jax.experimental.pallas import tpu as pltpu
from jax.sharding import PartitionSpec as P

QUERY_HEADS = 32
KEY_VALUE_HEADS = 4
HEAD_SIZE = 64
WINDOW_TOKENS = 128


def shifted(value, axis, steps):
    count = lax.axis_size(axis)
    leading, last = (max(0, -steps), min(count, count - steps))
    return lax.ppermute(value, axis, [(source, source + steps) for source in range(leading, last)])


def apply_rotation(heads, positions):
    half = heads.shape[-1] // 2
    freq = 150000.0 ** (-(jnp.arange(half, dtype=jnp.float32) * 2.0 / heads.shape[-1]))
    angle = positions.astype(jnp.float32)[:, None] * freq[None, :]
    cosine = jnp.cos(angle)[:, None, :]
    sine = jnp.sin(angle)[:, None, :]
    first = heads[..., :half]
    second = heads[..., half:]
    return jnp.concatenate(
        [first * cosine - second * sine, second * cosine + first * sine], axis=-1
    )


def attend_head(query_rows, key_rows, value_rows, sink_row, visible):
    scores = jnp.einsum(
        "nrgd,nkd->ngrk", query_rows, key_rows, preferred_element_type=jnp.float32
    ) * HEAD_SIZE ** (-0.5)
    scores = jnp.where(visible[:, None], scores, -1e30)
    top = jnp.maximum(jnp.max(scores, axis=-1), sink_row[None, :, None])
    expo = jnp.exp(scores - top[..., None])
    total = jnp.sum(expo, axis=-1) + jnp.exp(sink_row[None, :, None] - top)
    probs = (expo / total[..., None]).astype(jnp.bfloat16)
    out = jnp.einsum("ngrk,nkd->nrgd", probs, value_rows, preferred_element_type=jnp.float32)
    return out.astype(jnp.bfloat16)


def attention_kernel(sinks_ref, limit_ref, cos_ref, sin_ref, q_ref, k_ref, v_ref, out_ref):
    rows = q_ref.shape[0]
    query_group = QUERY_HEADS // KEY_VALUE_HEADS
    group_width = query_group * HEAD_SIZE
    half = HEAD_SIZE // 2
    lanes = cos_ref.shape[1]
    cosine = cos_ref[...]
    sine = sin_ref[...]
    lane = lax.broadcasted_iota(jnp.int32, (rows, lanes), 1)
    source = pltpu.roll(lane, half, 1)
    partner_lane = jnp.where(lane % HEAD_SIZE < half, lane + half, lane - half)
    take_first = source == partner_lane
    block = WINDOW_TOKENS
    query_index = lax.broadcasted_iota(jnp.int32, (block, 2 * block), 0)
    key_index = lax.broadcasted_iota(jnp.int32, (block, 2 * block), 1)
    rel = query_index - key_index + block
    visible = []
    for part in range(rows // block):
        limit = limit_ref[part * block : (part + 1) * block, :]
        visible.append((rel >= 0) & (rel <= limit))
    heads_per_chunk = lanes // HEAD_SIZE
    for group in range(KEY_VALUE_HEADS):
        for chunk in range(group_width // lanes):
            offset = group * group_width + chunk * lanes
            x = q_ref[:, offset : offset + lanes]
            first = pltpu.roll(x, half, 1)
            second = pltpu.roll(x, lanes - half, 1)
            partner = jnp.where(take_first, first, second)
            rotated = ((x * cosine + partner * sine) * HEAD_SIZE ** (-0.5)).astype(jnp.bfloat16)
            for inner in range(heads_per_chunk):
                head = group * query_group + chunk * heads_per_chunk + inner
                sink = sinks_ref[head]
                query_head = rotated[:, inner * HEAD_SIZE : (inner + 1) * HEAD_SIZE]
                for part in range(rows // block):
                    queries = query_head[part * block : (part + 1) * block]
                    keys = k_ref[group, part * block : part * block + 2 * block, :]
                    values = v_ref[group, part * block : part * block + 2 * block, :]
                    scores = lax.dot_general(
                        queries, keys, (((1,), (1,)), ((), ())), preferred_element_type=jnp.float32
                    )
                    scores = jnp.where(visible[part], scores, -1e30)
                    top = jnp.maximum(jnp.max(scores, axis=1, keepdims=True), sink)
                    expo = jnp.exp(scores - top)
                    total = jnp.sum(expo, axis=1, keepdims=True) + jnp.exp(sink - top)
                    probs = (expo * (1.0 / total)).astype(jnp.bfloat16)
                    out = jnp.dot(probs, values, preferred_element_type=jnp.float32)
                    out_ref[part * block : (part + 1) * block, head * HEAD_SIZE : (head + 1) * HEAD_SIZE] = (
                        out.astype(jnp.bfloat16)
                    )


def rotation_tables(positions, lanes):
    half = HEAD_SIZE // 2
    freq = 150000.0 ** (-(jnp.arange(half, dtype=jnp.float32) * 2.0 / HEAD_SIZE))
    angle = positions.astype(jnp.float32)[:, None] * freq[None, :]
    cosine = jnp.cos(angle)
    sine = jnp.sin(angle)
    repeats = lanes // HEAD_SIZE
    cos_table = jnp.tile(jnp.concatenate([cosine, cosine], axis=1), (1, repeats))
    sin_table = jnp.tile(jnp.concatenate([-sine, sine], axis=1), (1, repeats))
    return cos_table, sin_table


def attend(combined_output, joined_keys, joined_values, tables, sinks):
    token_rows = combined_output.shape[0]
    query_group = QUERY_HEADS // KEY_VALUE_HEADS
    group_width = query_group * HEAD_SIZE
    cos_table, sin_table, limit = tables
    lanes = cos_table.shape[1]
    keys = jnp.moveaxis(joined_keys, 1, 0)
    values = jnp.moveaxis(joined_values, 1, 0)
    key_rows = keys.shape[1]
    in_vmem = pl.BlockSpec(memory_space=pltpu.VMEM)
    return pl.pallas_call(
        attention_kernel,
        in_specs=[pl.BlockSpec(memory_space=pltpu.SMEM)] + [in_vmem] * 6,
        out_specs=in_vmem,
        out_shape=jax.ShapeDtypeStruct((token_rows, QUERY_HEADS * HEAD_SIZE), jnp.bfloat16),
    )(sinks, limit, cos_table, sin_table, combined_output, keys, values)


def send_rim(window_output, token_rows):
    return shifted(window_output[:, token_rows - WINDOW_TOKENS :], "ctx", 1)


def split_mixed(combined_output, positions, token_rows, query_length, key_length):
    key_rows = apply_rotation(
        combined_output[:, query_length : query_length + key_length].reshape(
            token_rows, KEY_VALUE_HEADS, HEAD_SIZE
        ),
        positions,
    ).astype(jnp.bfloat16)
    value_rows = combined_output[:, query_length + key_length :].astype(jnp.bfloat16)
    window_output = jnp.stack([key_rows.reshape(token_rows, key_length), value_rows])
    received = send_rim(window_output, token_rows)
    query_rows = apply_rotation(
        combined_output[:, :query_length].reshape(token_rows, QUERY_HEADS, HEAD_SIZE), positions
    ).astype(jnp.bfloat16)
    return (window_output, received, query_rows)


def gather_weight(qkv_weight):
    pairs = lax.axis_size("dp")
    columns = qkv_weight.shape[1]
    if columns % pairs:
        return lax.all_gather(qkv_weight.T, "ctx", axis=0, tiled=True)
    piece = columns // pairs
    own = lax.dynamic_slice_in_dim(qkv_weight, lax.axis_index("dp") * piece, piece, axis=1)
    return lax.all_gather(own.T, ("ctx", "dp"), axis=0, tiled=True)


def on_device(
    tokens, positions, norm_gain, qkv_weight, qkv_bias, sinks, earlier_keys, earlier_values
):
    token_rows = tokens.shape[0]
    query_group = QUERY_HEADS // KEY_VALUE_HEADS
    query_length = QUERY_HEADS * HEAD_SIZE
    key_length = KEY_VALUE_HEADS * HEAD_SIZE
    flat = tokens.astype(jnp.float32)
    scale = lax.rsqrt(jnp.mean(flat * flat, axis=-1, keepdims=True) + 1e-05)
    normed = (flat * scale * norm_gain[None, :]).astype(jnp.bfloat16)
    tables = rotation_tables(positions, 128) + (
        jnp.minimum(positions, WINDOW_TOKENS - 1).astype(jnp.int32)[:, None],
    )
    normed, tables = lax.optimization_barrier((normed, tables))
    combined_output = lax.dot_general(
        normed,
        gather_weight(qkv_weight),
        (((1,), (1,)), ((), ())),
        preferred_element_type=jnp.float32,
    )
    combined_output = combined_output + qkv_bias[None, :]
    key_rows = apply_rotation(
        combined_output[:, query_length : query_length + key_length].reshape(
            token_rows, KEY_VALUE_HEADS, HEAD_SIZE
        ),
        positions,
    ).astype(jnp.bfloat16)
    value_rows = combined_output[:, query_length + key_length :].astype(jnp.bfloat16)
    window_output = jnp.stack([key_rows.reshape(token_rows, key_length), value_rows])
    received = send_rim(window_output, token_rows)
    prior = jnp.stack([earlier_keys, earlier_values])
    border_tokens = jnp.where(lax.axis_index("ctx") == 0, prior, received)
    padded_rows = jnp.concatenate([border_tokens, window_output], axis=1).reshape(
        2, WINDOW_TOKENS + token_rows, KEY_VALUE_HEADS, HEAD_SIZE
    )
    return attend(combined_output, padded_rows[0], padded_rows[1], tables, sinks)


def solution(mesh):
    placed = (
        P(("dp", "ctx"), None),
        P(("dp", "ctx")),
        P(),
        P(None, "ctx"),
        P(),
        P(),
        P("dp", None),
        P("dp", None),
    )
    return jax.shard_map(
        on_device, mesh=mesh, in_specs=placed, out_specs=P(("dp", "ctx"), None), check_vma=False
    )
```

```python
import jax
import jax.numpy as jnp
from jax import lax
from jax.experimental import pallas as pl
from jax.experimental.pallas import tpu as pltpu
from jax.sharding import PartitionSpec as P

QUERY_HEADS = 32
KEY_VALUE_HEADS = 4
HEAD_SIZE = 64
WINDOW_TOKENS = 128


def shifted(value, axis, steps):
    count = lax.axis_size(axis)
    leading, last = (max(0, -steps), min(count, count - steps))
    return lax.ppermute(value, axis, [(source, source + steps) for source in range(leading, last)])


def apply_rotation(heads, positions):
    half = heads.shape[-1] // 2
    freq = 150000.0 ** (-(jnp.arange(half, dtype=jnp.float32) * 2.0 / heads.shape[-1]))
    angle = positions.astype(jnp.float32)[:, None] * freq[None, :]
    cosine = jnp.cos(angle)[:, None, :]
    sine = jnp.sin(angle)[:, None, :]
    first = heads[..., :half]
    second = heads[..., half:]
    return jnp.concatenate(
        [first * cosine - second * sine, second * cosine + first * sine], axis=-1
    )


def attend_head(query_rows, key_rows, value_rows, sink_row, visible):
    scores = jnp.einsum(
        "nrgd,nkd->ngrk", query_rows, key_rows, preferred_element_type=jnp.float32
    ) * HEAD_SIZE ** (-0.5)
    scores = jnp.where(visible[:, None], scores, -1e30)
    top = jnp.maximum(jnp.max(scores, axis=-1), sink_row[None, :, None])
    expo = jnp.exp(scores - top[..., None])
    total = jnp.sum(expo, axis=-1) + jnp.exp(sink_row[None, :, None] - top)
    probs = (expo / total[..., None]).astype(jnp.bfloat16)
    out = jnp.einsum("ngrk,nkd->nrgd", probs, value_rows, preferred_element_type=jnp.float32)
    return out.astype(jnp.bfloat16)


def attention_kernel(sinks_ref, limit_ref, cos_ref, sin_ref, q_ref, k_ref, v_ref, out_ref):
    group = pl.program_id(0)
    rows = q_ref.shape[0]
    query_group = q_ref.shape[1] // HEAD_SIZE
    half = HEAD_SIZE // 2
    lanes = cos_ref.shape[1]
    cosine = cos_ref[...]
    sine = sin_ref[...]
    lane = lax.broadcasted_iota(jnp.int32, (rows, lanes), 1)
    source = pltpu.roll(lane, half, 1)
    partner_lane = jnp.where(lane % HEAD_SIZE < half, lane + half, lane - half)
    take_first = source == partner_lane
    block = WINDOW_TOKENS
    query_index = lax.broadcasted_iota(jnp.int32, (block, 2 * block), 0)
    key_index = lax.broadcasted_iota(jnp.int32, (block, 2 * block), 1)
    rel = query_index - key_index + block
    visible = []
    for part in range(rows // block):
        limit = limit_ref[part * block : (part + 1) * block, :]
        visible.append((rel >= 0) & (rel <= limit))
    heads_per_chunk = lanes // HEAD_SIZE
    pick_first = group % 2 == 0
    window_keys = []
    window_values = []
    for part in range(rows // block):
        key_block = k_ref[part * block : part * block + 2 * block, :]
        value_block = v_ref[part * block : part * block + 2 * block, :]
        window_keys.append(jnp.where(pick_first, key_block[:, :HEAD_SIZE], key_block[:, HEAD_SIZE:]))
        window_values.append(jnp.where(pick_first, value_block[:, :HEAD_SIZE], value_block[:, HEAD_SIZE:]))
    for chunk in range(q_ref.shape[1] // lanes):
        x = q_ref[:, chunk * lanes : (chunk + 1) * lanes]
        first = pltpu.roll(x, half, 1)
        second = pltpu.roll(x, lanes - half, 1)
        partner = jnp.where(take_first, first, second)
        rotated = ((x * cosine + partner * sine) * HEAD_SIZE ** (-0.5)).astype(jnp.bfloat16)
        for inner in range(heads_per_chunk):
            head = chunk * heads_per_chunk + inner
            sink = sinks_ref[group * query_group + head]
            query_head = rotated[:, inner * HEAD_SIZE : (inner + 1) * HEAD_SIZE]
            for part in range(rows // block):
                queries = query_head[part * block : (part + 1) * block]
                keys = window_keys[part]
                values = window_values[part]
                scores = lax.dot_general(
                    queries, keys, (((1,), (1,)), ((), ())), preferred_element_type=jnp.float32
                )
                scores = jnp.where(visible[part], scores, -1e30)
                top = jnp.maximum(jnp.max(scores, axis=1, keepdims=True), sink)
                expo = jnp.exp(scores - top)
                total = jnp.sum(expo, axis=1, keepdims=True) + jnp.exp(sink - top)
                probs = (expo * (1.0 / total)).astype(jnp.bfloat16)
                out = jnp.dot(probs, values, preferred_element_type=jnp.float32)
                out_ref[part * block : (part + 1) * block, head * HEAD_SIZE : (head + 1) * HEAD_SIZE] = out.astype(
                    jnp.bfloat16
                )


def rotation_tables(positions, lanes):
    half = HEAD_SIZE // 2
    freq = 150000.0 ** (-(jnp.arange(half, dtype=jnp.float32) * 2.0 / HEAD_SIZE))
    angle = positions.astype(jnp.float32)[:, None] * freq[None, :]
    cosine = jnp.cos(angle)
    sine = jnp.sin(angle)
    repeats = lanes // HEAD_SIZE
    cos_table = jnp.tile(jnp.concatenate([cosine, cosine], axis=1), (1, repeats))
    sin_table = jnp.tile(jnp.concatenate([-sine, sine], axis=1), (1, repeats))
    return cos_table, sin_table


def attend(combined_output, joined_keys, joined_values, tables, sinks):
    token_rows = combined_output.shape[0]
    query_group = QUERY_HEADS // KEY_VALUE_HEADS
    group_width = query_group * HEAD_SIZE
    cos_table, sin_table, limit = tables
    lanes = cos_table.shape[1]
    key_rows = joined_keys.shape[0]
    keys = joined_keys.reshape(key_rows, -1)
    values = joined_values.reshape(key_rows, -1)
    return pl.pallas_call(
        attention_kernel,
        grid=(KEY_VALUE_HEADS,),
        in_specs=[
            pl.BlockSpec(memory_space=pltpu.SMEM),
            pl.BlockSpec((token_rows, 1), lambda g: (0, 0)),
            pl.BlockSpec((token_rows, lanes), lambda g: (0, 0)),
            pl.BlockSpec((token_rows, lanes), lambda g: (0, 0)),
            pl.BlockSpec((token_rows, group_width), lambda g: (0, g)),
            pl.BlockSpec((key_rows, 2 * HEAD_SIZE), lambda g: (0, g // 2)),
            pl.BlockSpec((key_rows, 2 * HEAD_SIZE), lambda g: (0, g // 2)),
        ],
        out_specs=pl.BlockSpec((token_rows, group_width), lambda g: (0, g)),
        out_shape=jax.ShapeDtypeStruct((token_rows, QUERY_HEADS * HEAD_SIZE), jnp.bfloat16),
    )(sinks, limit, cos_table, sin_table, combined_output, keys, values)


def send_rim(window_output, token_rows):
    return shifted(window_output[:, token_rows - WINDOW_TOKENS :], "ctx", 1)


def split_mixed(combined_output, positions, token_rows, query_length, key_length):
    key_rows = apply_rotation(
        combined_output[:, query_length : query_length + key_length].reshape(
            token_rows, KEY_VALUE_HEADS, HEAD_SIZE
        ),
        positions,
    ).astype(jnp.bfloat16)
    value_rows = combined_output[:, query_length + key_length :].astype(jnp.bfloat16)
    window_output = jnp.stack([key_rows.reshape(token_rows, key_length), value_rows])
    received = send_rim(window_output, token_rows)
    query_rows = apply_rotation(
        combined_output[:, :query_length].reshape(token_rows, QUERY_HEADS, HEAD_SIZE), positions
    ).astype(jnp.bfloat16)
    return (window_output, received, query_rows)


def gather_weight(qkv_weight):
    pairs = lax.axis_size("dp")
    columns = qkv_weight.shape[1]
    if columns % pairs:
        return lax.all_gather(qkv_weight.T, "ctx", axis=0, tiled=True)
    piece = columns // pairs
    own = lax.dynamic_slice_in_dim(qkv_weight, lax.axis_index("dp") * piece, piece, axis=1)
    return lax.all_gather(own.T, ("ctx", "dp"), axis=0, tiled=True)


def on_device(
    tokens, positions, norm_gain, qkv_weight, qkv_bias, sinks, earlier_keys, earlier_values
):
    token_rows = tokens.shape[0]
    query_group = QUERY_HEADS // KEY_VALUE_HEADS
    query_length = QUERY_HEADS * HEAD_SIZE
    key_length = KEY_VALUE_HEADS * HEAD_SIZE
    flat = tokens.astype(jnp.float32)
    scale = lax.rsqrt(jnp.mean(flat * flat, axis=-1, keepdims=True) + 1e-05)
    normed = (flat * scale * norm_gain[None, :]).astype(jnp.bfloat16)
    tables = rotation_tables(positions, 128) + (
        jnp.minimum(positions, WINDOW_TOKENS - 1).astype(jnp.int32)[:, None],
    )
    normed, tables = lax.optimization_barrier((normed, tables))
    combined_output = lax.dot_general(
        normed,
        gather_weight(qkv_weight),
        (((1,), (1,)), ((), ())),
        preferred_element_type=jnp.float32,
    )
    combined_output = combined_output + qkv_bias[None, :]
    key_rows = apply_rotation(
        combined_output[:, query_length : query_length + key_length].reshape(
            token_rows, KEY_VALUE_HEADS, HEAD_SIZE
        ),
        positions,
    ).astype(jnp.bfloat16)
    value_rows = combined_output[:, query_length + key_length :].astype(jnp.bfloat16)
    window_output = jnp.stack([key_rows.reshape(token_rows, key_length), value_rows])
    received = send_rim(window_output, token_rows)
    prior = jnp.stack([earlier_keys, earlier_values])
    border_tokens = jnp.where(lax.axis_index("ctx") == 0, prior, received)
    padded_rows = jnp.concatenate([border_tokens, window_output], axis=1).reshape(
        2, WINDOW_TOKENS + token_rows, KEY_VALUE_HEADS, HEAD_SIZE
    )
    return attend(combined_output, padded_rows[0], padded_rows[1], tables, sinks)


def solution(mesh):
    placed = (
        P(("dp", "ctx"), None),
        P(("dp", "ctx")),
        P(),
        P(None, "ctx"),
        P(),
        P(),
        P("dp", None),
        P("dp", None),
    )
    return jax.shard_map(
        on_device, mesh=mesh, in_specs=placed, out_specs=P(("dp", "ctx"), None), check_vma=False
    )
```

```python
import jax
import jax.numpy as jnp
from jax import lax
from jax.experimental import pallas as pl
from jax.experimental.pallas import tpu as pltpu
from jax.sharding import PartitionSpec as P

QUERY_HEADS = 32
KEY_VALUE_HEADS = 4
HEAD_SIZE = 64
WINDOW_TOKENS = 128


def shifted(value, axis, steps):
    count = lax.axis_size(axis)
    leading, last = (max(0, -steps), min(count, count - steps))
    return lax.ppermute(value, axis, [(source, source + steps) for source in range(leading, last)])


def apply_rotation(heads, positions):
    half = heads.shape[-1] // 2
    freq = 150000.0 ** (-(jnp.arange(half, dtype=jnp.float32) * 2.0 / heads.shape[-1]))
    angle = positions.astype(jnp.float32)[:, None] * freq[None, :]
    cosine = jnp.cos(angle)[:, None, :]
    sine = jnp.sin(angle)[:, None, :]
    first = heads[..., :half]
    second = heads[..., half:]
    return jnp.concatenate(
        [first * cosine - second * sine, second * cosine + first * sine], axis=-1
    )


def attend_head(query_rows, key_rows, value_rows, sink_row, visible):
    scores = jnp.einsum(
        "nrgd,nkd->ngrk", query_rows, key_rows, preferred_element_type=jnp.float32
    ) * HEAD_SIZE ** (-0.5)
    scores = jnp.where(visible[:, None], scores, -1e30)
    top = jnp.maximum(jnp.max(scores, axis=-1), sink_row[None, :, None])
    expo = jnp.exp(scores - top[..., None])
    total = jnp.sum(expo, axis=-1) + jnp.exp(sink_row[None, :, None] - top)
    probs = (expo / total[..., None]).astype(jnp.bfloat16)
    out = jnp.einsum("ngrk,nkd->nrgd", probs, value_rows, preferred_element_type=jnp.float32)
    return out.astype(jnp.bfloat16)


def attention_kernel(sinks_ref, limit_ref, cos_ref, sin_ref, q_ref, k_ref, v_ref, out_ref):
    group = pl.program_id(0)
    rows = q_ref.shape[0]
    query_group = q_ref.shape[1] // HEAD_SIZE
    half = HEAD_SIZE // 2
    lanes = cos_ref.shape[1]
    cosine = cos_ref[...]
    sine = sin_ref[...]
    lane = lax.broadcasted_iota(jnp.int32, (rows, lanes), 1)
    source = pltpu.roll(lane, half, 1)
    partner_lane = jnp.where(lane % HEAD_SIZE < half, lane + half, lane - half)
    take_first = source == partner_lane
    block = WINDOW_TOKENS
    query_index = lax.broadcasted_iota(jnp.int32, (block, 2 * block), 0)
    key_index = lax.broadcasted_iota(jnp.int32, (block, 2 * block), 1)
    rel = query_index - key_index + block
    visible = []
    for part in range(rows // block):
        limit = limit_ref[part * block : (part + 1) * block, :]
        visible.append((rel >= 0) & (rel <= limit))
    heads_per_chunk = lanes // HEAD_SIZE
    pick_first = group % 2 == 0
    window_keys = []
    window_values = []
    for part in range(rows // block):
        key_block = k_ref[part * block : part * block + 2 * block, :]
        value_block = v_ref[part * block : part * block + 2 * block, :]
        window_keys.append(jnp.where(pick_first, key_block[:, :HEAD_SIZE], key_block[:, HEAD_SIZE:]))
        value_lane = lax.broadcasted_iota(jnp.int32, value_block.shape, 1)
        own_lanes = value_lane // HEAD_SIZE == group % 2
        window_values.append(jnp.where(own_lanes, value_block, jnp.ones_like(value_block)))
    for chunk in range(q_ref.shape[1] // lanes):
        x = q_ref[:, chunk * lanes : (chunk + 1) * lanes]
        first = pltpu.roll(x, half, 1)
        second = pltpu.roll(x, lanes - half, 1)
        partner = jnp.where(take_first, first, second)
        rotated = ((x * cosine + partner * sine) * HEAD_SIZE ** (-0.5)).astype(jnp.bfloat16)
        for inner in range(heads_per_chunk):
            head = chunk * heads_per_chunk + inner
            sink = sinks_ref[group * query_group + head]
            query_head = rotated[:, inner * HEAD_SIZE : (inner + 1) * HEAD_SIZE]
            for part in range(rows // block):
                queries = query_head[part * block : (part + 1) * block]
                keys = window_keys[part]
                values = window_values[part]
                scores = lax.dot_general(
                    queries, keys, (((1,), (1,)), ((), ())), preferred_element_type=jnp.float32
                )
                scores = jnp.where(visible[part], scores, -1e30)
                top = jnp.maximum(jnp.max(scores, axis=1, keepdims=True), sink)
                expo = jnp.exp(scores - top).astype(jnp.bfloat16)
                weighted = jnp.dot(expo, values, preferred_element_type=jnp.float32)
                swapped = pltpu.roll(weighted, HEAD_SIZE, 1)
                numerator = jnp.where(pick_first, weighted, swapped)[:, :HEAD_SIZE]
                total = jnp.where(pick_first, swapped, weighted)[:, :HEAD_SIZE] + jnp.exp(sink - top)
                out = numerator * (1.0 / total)
                out_ref[part * block : (part + 1) * block, head * HEAD_SIZE : (head + 1) * HEAD_SIZE] = out.astype(
                    jnp.bfloat16
                )


def rotation_tables(positions, lanes):
    half = HEAD_SIZE // 2
    freq = 150000.0 ** (-(jnp.arange(half, dtype=jnp.float32) * 2.0 / HEAD_SIZE))
    angle = positions.astype(jnp.float32)[:, None] * freq[None, :]
    cosine = jnp.cos(angle)
    sine = jnp.sin(angle)
    repeats = lanes // HEAD_SIZE
    cos_table = jnp.tile(jnp.concatenate([cosine, cosine], axis=1), (1, repeats))
    sin_table = jnp.tile(jnp.concatenate([-sine, sine], axis=1), (1, repeats))
    return cos_table, sin_table


def attend(combined_output, joined_keys, joined_values, tables, sinks):
    token_rows = combined_output.shape[0]
    query_group = QUERY_HEADS // KEY_VALUE_HEADS
    group_width = query_group * HEAD_SIZE
    cos_table, sin_table, limit = tables
    lanes = cos_table.shape[1]
    key_rows = joined_keys.shape[0]
    keys = joined_keys.reshape(key_rows, -1)
    values = joined_values.reshape(key_rows, -1)
    return pl.pallas_call(
        attention_kernel,
        grid=(KEY_VALUE_HEADS,),
        in_specs=[
            pl.BlockSpec(memory_space=pltpu.SMEM),
            pl.BlockSpec((token_rows, 1), lambda g: (0, 0)),
            pl.BlockSpec((token_rows, lanes), lambda g: (0, 0)),
            pl.BlockSpec((token_rows, lanes), lambda g: (0, 0)),
            pl.BlockSpec((token_rows, group_width), lambda g: (0, g)),
            pl.BlockSpec((key_rows, 2 * HEAD_SIZE), lambda g: (0, g // 2)),
            pl.BlockSpec((key_rows, 2 * HEAD_SIZE), lambda g: (0, g // 2)),
        ],
        out_specs=pl.BlockSpec((token_rows, group_width), lambda g: (0, g)),
        out_shape=jax.ShapeDtypeStruct((token_rows, QUERY_HEADS * HEAD_SIZE), jnp.bfloat16),
    )(sinks, limit, cos_table, sin_table, combined_output, keys, values)


def send_rim(window_output, token_rows):
    return shifted(window_output[:, token_rows - WINDOW_TOKENS :], "ctx", 1)


def split_mixed(combined_output, positions, token_rows, query_length, key_length):
    key_rows = apply_rotation(
        combined_output[:, query_length : query_length + key_length].reshape(
            token_rows, KEY_VALUE_HEADS, HEAD_SIZE
        ),
        positions,
    ).astype(jnp.bfloat16)
    value_rows = combined_output[:, query_length + key_length :].astype(jnp.bfloat16)
    window_output = jnp.stack([key_rows.reshape(token_rows, key_length), value_rows])
    received = send_rim(window_output, token_rows)
    query_rows = apply_rotation(
        combined_output[:, :query_length].reshape(token_rows, QUERY_HEADS, HEAD_SIZE), positions
    ).astype(jnp.bfloat16)
    return (window_output, received, query_rows)


def gather_weight(qkv_weight):
    pairs = lax.axis_size("dp")
    columns = qkv_weight.shape[1]
    if columns % pairs:
        return lax.all_gather(qkv_weight.T, "ctx", axis=0, tiled=True)
    piece = columns // pairs
    own = lax.dynamic_slice_in_dim(qkv_weight, lax.axis_index("dp") * piece, piece, axis=1)
    return lax.all_gather(own.T, ("ctx", "dp"), axis=0, tiled=True)


def on_device(
    tokens, positions, norm_gain, qkv_weight, qkv_bias, sinks, earlier_keys, earlier_values
):
    token_rows = tokens.shape[0]
    query_group = QUERY_HEADS // KEY_VALUE_HEADS
    query_length = QUERY_HEADS * HEAD_SIZE
    key_length = KEY_VALUE_HEADS * HEAD_SIZE
    flat = tokens.astype(jnp.float32)
    scale = lax.rsqrt(jnp.mean(flat * flat, axis=-1, keepdims=True) + 1e-05)
    normed = (flat * scale * norm_gain[None, :]).astype(jnp.bfloat16)
    tables = rotation_tables(positions, 128) + (
        jnp.minimum(positions, WINDOW_TOKENS - 1).astype(jnp.int32)[:, None],
    )
    normed, tables = lax.optimization_barrier((normed, tables))
    combined_output = lax.dot_general(
        normed,
        gather_weight(qkv_weight),
        (((1,), (1,)), ((), ())),
        preferred_element_type=jnp.float32,
    )
    combined_output = combined_output + qkv_bias[None, :]
    key_rows = apply_rotation(
        combined_output[:, query_length : query_length + key_length].reshape(
            token_rows, KEY_VALUE_HEADS, HEAD_SIZE
        ),
        positions,
    ).astype(jnp.bfloat16)
    value_rows = combined_output[:, query_length + key_length :].astype(jnp.bfloat16)
    window_output = jnp.stack([key_rows.reshape(token_rows, key_length), value_rows])
    received = send_rim(window_output, token_rows)
    prior = jnp.stack([earlier_keys, earlier_values])
    border_tokens = jnp.where(lax.axis_index("ctx") == 0, prior, received)
    padded_rows = jnp.concatenate([border_tokens, window_output], axis=1).reshape(
        2, WINDOW_TOKENS + token_rows, KEY_VALUE_HEADS, HEAD_SIZE
    )
    return attend(combined_output, padded_rows[0], padded_rows[1], tables, sinks)


def solution(mesh):
    placed = (
        P(("dp", "ctx"), None),
        P(("dp", "ctx")),
        P(),
        P(None, "ctx"),
        P(),
        P(),
        P("dp", None),
        P("dp", None),
    )
    return jax.shard_map(
        on_device, mesh=mesh, in_specs=placed, out_specs=P(("dp", "ctx"), None), check_vma=False
    )
```

```python
import jax
import jax.numpy as jnp
from jax import lax
from jax.experimental import pallas as pl
from jax.experimental.pallas import tpu as pltpu
from jax.sharding import PartitionSpec as P

QUERY_HEADS = 32
KEY_VALUE_HEADS = 4
HEAD_SIZE = 64
WINDOW_TOKENS = 128


def shifted(value, axis, steps):
    count = lax.axis_size(axis)
    leading, last = (max(0, -steps), min(count, count - steps))
    return lax.ppermute(value, axis, [(source, source + steps) for source in range(leading, last)])


def apply_rotation(heads, positions):
    half = heads.shape[-1] // 2
    freq = 150000.0 ** (-(jnp.arange(half, dtype=jnp.float32) * 2.0 / heads.shape[-1]))
    angle = positions.astype(jnp.float32)[:, None] * freq[None, :]
    cosine = jnp.cos(angle)[:, None, :]
    sine = jnp.sin(angle)[:, None, :]
    first = heads[..., :half]
    second = heads[..., half:]
    return jnp.concatenate(
        [first * cosine - second * sine, second * cosine + first * sine], axis=-1
    )


def attend_head(query_rows, key_rows, value_rows, sink_row, visible):
    scores = jnp.einsum(
        "nrgd,nkd->ngrk", query_rows, key_rows, preferred_element_type=jnp.float32
    ) * HEAD_SIZE ** (-0.5)
    scores = jnp.where(visible[:, None], scores, -1e30)
    top = jnp.maximum(jnp.max(scores, axis=-1), sink_row[None, :, None])
    expo = jnp.exp(scores - top[..., None])
    total = jnp.sum(expo, axis=-1) + jnp.exp(sink_row[None, :, None] - top)
    probs = (expo / total[..., None]).astype(jnp.bfloat16)
    out = jnp.einsum("ngrk,nkd->nrgd", probs, value_rows, preferred_element_type=jnp.float32)
    return out.astype(jnp.bfloat16)


def attention_kernel(
    sinks_ref, limit_ref, cos_ref, sin_ref, normed_ref, weight_ref, bias_ref, k_ref, v_ref, out_ref
):
    group = pl.program_id(0)
    queries_all = lax.dot_general(
        normed_ref[...], weight_ref[...], (((1,), (1,)), ((), ())), preferred_element_type=jnp.float32
    )
    queries_all = queries_all + bias_ref[...]
    rows = queries_all.shape[0]
    query_group = queries_all.shape[1] // HEAD_SIZE
    half = HEAD_SIZE // 2
    lanes = cos_ref.shape[1]
    cosine = cos_ref[...]
    sine = sin_ref[...]
    lane = lax.broadcasted_iota(jnp.int32, (rows, lanes), 1)
    source = pltpu.roll(lane, half, 1)
    partner_lane = jnp.where(lane % HEAD_SIZE < half, lane + half, lane - half)
    take_first = source == partner_lane
    block = WINDOW_TOKENS
    query_index = lax.broadcasted_iota(jnp.int32, (block, 2 * block), 0)
    key_index = lax.broadcasted_iota(jnp.int32, (block, 2 * block), 1)
    rel = query_index - key_index + block
    visible = []
    for part in range(rows // block):
        limit = limit_ref[part * block : (part + 1) * block, :]
        visible.append((rel >= 0) & (rel <= limit))
    heads_per_chunk = lanes // HEAD_SIZE
    pick_first = group % 2 == 0
    window_keys = []
    window_values = []
    for part in range(rows // block):
        key_block = k_ref[part * block : part * block + 2 * block, :]
        value_block = v_ref[part * block : part * block + 2 * block, :]
        window_keys.append(jnp.where(pick_first, key_block[:, :HEAD_SIZE], key_block[:, HEAD_SIZE:]))
        window_values.append(jnp.where(pick_first, value_block[:, :HEAD_SIZE], value_block[:, HEAD_SIZE:]))
    for chunk in range(queries_all.shape[1] // lanes):
        x = queries_all[:, chunk * lanes : (chunk + 1) * lanes]
        first = pltpu.roll(x, half, 1)
        second = pltpu.roll(x, lanes - half, 1)
        partner = jnp.where(take_first, first, second)
        rotated = ((x * cosine + partner * sine) * HEAD_SIZE ** (-0.5)).astype(jnp.bfloat16)
        for inner in range(heads_per_chunk):
            head = chunk * heads_per_chunk + inner
            sink = sinks_ref[group * query_group + head]
            query_head = rotated[:, inner * HEAD_SIZE : (inner + 1) * HEAD_SIZE]
            for part in range(rows // block):
                queries = query_head[part * block : (part + 1) * block]
                keys = window_keys[part]
                values = window_values[part]
                scores = lax.dot_general(
                    queries, keys, (((1,), (1,)), ((), ())), preferred_element_type=jnp.float32
                )
                scores = jnp.where(visible[part], scores, -1e30)
                top = jnp.maximum(jnp.max(scores, axis=1, keepdims=True), sink)
                expo = jnp.exp(scores - top)
                total = jnp.sum(expo, axis=1, keepdims=True) + jnp.exp(sink - top)
                probs = (expo * (1.0 / total)).astype(jnp.bfloat16)
                out = jnp.dot(probs, values, preferred_element_type=jnp.float32)
                out_ref[part * block : (part + 1) * block, head * HEAD_SIZE : (head + 1) * HEAD_SIZE] = out.astype(
                    jnp.bfloat16
                )


def rotation_tables(positions, lanes):
    half = HEAD_SIZE // 2
    freq = 150000.0 ** (-(jnp.arange(half, dtype=jnp.float32) * 2.0 / HEAD_SIZE))
    angle = positions.astype(jnp.float32)[:, None] * freq[None, :]
    cosine = jnp.cos(angle)
    sine = jnp.sin(angle)
    repeats = lanes // HEAD_SIZE
    cos_table = jnp.tile(jnp.concatenate([cosine, cosine], axis=1), (1, repeats))
    sin_table = jnp.tile(jnp.concatenate([-sine, sine], axis=1), (1, repeats))
    return cos_table, sin_table


def attend(normed, weight_rows, query_bias, joined_keys, joined_values, tables, sinks):
    token_rows = normed.shape[0]
    model_width = normed.shape[1]
    query_group = QUERY_HEADS // KEY_VALUE_HEADS
    group_width = query_group * HEAD_SIZE
    cos_table, sin_table, limit = tables
    lanes = cos_table.shape[1]
    key_rows = joined_keys.shape[0]
    keys = joined_keys.reshape(key_rows, -1)
    values = joined_values.reshape(key_rows, -1)
    return pl.pallas_call(
        attention_kernel,
        grid=(KEY_VALUE_HEADS,),
        in_specs=[
            pl.BlockSpec(memory_space=pltpu.SMEM),
            pl.BlockSpec((token_rows, 1), lambda g: (0, 0)),
            pl.BlockSpec((token_rows, lanes), lambda g: (0, 0)),
            pl.BlockSpec((token_rows, lanes), lambda g: (0, 0)),
            pl.BlockSpec((token_rows, model_width), lambda g: (0, 0)),
            pl.BlockSpec((group_width, model_width), lambda g: (g, 0)),
            pl.BlockSpec((1, group_width), lambda g: (0, g)),
            pl.BlockSpec((key_rows, 2 * HEAD_SIZE), lambda g: (0, g // 2)),
            pl.BlockSpec((key_rows, 2 * HEAD_SIZE), lambda g: (0, g // 2)),
        ],
        out_specs=pl.BlockSpec((token_rows, group_width), lambda g: (0, g)),
        out_shape=jax.ShapeDtypeStruct((token_rows, QUERY_HEADS * HEAD_SIZE), jnp.bfloat16),
    )(sinks, limit, cos_table, sin_table, normed, weight_rows, query_bias, keys, values)


def send_rim(window_output, token_rows):
    return shifted(window_output[:, token_rows - WINDOW_TOKENS :], "ctx", 1)


def split_mixed(combined_output, positions, token_rows, query_length, key_length):
    key_rows = apply_rotation(
        combined_output[:, query_length : query_length + key_length].reshape(
            token_rows, KEY_VALUE_HEADS, HEAD_SIZE
        ),
        positions,
    ).astype(jnp.bfloat16)
    value_rows = combined_output[:, query_length + key_length :].astype(jnp.bfloat16)
    window_output = jnp.stack([key_rows.reshape(token_rows, key_length), value_rows])
    received = send_rim(window_output, token_rows)
    query_rows = apply_rotation(
        combined_output[:, :query_length].reshape(token_rows, QUERY_HEADS, HEAD_SIZE), positions
    ).astype(jnp.bfloat16)
    return (window_output, received, query_rows)


def gather_weight(qkv_weight):
    pairs = lax.axis_size("dp")
    columns = qkv_weight.shape[1]
    if columns % pairs:
        return lax.all_gather(qkv_weight.T, "ctx", axis=0, tiled=True)
    piece = columns // pairs
    own = lax.dynamic_slice_in_dim(qkv_weight, lax.axis_index("dp") * piece, piece, axis=1)
    return lax.all_gather(own.T, ("ctx", "dp"), axis=0, tiled=True)


def on_device(
    tokens, positions, norm_gain, qkv_weight, qkv_bias, sinks, earlier_keys, earlier_values
):
    token_rows = tokens.shape[0]
    query_group = QUERY_HEADS // KEY_VALUE_HEADS
    query_length = QUERY_HEADS * HEAD_SIZE
    key_length = KEY_VALUE_HEADS * HEAD_SIZE
    flat = tokens.astype(jnp.float32)
    scale = lax.rsqrt(jnp.mean(flat * flat, axis=-1, keepdims=True) + 1e-05)
    normed = (flat * scale * norm_gain[None, :]).astype(jnp.bfloat16)
    tables = rotation_tables(positions, 128) + (
        jnp.minimum(positions, WINDOW_TOKENS - 1).astype(jnp.int32)[:, None],
    )
    normed, tables = lax.optimization_barrier((normed, tables))
    weight_rows = gather_weight(qkv_weight)
    key_value_output = lax.dot_general(
        normed,
        weight_rows[query_length:],
        (((1,), (1,)), ((), ())),
        preferred_element_type=jnp.float32,
    )
    key_value_output = key_value_output + qkv_bias[None, query_length:]
    key_rows = apply_rotation(
        key_value_output[:, :key_length].reshape(token_rows, KEY_VALUE_HEADS, HEAD_SIZE),
        positions,
    ).astype(jnp.bfloat16)
    value_rows = key_value_output[:, key_length:].astype(jnp.bfloat16)
    window_output = jnp.stack([key_rows.reshape(token_rows, key_length), value_rows])
    received = send_rim(window_output, token_rows)
    prior = jnp.stack([earlier_keys, earlier_values])
    border_tokens = jnp.where(lax.axis_index("ctx") == 0, prior, received)
    padded_rows = jnp.concatenate([border_tokens, window_output], axis=1).reshape(
        2, WINDOW_TOKENS + token_rows, KEY_VALUE_HEADS, HEAD_SIZE
    )
    return attend(
        normed,
        weight_rows,
        qkv_bias[None, :query_length],
        padded_rows[0],
        padded_rows[1],
        tables,
        sinks,
    )


def solution(mesh):
    placed = (
        P(("dp", "ctx"), None),
        P(("dp", "ctx")),
        P(),
        P(None, "ctx"),
        P(),
        P(),
        P("dp", None),
        P("dp", None),
    )
    return jax.shard_map(
        on_device, mesh=mesh, in_specs=placed, out_specs=P(("dp", "ctx"), None), check_vma=False
    )
```

```python
import jax
import jax.numpy as jnp
from jax import lax
from jax.experimental import pallas as pl
from jax.experimental.pallas import tpu as pltpu
from jax.sharding import PartitionSpec as P

QUERY_HEADS = 32
KEY_VALUE_HEADS = 4
HEAD_SIZE = 64
WINDOW_TOKENS = 128


def shifted(value, axis, steps):
    count = lax.axis_size(axis)
    leading, last = (max(0, -steps), min(count, count - steps))
    return lax.ppermute(value, axis, [(source, source + steps) for source in range(leading, last)])


def apply_rotation(heads, positions):
    half = heads.shape[-1] // 2
    freq = 150000.0 ** (-(jnp.arange(half, dtype=jnp.float32) * 2.0 / heads.shape[-1]))
    angle = positions.astype(jnp.float32)[:, None] * freq[None, :]
    cosine = jnp.cos(angle)[:, None, :]
    sine = jnp.sin(angle)[:, None, :]
    first = heads[..., :half]
    second = heads[..., half:]
    return jnp.concatenate(
        [first * cosine - second * sine, second * cosine + first * sine], axis=-1
    )


def attend_head(query_rows, key_rows, value_rows, sink_row, visible):
    scores = jnp.einsum(
        "nrgd,nkd->ngrk", query_rows, key_rows, preferred_element_type=jnp.float32
    ) * HEAD_SIZE ** (-0.5)
    scores = jnp.where(visible[:, None], scores, -1e30)
    top = jnp.maximum(jnp.max(scores, axis=-1), sink_row[None, :, None])
    expo = jnp.exp(scores - top[..., None])
    total = jnp.sum(expo, axis=-1) + jnp.exp(sink_row[None, :, None] - top)
    probs = (expo / total[..., None]).astype(jnp.bfloat16)
    out = jnp.einsum("ngrk,nkd->nrgd", probs, value_rows, preferred_element_type=jnp.float32)
    return out.astype(jnp.bfloat16)


def attention_kernel(
    sinks_ref, limit_ref, cos_ref, sin_ref, normed_ref, weight_ref, bias_ref, k_ref, v_ref, out_ref
):
    group = pl.program_id(0)
    queries_all = lax.dot_general(
        normed_ref[...], weight_ref[...], (((1,), (1,)), ((), ())), preferred_element_type=jnp.float32
    )
    queries_all = queries_all + bias_ref[...]
    rows = queries_all.shape[0]
    query_group = queries_all.shape[1] // HEAD_SIZE
    half = HEAD_SIZE // 2
    lanes = cos_ref.shape[1]
    cosine = cos_ref[...]
    sine = sin_ref[...]
    lane = lax.broadcasted_iota(jnp.int32, (rows, lanes), 1)
    source = pltpu.roll(lane, half, 1)
    partner_lane = jnp.where(lane % HEAD_SIZE < half, lane + half, lane - half)
    take_first = source == partner_lane
    block = WINDOW_TOKENS
    query_index = lax.broadcasted_iota(jnp.int32, (block, 2 * block), 0)
    key_index = lax.broadcasted_iota(jnp.int32, (block, 2 * block), 1)
    rel = query_index - key_index + block
    visible = []
    for part in range(rows // block):
        limit = limit_ref[part * block : (part + 1) * block, :]
        visible.append((rel >= 0) & (rel <= limit))
    heads_per_chunk = lanes // HEAD_SIZE
    pick_first = group % 2 == 0
    window_keys = []
    window_values = []
    for part in range(rows // block):
        key_block = k_ref[part * block : part * block + 2 * block, :]
        value_block = v_ref[part * block : part * block + 2 * block, :]
        window_keys.append(jnp.where(pick_first, key_block[:, :HEAD_SIZE], key_block[:, HEAD_SIZE:]))
        value_lane = lax.broadcasted_iota(jnp.int32, value_block.shape, 1)
        own_lanes = value_lane // HEAD_SIZE == group % 2
        window_values.append(jnp.where(own_lanes, value_block, jnp.ones_like(value_block)))
    for chunk in range(queries_all.shape[1] // lanes):
        x = queries_all[:, chunk * lanes : (chunk + 1) * lanes]
        first = pltpu.roll(x, half, 1)
        second = pltpu.roll(x, lanes - half, 1)
        partner = jnp.where(take_first, first, second)
        rotated = ((x * cosine + partner * sine) * HEAD_SIZE ** (-0.5)).astype(jnp.bfloat16)
        for inner in range(heads_per_chunk):
            head = chunk * heads_per_chunk + inner
            sink = sinks_ref[group * query_group + head]
            query_head = rotated[:, inner * HEAD_SIZE : (inner + 1) * HEAD_SIZE]
            for part in range(rows // block):
                queries = query_head[part * block : (part + 1) * block]
                keys = window_keys[part]
                values = window_values[part]
                scores = lax.dot_general(
                    queries, keys, (((1,), (1,)), ((), ())), preferred_element_type=jnp.float32
                )
                scores = jnp.where(visible[part], scores, -1e30)
                top = jnp.maximum(jnp.max(scores, axis=1, keepdims=True), sink)
                expo = jnp.exp(scores - top).astype(jnp.bfloat16)
                weighted = jnp.dot(expo, values, preferred_element_type=jnp.float32)
                swapped = pltpu.roll(weighted, HEAD_SIZE, 1)
                numerator = jnp.where(pick_first, weighted, swapped)[:, :HEAD_SIZE]
                total = jnp.where(pick_first, swapped, weighted)[:, :HEAD_SIZE] + jnp.exp(sink - top)
                out = numerator * (1.0 / total)
                out_ref[part * block : (part + 1) * block, head * HEAD_SIZE : (head + 1) * HEAD_SIZE] = out.astype(
                    jnp.bfloat16
                )


def rotation_tables(positions, lanes):
    half = HEAD_SIZE // 2
    freq = 150000.0 ** (-(jnp.arange(half, dtype=jnp.float32) * 2.0 / HEAD_SIZE))
    angle = positions.astype(jnp.float32)[:, None] * freq[None, :]
    cosine = jnp.cos(angle)
    sine = jnp.sin(angle)
    repeats = lanes // HEAD_SIZE
    cos_table = jnp.tile(jnp.concatenate([cosine, cosine], axis=1), (1, repeats))
    sin_table = jnp.tile(jnp.concatenate([-sine, sine], axis=1), (1, repeats))
    return cos_table, sin_table


def attend(normed, weight_rows, query_bias, joined_keys, joined_values, tables, sinks):
    token_rows = normed.shape[0]
    model_width = normed.shape[1]
    query_group = QUERY_HEADS // KEY_VALUE_HEADS
    group_width = query_group * HEAD_SIZE
    cos_table, sin_table, limit = tables
    lanes = cos_table.shape[1]
    key_rows = joined_keys.shape[0]
    keys = joined_keys.reshape(key_rows, -1)
    values = joined_values.reshape(key_rows, -1)
    return pl.pallas_call(
        attention_kernel,
        grid=(KEY_VALUE_HEADS,),
        in_specs=[
            pl.BlockSpec(memory_space=pltpu.SMEM),
            pl.BlockSpec((token_rows, 1), lambda g: (0, 0)),
            pl.BlockSpec((token_rows, lanes), lambda g: (0, 0)),
            pl.BlockSpec((token_rows, lanes), lambda g: (0, 0)),
            pl.BlockSpec((token_rows, model_width), lambda g: (0, 0)),
            pl.BlockSpec((group_width, model_width), lambda g: (g, 0)),
            pl.BlockSpec((1, group_width), lambda g: (0, g)),
            pl.BlockSpec((key_rows, 2 * HEAD_SIZE), lambda g: (0, g // 2)),
            pl.BlockSpec((key_rows, 2 * HEAD_SIZE), lambda g: (0, g // 2)),
        ],
        out_specs=pl.BlockSpec((token_rows, group_width), lambda g: (0, g)),
        out_shape=jax.ShapeDtypeStruct((token_rows, QUERY_HEADS * HEAD_SIZE), jnp.bfloat16),
    )(sinks, limit, cos_table, sin_table, normed, weight_rows, query_bias, keys, values)


def send_rim(window_output, token_rows):
    return shifted(window_output[:, token_rows - WINDOW_TOKENS :], "ctx", 1)


def split_mixed(combined_output, positions, token_rows, query_length, key_length):
    key_rows = apply_rotation(
        combined_output[:, query_length : query_length + key_length].reshape(
            token_rows, KEY_VALUE_HEADS, HEAD_SIZE
        ),
        positions,
    ).astype(jnp.bfloat16)
    value_rows = combined_output[:, query_length + key_length :].astype(jnp.bfloat16)
    window_output = jnp.stack([key_rows.reshape(token_rows, key_length), value_rows])
    received = send_rim(window_output, token_rows)
    query_rows = apply_rotation(
        combined_output[:, :query_length].reshape(token_rows, QUERY_HEADS, HEAD_SIZE), positions
    ).astype(jnp.bfloat16)
    return (window_output, received, query_rows)


def gather_weight(qkv_weight):
    pairs = lax.axis_size("dp")
    columns = qkv_weight.shape[1]
    if columns % pairs:
        return lax.all_gather(qkv_weight.T, "ctx", axis=0, tiled=True)
    piece = columns // pairs
    own = lax.dynamic_slice_in_dim(qkv_weight, lax.axis_index("dp") * piece, piece, axis=1)
    return lax.all_gather(own.T, ("ctx", "dp"), axis=0, tiled=True)


def on_device(
    tokens, positions, norm_gain, qkv_weight, qkv_bias, sinks, earlier_keys, earlier_values
):
    token_rows = tokens.shape[0]
    query_group = QUERY_HEADS // KEY_VALUE_HEADS
    query_length = QUERY_HEADS * HEAD_SIZE
    key_length = KEY_VALUE_HEADS * HEAD_SIZE
    flat = tokens.astype(jnp.float32)
    scale = lax.rsqrt(jnp.mean(flat * flat, axis=-1, keepdims=True) + 1e-05)
    normed = (flat * scale * norm_gain[None, :]).astype(jnp.bfloat16)
    tables = rotation_tables(positions, 128) + (
        jnp.minimum(positions, WINDOW_TOKENS - 1).astype(jnp.int32)[:, None],
    )
    normed, tables = lax.optimization_barrier((normed, tables))
    weight_rows = gather_weight(qkv_weight)
    key_value_output = lax.dot_general(
        normed,
        weight_rows[query_length:],
        (((1,), (1,)), ((), ())),
        preferred_element_type=jnp.float32,
    )
    key_value_output = key_value_output + qkv_bias[None, query_length:]
    key_rows = apply_rotation(
        key_value_output[:, :key_length].reshape(token_rows, KEY_VALUE_HEADS, HEAD_SIZE),
        positions,
    ).astype(jnp.bfloat16)
    value_rows = key_value_output[:, key_length:].astype(jnp.bfloat16)
    window_output = jnp.stack([key_rows.reshape(token_rows, key_length), value_rows])
    received = send_rim(window_output, token_rows)
    prior = jnp.stack([earlier_keys, earlier_values])
    border_tokens = jnp.where(lax.axis_index("ctx") == 0, prior, received)
    padded_rows = jnp.concatenate([border_tokens, window_output], axis=1).reshape(
        2, WINDOW_TOKENS + token_rows, KEY_VALUE_HEADS, HEAD_SIZE
    )
    return attend(
        normed,
        weight_rows,
        qkv_bias[None, :query_length],
        padded_rows[0],
        padded_rows[1],
        tables,
        sinks,
    )


def solution(mesh):
    placed = (
        P(("dp", "ctx"), None),
        P(("dp", "ctx")),
        P(),
        P(None, "ctx"),
        P(),
        P(),
        P("dp", None),
        P("dp", None),
    )
    return jax.shard_map(
        on_device, mesh=mesh, in_specs=placed, out_specs=P(("dp", "ctx"), None), check_vma=False
    )
```

```python
import jax
import jax.numpy as jnp
from jax import lax
from jax.experimental import pallas as pl
from jax.experimental.pallas import tpu as pltpu
from jax.sharding import PartitionSpec as P

QUERY_HEADS = 32
KEY_VALUE_HEADS = 4
HEAD_SIZE = 64
WINDOW_TOKENS = 128


def shifted(value, axis, steps):
    count = lax.axis_size(axis)
    leading, last = (max(0, -steps), min(count, count - steps))
    return lax.ppermute(value, axis, [(source, source + steps) for source in range(leading, last)])


def apply_rotation(heads, positions):
    half = heads.shape[-1] // 2
    freq = 150000.0 ** (-(jnp.arange(half, dtype=jnp.float32) * 2.0 / heads.shape[-1]))
    angle = positions.astype(jnp.float32)[:, None] * freq[None, :]
    cosine = jnp.cos(angle)[:, None, :]
    sine = jnp.sin(angle)[:, None, :]
    first = heads[..., :half]
    second = heads[..., half:]
    return jnp.concatenate(
        [first * cosine - second * sine, second * cosine + first * sine], axis=-1
    )


def attend_head(query_rows, key_rows, value_rows, sink_row, visible):
    scores = jnp.einsum(
        "nrgd,nkd->ngrk", query_rows, key_rows, preferred_element_type=jnp.float32
    ) * HEAD_SIZE ** (-0.5)
    scores = jnp.where(visible[:, None], scores, -1e30)
    top = jnp.maximum(jnp.max(scores, axis=-1), sink_row[None, :, None])
    expo = jnp.exp(scores - top[..., None])
    total = jnp.sum(expo, axis=-1) + jnp.exp(sink_row[None, :, None] - top)
    probs = (expo / total[..., None]).astype(jnp.bfloat16)
    out = jnp.einsum("ngrk,nkd->nrgd", probs, value_rows, preferred_element_type=jnp.float32)
    return out.astype(jnp.bfloat16)


def attention_kernel(
    sinks_ref, limit_ref, cos_ref, sin_ref, normed_ref, weight_ref, bias_ref, k_ref, v_ref, out_ref
):
    group = pl.program_id(0)
    queries_all = lax.dot_general(
        normed_ref[...], weight_ref[...], (((1,), (1,)), ((), ())), preferred_element_type=jnp.float32
    )
    queries_all = queries_all + bias_ref[...]
    rows = queries_all.shape[0]
    query_group = queries_all.shape[1] // HEAD_SIZE
    half = HEAD_SIZE // 2
    lanes = cos_ref.shape[1]
    cosine = cos_ref[...]
    sine = sin_ref[...]
    lane = lax.broadcasted_iota(jnp.int32, (rows, lanes), 1)
    source = pltpu.roll(lane, half, 1)
    partner_lane = jnp.where(lane % HEAD_SIZE < half, lane + half, lane - half)
    take_first = source == partner_lane
    block = WINDOW_TOKENS
    query_index = lax.broadcasted_iota(jnp.int32, (block, 2 * block), 0)
    key_index = lax.broadcasted_iota(jnp.int32, (block, 2 * block), 1)
    rel = query_index - key_index + block
    visible = []
    for part in range(rows // block):
        limit = limit_ref[part * block : (part + 1) * block, :]
        visible.append((rel >= 0) & (rel <= limit))
    heads_per_chunk = lanes // HEAD_SIZE
    pick_first = group % 2 == 0
    window_keys = []
    window_values = []
    for part in range(rows // block):
        key_block = k_ref[part * block : part * block + 2 * block, :]
        value_block = v_ref[part * block : part * block + 2 * block, :]
        window_keys.append(jnp.where(pick_first, key_block[:, :HEAD_SIZE], key_block[:, HEAD_SIZE:]))
        window_values.append(jnp.where(pick_first, value_block[:, :HEAD_SIZE], value_block[:, HEAD_SIZE:]))
    for chunk in range(queries_all.shape[1] // lanes):
        x = queries_all[:, chunk * lanes : (chunk + 1) * lanes]
        first = pltpu.roll(x, half, 1)
        second = pltpu.roll(x, lanes - half, 1)
        partner = jnp.where(take_first, first, second)
        rotated = ((x * cosine + partner * sine) * HEAD_SIZE ** (-0.5)).astype(jnp.bfloat16)
        for inner in range(heads_per_chunk):
            head = chunk * heads_per_chunk + inner
            sink = sinks_ref[group * query_group + head]
            query_head = rotated[:, inner * HEAD_SIZE : (inner + 1) * HEAD_SIZE]
            for part in range(rows // block):
                queries = query_head[part * block : (part + 1) * block]
                keys = window_keys[part]
                values = window_values[part]
                scores = lax.dot_general(
                    queries, keys, (((1,), (1,)), ((), ())), preferred_element_type=jnp.float32
                )
                scores = jnp.where(visible[part], scores, -1e30)
                top = jnp.maximum(jnp.max(scores, axis=1, keepdims=True), sink)
                expo = jnp.exp(scores - top)
                total = jnp.sum(expo, axis=1, keepdims=True) + jnp.exp(sink - top)
                probs = (expo * (1.0 / total)).astype(jnp.bfloat16)
                out = jnp.dot(probs, values, preferred_element_type=jnp.float32)
                out_ref[part * block : (part + 1) * block, head * HEAD_SIZE : (head + 1) * HEAD_SIZE] = out.astype(
                    jnp.bfloat16
                )


def key_value_kernel(cos_ref, sin_ref, normed_ref, weight_ref, bias_ref, out_ref):
    column = pl.program_id(0)
    x = lax.dot_general(
        normed_ref[...], weight_ref[...], (((1,), (1,)), ((), ())), preferred_element_type=jnp.float32
    )
    x = x + bias_ref[...]
    rows, lanes = x.shape
    half = HEAD_SIZE // 2
    lane = lax.broadcasted_iota(jnp.int32, (rows, lanes), 1)
    source = pltpu.roll(lane, half, 1)
    partner_lane = jnp.where(lane % HEAD_SIZE < half, lane + half, lane - half)
    first = pltpu.roll(x, half, 1)
    second = pltpu.roll(x, lanes - half, 1)
    partner = jnp.where(source == partner_lane, first, second)
    rotated = x * cos_ref[...] + partner * sin_ref[...]
    is_key = column < (KEY_VALUE_HEADS * HEAD_SIZE) // lanes
    out_ref[...] = jnp.where(is_key, rotated, x).astype(jnp.bfloat16)


def project_keys_values(normed, weight_rows, qkv_bias, tables, query_length):
    token_rows, model_width = normed.shape
    cos_table, sin_table, _ = tables
    lanes = cos_table.shape[1]
    width = weight_rows.shape[0] - query_length
    first_block = query_length // lanes
    bias = qkv_bias[None, :]
    return pl.pallas_call(
        key_value_kernel,
        grid=(width // lanes,),
        in_specs=[
            pl.BlockSpec((token_rows, lanes), lambda j: (0, 0)),
            pl.BlockSpec((token_rows, lanes), lambda j: (0, 0)),
            pl.BlockSpec((token_rows, model_width), lambda j: (0, 0)),
            pl.BlockSpec((lanes, model_width), lambda j: (first_block + j, 0)),
            pl.BlockSpec((1, lanes), lambda j: (0, first_block + j)),
        ],
        out_specs=pl.BlockSpec((token_rows, lanes), lambda j: (0, j)),
        out_shape=jax.ShapeDtypeStruct((token_rows, width), jnp.bfloat16),
    )(cos_table, sin_table, normed, weight_rows, bias)


def rotation_tables(positions, lanes):
    half = HEAD_SIZE // 2
    freq = 150000.0 ** (-(jnp.arange(half, dtype=jnp.float32) * 2.0 / HEAD_SIZE))
    angle = positions.astype(jnp.float32)[:, None] * freq[None, :]
    cosine = jnp.cos(angle)
    sine = jnp.sin(angle)
    repeats = lanes // HEAD_SIZE
    cos_table = jnp.tile(jnp.concatenate([cosine, cosine], axis=1), (1, repeats))
    sin_table = jnp.tile(jnp.concatenate([-sine, sine], axis=1), (1, repeats))
    return cos_table, sin_table


def attend(normed, weight_rows, query_bias, joined_keys, joined_values, tables, sinks):
    token_rows = normed.shape[0]
    model_width = normed.shape[1]
    query_group = QUERY_HEADS // KEY_VALUE_HEADS
    group_width = query_group * HEAD_SIZE
    cos_table, sin_table, limit = tables
    lanes = cos_table.shape[1]
    key_rows = joined_keys.shape[0]
    keys = joined_keys.reshape(key_rows, -1)
    values = joined_values.reshape(key_rows, -1)
    return pl.pallas_call(
        attention_kernel,
        grid=(KEY_VALUE_HEADS,),
        in_specs=[
            pl.BlockSpec(memory_space=pltpu.SMEM),
            pl.BlockSpec((token_rows, 1), lambda g: (0, 0)),
            pl.BlockSpec((token_rows, lanes), lambda g: (0, 0)),
            pl.BlockSpec((token_rows, lanes), lambda g: (0, 0)),
            pl.BlockSpec((token_rows, model_width), lambda g: (0, 0)),
            pl.BlockSpec((group_width, model_width), lambda g: (g, 0)),
            pl.BlockSpec((1, group_width), lambda g: (0, g)),
            pl.BlockSpec((key_rows, 2 * HEAD_SIZE), lambda g: (0, g // 2)),
            pl.BlockSpec((key_rows, 2 * HEAD_SIZE), lambda g: (0, g // 2)),
        ],
        out_specs=pl.BlockSpec((token_rows, group_width), lambda g: (0, g)),
        out_shape=jax.ShapeDtypeStruct((token_rows, QUERY_HEADS * HEAD_SIZE), jnp.bfloat16),
    )(sinks, limit, cos_table, sin_table, normed, weight_rows, query_bias, keys, values)


def send_rim(window_output, token_rows):
    return shifted(window_output[:, token_rows - WINDOW_TOKENS :], "ctx", 1)


def split_mixed(combined_output, positions, token_rows, query_length, key_length):
    key_rows = apply_rotation(
        combined_output[:, query_length : query_length + key_length].reshape(
            token_rows, KEY_VALUE_HEADS, HEAD_SIZE
        ),
        positions,
    ).astype(jnp.bfloat16)
    value_rows = combined_output[:, query_length + key_length :].astype(jnp.bfloat16)
    window_output = jnp.stack([key_rows.reshape(token_rows, key_length), value_rows])
    received = send_rim(window_output, token_rows)
    query_rows = apply_rotation(
        combined_output[:, :query_length].reshape(token_rows, QUERY_HEADS, HEAD_SIZE), positions
    ).astype(jnp.bfloat16)
    return (window_output, received, query_rows)


def gather_weight(qkv_weight):
    pairs = lax.axis_size("dp")
    columns = qkv_weight.shape[1]
    if columns % pairs:
        return lax.all_gather(qkv_weight.T, "ctx", axis=0, tiled=True)
    piece = columns // pairs
    own = lax.dynamic_slice_in_dim(qkv_weight, lax.axis_index("dp") * piece, piece, axis=1)
    return lax.all_gather(own.T, ("ctx", "dp"), axis=0, tiled=True)


def on_device(
    tokens, positions, norm_gain, qkv_weight, qkv_bias, sinks, earlier_keys, earlier_values
):
    token_rows = tokens.shape[0]
    query_group = QUERY_HEADS // KEY_VALUE_HEADS
    query_length = QUERY_HEADS * HEAD_SIZE
    key_length = KEY_VALUE_HEADS * HEAD_SIZE
    flat = tokens.astype(jnp.float32)
    scale = lax.rsqrt(jnp.mean(flat * flat, axis=-1, keepdims=True) + 1e-05)
    normed = (flat * scale * norm_gain[None, :]).astype(jnp.bfloat16)
    tables = rotation_tables(positions, 128) + (
        jnp.minimum(positions, WINDOW_TOKENS - 1).astype(jnp.int32)[:, None],
    )
    normed, tables = lax.optimization_barrier((normed, tables))
    weight_rows = gather_weight(qkv_weight)
    key_value_output = project_keys_values(normed, weight_rows, qkv_bias, tables, query_length)
    window_output = jnp.moveaxis(key_value_output.reshape(token_rows, 2, key_length), 1, 0)
    received = send_rim(window_output, token_rows)
    prior = jnp.stack([earlier_keys, earlier_values])
    border_tokens = jnp.where(lax.axis_index("ctx") == 0, prior, received)
    padded_rows = jnp.concatenate([border_tokens, window_output], axis=1).reshape(
        2, WINDOW_TOKENS + token_rows, KEY_VALUE_HEADS, HEAD_SIZE
    )
    return attend(
        normed,
        weight_rows,
        qkv_bias[None, :query_length],
        padded_rows[0],
        padded_rows[1],
        tables,
        sinks,
    )


def solution(mesh):
    placed = (
        P(("dp", "ctx"), None),
        P(("dp", "ctx")),
        P(),
        P(None, "ctx"),
        P(),
        P(),
        P("dp", None),
        P("dp", None),
    )
    return jax.shard_map(
        on_device, mesh=mesh, in_specs=placed, out_specs=P(("dp", "ctx"), None), check_vma=False
    )
```

```python
import jax
import jax.numpy as jnp
from jax import lax
from jax.experimental import pallas as pl
from jax.experimental.pallas import tpu as pltpu
from jax.sharding import PartitionSpec as P

QUERY_HEADS = 32
KEY_VALUE_HEADS = 4
HEAD_SIZE = 64
WINDOW_TOKENS = 128


def shifted(value, axis, steps):
    count = lax.axis_size(axis)
    leading, last = (max(0, -steps), min(count, count - steps))
    return lax.ppermute(value, axis, [(source, source + steps) for source in range(leading, last)])


def apply_rotation(heads, positions):
    half = heads.shape[-1] // 2
    freq = 150000.0 ** (-(jnp.arange(half, dtype=jnp.float32) * 2.0 / heads.shape[-1]))
    angle = positions.astype(jnp.float32)[:, None] * freq[None, :]
    cosine = jnp.cos(angle)[:, None, :]
    sine = jnp.sin(angle)[:, None, :]
    first = heads[..., :half]
    second = heads[..., half:]
    return jnp.concatenate(
        [first * cosine - second * sine, second * cosine + first * sine], axis=-1
    )


def attend_head(query_rows, key_rows, value_rows, sink_row, visible):
    scores = jnp.einsum(
        "nrgd,nkd->ngrk", query_rows, key_rows, preferred_element_type=jnp.float32
    ) * HEAD_SIZE ** (-0.5)
    scores = jnp.where(visible[:, None], scores, -1e30)
    top = jnp.maximum(jnp.max(scores, axis=-1), sink_row[None, :, None])
    expo = jnp.exp(scores - top[..., None])
    total = jnp.sum(expo, axis=-1) + jnp.exp(sink_row[None, :, None] - top)
    probs = (expo / total[..., None]).astype(jnp.bfloat16)
    out = jnp.einsum("ngrk,nkd->nrgd", probs, value_rows, preferred_element_type=jnp.float32)
    return out.astype(jnp.bfloat16)


def attention_kernel(
    sinks_ref, limit_ref, cos_ref, sin_ref, normed_ref, weight_ref, bias_ref, k_ref, v_ref, out_ref
):
    group = pl.program_id(0)
    queries_all = lax.dot_general(
        normed_ref[...], weight_ref[...], (((1,), (1,)), ((), ())), preferred_element_type=jnp.float32
    )
    queries_all = queries_all + bias_ref[...]
    rows = queries_all.shape[0]
    query_group = queries_all.shape[1] // HEAD_SIZE
    half = HEAD_SIZE // 2
    lanes = cos_ref.shape[1]
    cosine = cos_ref[...]
    sine = sin_ref[...]
    lane = lax.broadcasted_iota(jnp.int32, (rows, lanes), 1)
    source = pltpu.roll(lane, half, 1)
    partner_lane = jnp.where(lane % HEAD_SIZE < half, lane + half, lane - half)
    take_first = source == partner_lane
    block = WINDOW_TOKENS
    query_index = lax.broadcasted_iota(jnp.int32, (block, 2 * block), 0)
    key_index = lax.broadcasted_iota(jnp.int32, (block, 2 * block), 1)
    rel = query_index - key_index + block
    visible = []
    for part in range(rows // block):
        limit = limit_ref[part * block : (part + 1) * block, :]
        visible.append((rel >= 0) & (rel <= limit))
    heads_per_chunk = lanes // HEAD_SIZE
    pick_first = group % 2 == 0
    window_keys = []
    window_values = []
    for part in range(rows // block):
        key_block = k_ref[part * block : part * block + 2 * block, :]
        value_block = v_ref[part * block : part * block + 2 * block, :]
        window_keys.append(jnp.where(pick_first, key_block[:, :HEAD_SIZE], key_block[:, HEAD_SIZE:]))
        window_values.append(jnp.where(pick_first, value_block[:, :HEAD_SIZE], value_block[:, HEAD_SIZE:]))
    for chunk in range(queries_all.shape[1] // lanes):
        x = queries_all[:, chunk * lanes : (chunk + 1) * lanes]
        first = pltpu.roll(x, half, 1)
        second = pltpu.roll(x, lanes - half, 1)
        partner = jnp.where(take_first, first, second)
        rotated = ((x * cosine + partner * sine) * HEAD_SIZE ** (-0.5)).astype(jnp.bfloat16)
        for inner in range(heads_per_chunk):
            head = chunk * heads_per_chunk + inner
            sink = sinks_ref[group * query_group + head]
            query_head = rotated[:, inner * HEAD_SIZE : (inner + 1) * HEAD_SIZE]
            for part in range(rows // block):
                queries = query_head[part * block : (part + 1) * block]
                keys = window_keys[part]
                values = window_values[part]
                scores = lax.dot_general(
                    queries, keys, (((1,), (1,)), ((), ())), preferred_element_type=jnp.float32
                )
                scores = jnp.where(visible[part], scores, -1e30)
                top = jnp.maximum(jnp.max(scores, axis=1, keepdims=True), sink)
                expo = jnp.exp(scores - top)
                total = jnp.sum(expo, axis=1, keepdims=True) + jnp.exp(sink - top)
                probs = (expo * (1.0 / total)).astype(jnp.bfloat16)
                out = jnp.dot(probs, values, preferred_element_type=jnp.float32)
                out_ref[part * block : (part + 1) * block, head * HEAD_SIZE : (head + 1) * HEAD_SIZE] = out.astype(
                    jnp.bfloat16
                )


def rotation_tables(positions, lanes):
    half = HEAD_SIZE // 2
    freq = 150000.0 ** (-(jnp.arange(half, dtype=jnp.float32) * 2.0 / HEAD_SIZE))
    angle = positions.astype(jnp.float32)[:, None] * freq[None, :]
    cosine = jnp.cos(angle)
    sine = jnp.sin(angle)
    repeats = lanes // HEAD_SIZE
    cos_table = jnp.tile(jnp.concatenate([cosine, cosine], axis=1), (1, repeats))
    sin_table = jnp.tile(jnp.concatenate([-sine, sine], axis=1), (1, repeats))
    return cos_table, sin_table


def attend(normed, weight_rows, query_bias, joined_keys, joined_values, tables, sinks):
    token_rows = normed.shape[0]
    model_width = normed.shape[1]
    query_group = QUERY_HEADS // KEY_VALUE_HEADS
    group_width = query_group * HEAD_SIZE
    cos_table, sin_table, limit = tables
    lanes = cos_table.shape[1]
    key_rows = joined_keys.shape[0]
    keys = joined_keys
    values = joined_values
    return pl.pallas_call(
        attention_kernel,
        grid=(KEY_VALUE_HEADS,),
        in_specs=[
            pl.BlockSpec(memory_space=pltpu.SMEM),
            pl.BlockSpec((token_rows, 1), lambda g: (0, 0)),
            pl.BlockSpec((token_rows, lanes), lambda g: (0, 0)),
            pl.BlockSpec((token_rows, lanes), lambda g: (0, 0)),
            pl.BlockSpec((token_rows, model_width), lambda g: (0, 0)),
            pl.BlockSpec((group_width, model_width), lambda g: (g, 0)),
            pl.BlockSpec((1, group_width), lambda g: (0, g)),
            pl.BlockSpec((key_rows, 2 * HEAD_SIZE), lambda g: (0, g // 2)),
            pl.BlockSpec((key_rows, 2 * HEAD_SIZE), lambda g: (0, g // 2)),
        ],
        out_specs=pl.BlockSpec((token_rows, group_width), lambda g: (0, g)),
        out_shape=jax.ShapeDtypeStruct((token_rows, QUERY_HEADS * HEAD_SIZE), jnp.bfloat16),
    )(sinks, limit, cos_table, sin_table, normed, weight_rows, query_bias, keys, values)


def send_rim(window_output, token_rows):
    return shifted(window_output[:, token_rows - WINDOW_TOKENS :], "ctx", 1)


def split_mixed(combined_output, positions, token_rows, query_length, key_length):
    key_rows = apply_rotation(
        combined_output[:, query_length : query_length + key_length].reshape(
            token_rows, KEY_VALUE_HEADS, HEAD_SIZE
        ),
        positions,
    ).astype(jnp.bfloat16)
    value_rows = combined_output[:, query_length + key_length :].astype(jnp.bfloat16)
    window_output = jnp.stack([key_rows.reshape(token_rows, key_length), value_rows])
    received = send_rim(window_output, token_rows)
    query_rows = apply_rotation(
        combined_output[:, :query_length].reshape(token_rows, QUERY_HEADS, HEAD_SIZE), positions
    ).astype(jnp.bfloat16)
    return (window_output, received, query_rows)


def gather_weight(qkv_weight):
    pairs = lax.axis_size("dp")
    columns = qkv_weight.shape[1]
    if columns % pairs:
        return lax.all_gather(qkv_weight.T, "ctx", axis=0, tiled=True)
    piece = columns // pairs
    own = lax.dynamic_slice_in_dim(qkv_weight, lax.axis_index("dp") * piece, piece, axis=1)
    return lax.all_gather(own.T, ("ctx", "dp"), axis=0, tiled=True)


def on_device(
    tokens, positions, norm_gain, qkv_weight, qkv_bias, sinks, earlier_keys, earlier_values
):
    token_rows = tokens.shape[0]
    query_group = QUERY_HEADS // KEY_VALUE_HEADS
    query_length = QUERY_HEADS * HEAD_SIZE
    key_length = KEY_VALUE_HEADS * HEAD_SIZE
    flat = tokens.astype(jnp.float32)
    scale = lax.rsqrt(jnp.mean(flat * flat, axis=-1, keepdims=True) + 1e-05)
    normed = (flat * scale * norm_gain[None, :]).astype(jnp.bfloat16)
    tables = rotation_tables(positions, 128) + (
        jnp.minimum(positions, WINDOW_TOKENS - 1).astype(jnp.int32)[:, None],
    )
    normed, tables = lax.optimization_barrier((normed, tables))
    weight_rows = gather_weight(qkv_weight)
    key_value_output = lax.dot_general(
        normed,
        weight_rows[query_length:],
        (((1,), (1,)), ((), ())),
        preferred_element_type=jnp.float32,
    )
    key_value_output = key_value_output + qkv_bias[None, query_length:]
    key_rows = apply_rotation(
        key_value_output[:, :key_length].reshape(token_rows, KEY_VALUE_HEADS, HEAD_SIZE),
        positions,
    ).astype(jnp.bfloat16)
    value_rows = key_value_output[:, key_length:].astype(jnp.bfloat16)
    window_output = jnp.stack([key_rows.reshape(token_rows, key_length), value_rows])
    received = send_rim(window_output, token_rows)
    prior = jnp.stack([earlier_keys, earlier_values])
    border_tokens = jnp.where(lax.axis_index("ctx") == 0, prior, received)
    padded_rows = jnp.concatenate([border_tokens, window_output], axis=1)
    query_bias = qkv_bias[None, :query_length]
    outputs = []
    for start in range(token_rows - WINDOW_TOKENS, -1, -WINDOW_TOKENS):
        rows = slice(start, start + WINDOW_TOKENS)
        if start >= WINDOW_TOKENS:
            window = window_output[:, start - WINDOW_TOKENS : start + WINDOW_TOKENS]
        else:
            window = padded_rows[:, start : start + 2 * WINDOW_TOKENS]
        outputs.insert(
            0,
            attend(
                normed[rows],
                weight_rows,
                query_bias,
                window[0],
                window[1],
                tuple(table[rows] for table in tables),
                sinks,
            ),
        )
    return jnp.concatenate(outputs, axis=0)


def solution(mesh):
    placed = (
        P(("dp", "ctx"), None),
        P(("dp", "ctx")),
        P(),
        P(None, "ctx"),
        P(),
        P(),
        P("dp", None),
        P("dp", None),
    )
    return jax.shard_map(
        on_device, mesh=mesh, in_specs=placed, out_specs=P(("dp", "ctx"), None), check_vma=False
    )
```

```python
import jax
import jax.numpy as jnp
from jax import lax
from jax.experimental import pallas as pl
from jax.experimental.pallas import tpu as pltpu
from jax.sharding import PartitionSpec as P

QUERY_HEADS = 32
KEY_VALUE_HEADS = 4
HEAD_SIZE = 64
WINDOW_TOKENS = 128


def shifted(value, axis, steps):
    count = lax.axis_size(axis)
    leading, last = (max(0, -steps), min(count, count - steps))
    return lax.ppermute(value, axis, [(source, source + steps) for source in range(leading, last)])


def apply_rotation(heads, positions):
    half = heads.shape[-1] // 2
    freq = 150000.0 ** (-(jnp.arange(half, dtype=jnp.float32) * 2.0 / heads.shape[-1]))
    angle = positions.astype(jnp.float32)[:, None] * freq[None, :]
    cosine = jnp.cos(angle)[:, None, :]
    sine = jnp.sin(angle)[:, None, :]
    first = heads[..., :half]
    second = heads[..., half:]
    return jnp.concatenate(
        [first * cosine - second * sine, second * cosine + first * sine], axis=-1
    )


def attend_head(query_rows, key_rows, value_rows, sink_row, visible):
    scores = jnp.einsum(
        "nrgd,nkd->ngrk", query_rows, key_rows, preferred_element_type=jnp.float32
    ) * HEAD_SIZE ** (-0.5)
    scores = jnp.where(visible[:, None], scores, -1e30)
    top = jnp.maximum(jnp.max(scores, axis=-1), sink_row[None, :, None])
    expo = jnp.exp(scores - top[..., None])
    total = jnp.sum(expo, axis=-1) + jnp.exp(sink_row[None, :, None] - top)
    probs = (expo / total[..., None]).astype(jnp.bfloat16)
    out = jnp.einsum("ngrk,nkd->nrgd", probs, value_rows, preferred_element_type=jnp.float32)
    return out.astype(jnp.bfloat16)


def attention_kernel(
    sinks_ref, limit_ref, cos_ref, sin_ref, normed_ref, weight_ref, bias_ref, k_ref, v_ref, out_ref
):
    group = pl.program_id(0)
    queries_all = lax.dot_general(
        normed_ref[...], weight_ref[...], (((1,), (1,)), ((), ())), preferred_element_type=jnp.float32
    )
    queries_all = queries_all + bias_ref[...]
    rows = queries_all.shape[0]
    query_group = queries_all.shape[1] // HEAD_SIZE
    half = HEAD_SIZE // 2
    lanes = cos_ref.shape[1]
    cosine = cos_ref[...]
    sine = sin_ref[...]
    lane = lax.broadcasted_iota(jnp.int32, (rows, lanes), 1)
    source = pltpu.roll(lane, half, 1)
    partner_lane = jnp.where(lane % HEAD_SIZE < half, lane + half, lane - half)
    take_first = source == partner_lane
    block = WINDOW_TOKENS
    query_index = lax.broadcasted_iota(jnp.int32, (block, 2 * block), 0)
    key_index = lax.broadcasted_iota(jnp.int32, (block, 2 * block), 1)
    rel = query_index - key_index + block
    visible = []
    for part in range(rows // block):
        limit = limit_ref[part * block : (part + 1) * block, :]
        visible.append((rel >= 0) & (rel <= limit))
    heads_per_chunk = lanes // HEAD_SIZE
    pick_first = group % 2 == 0
    window_keys = []
    window_values = []
    for part in range(rows // block):
        key_block = k_ref[part * block : part * block + 2 * block, :]
        value_block = v_ref[part * block : part * block + 2 * block, :]
        window_keys.append(jnp.where(pick_first, key_block[:, :HEAD_SIZE], key_block[:, HEAD_SIZE:]))
        window_values.append(jnp.where(pick_first, value_block[:, :HEAD_SIZE], value_block[:, HEAD_SIZE:]))
    for chunk in range(queries_all.shape[1] // lanes):
        x = queries_all[:, chunk * lanes : (chunk + 1) * lanes]
        first = pltpu.roll(x, half, 1)
        second = pltpu.roll(x, lanes - half, 1)
        partner = jnp.where(take_first, first, second)
        rotated = ((x * cosine + partner * sine) * HEAD_SIZE ** (-0.5)).astype(jnp.bfloat16)
        for inner in range(heads_per_chunk):
            head = chunk * heads_per_chunk + inner
            sink = sinks_ref[group * query_group + head]
            query_head = rotated[:, inner * HEAD_SIZE : (inner + 1) * HEAD_SIZE]
            for part in range(rows // block):
                queries = query_head[part * block : (part + 1) * block]
                keys = window_keys[part]
                values = window_values[part]
                scores = lax.dot_general(
                    queries, keys, (((1,), (1,)), ((), ())), preferred_element_type=jnp.float32
                )
                scores = jnp.where(visible[part], scores, -1e30)
                top = jnp.maximum(jnp.max(scores, axis=1, keepdims=True), sink)
                expo = jnp.exp(scores - top)
                total = jnp.sum(expo, axis=1, keepdims=True) + jnp.exp(sink - top)
                probs = (expo * (1.0 / total)).astype(jnp.bfloat16)
                out = jnp.dot(probs, values, preferred_element_type=jnp.float32)
                out_ref[part * block : (part + 1) * block, head * HEAD_SIZE : (head + 1) * HEAD_SIZE] = out.astype(
                    jnp.bfloat16
                )


def rotation_tables(positions, lanes):
    half = HEAD_SIZE // 2
    freq = 150000.0 ** (-(jnp.arange(half, dtype=jnp.float32) * 2.0 / HEAD_SIZE))
    angle = positions.astype(jnp.float32)[:, None] * freq[None, :]
    cosine = jnp.cos(angle)
    sine = jnp.sin(angle)
    repeats = lanes // HEAD_SIZE
    cos_table = jnp.tile(jnp.concatenate([cosine, cosine], axis=1), (1, repeats))
    sin_table = jnp.tile(jnp.concatenate([-sine, sine], axis=1), (1, repeats))
    return cos_table, sin_table


def attend(normed, weight_rows, query_bias, joined_rows, tables, sinks):
    token_rows = normed.shape[0]
    model_width = normed.shape[1]
    query_group = QUERY_HEADS // KEY_VALUE_HEADS
    group_width = query_group * HEAD_SIZE
    cos_table, sin_table, limit = tables
    lanes = cos_table.shape[1]
    key_rows = joined_rows.shape[1]
    return pl.pallas_call(
        attention_kernel,
        grid=(KEY_VALUE_HEADS,),
        in_specs=[
            pl.BlockSpec(memory_space=pltpu.SMEM),
            pl.BlockSpec((token_rows, 1), lambda g: (0, 0)),
            pl.BlockSpec((token_rows, lanes), lambda g: (0, 0)),
            pl.BlockSpec((token_rows, lanes), lambda g: (0, 0)),
            pl.BlockSpec((token_rows, model_width), lambda g: (0, 0)),
            pl.BlockSpec((group_width, model_width), lambda g: (g, 0)),
            pl.BlockSpec((1, group_width), lambda g: (0, g)),
            pl.BlockSpec((None, key_rows, 2 * HEAD_SIZE), lambda g: (0, 0, g // 2)),
            pl.BlockSpec((None, key_rows, 2 * HEAD_SIZE), lambda g: (1, 0, g // 2)),
        ],
        out_specs=pl.BlockSpec((token_rows, group_width), lambda g: (0, g)),
        out_shape=jax.ShapeDtypeStruct((token_rows, QUERY_HEADS * HEAD_SIZE), jnp.bfloat16),
    )(sinks, limit, cos_table, sin_table, normed, weight_rows, query_bias, joined_rows, joined_rows)


def send_rim(window_output, token_rows):
    return shifted(window_output[:, token_rows - WINDOW_TOKENS :], "ctx", 1)


def split_mixed(combined_output, positions, token_rows, query_length, key_length):
    key_rows = apply_rotation(
        combined_output[:, query_length : query_length + key_length].reshape(
            token_rows, KEY_VALUE_HEADS, HEAD_SIZE
        ),
        positions,
    ).astype(jnp.bfloat16)
    value_rows = combined_output[:, query_length + key_length :].astype(jnp.bfloat16)
    window_output = jnp.stack([key_rows.reshape(token_rows, key_length), value_rows])
    received = send_rim(window_output, token_rows)
    query_rows = apply_rotation(
        combined_output[:, :query_length].reshape(token_rows, QUERY_HEADS, HEAD_SIZE), positions
    ).astype(jnp.bfloat16)
    return (window_output, received, query_rows)


def gather_weight(qkv_weight):
    pairs = lax.axis_size("dp")
    columns = qkv_weight.shape[1]
    if columns % pairs:
        return lax.all_gather(qkv_weight.T, "ctx", axis=0, tiled=True)
    piece = columns // pairs
    own = lax.dynamic_slice_in_dim(qkv_weight, lax.axis_index("dp") * piece, piece, axis=1)
    return lax.all_gather(own.T, ("ctx", "dp"), axis=0, tiled=True)


def on_device(
    tokens, positions, norm_gain, qkv_weight, qkv_bias, sinks, earlier_keys, earlier_values
):
    token_rows = tokens.shape[0]
    query_group = QUERY_HEADS // KEY_VALUE_HEADS
    query_length = QUERY_HEADS * HEAD_SIZE
    key_length = KEY_VALUE_HEADS * HEAD_SIZE
    flat = tokens.astype(jnp.float32)
    scale = lax.rsqrt(jnp.mean(flat * flat, axis=-1, keepdims=True) + 1e-05)
    normed = (flat * scale * norm_gain[None, :]).astype(jnp.bfloat16)
    tables = rotation_tables(positions, 128) + (
        jnp.minimum(positions, WINDOW_TOKENS - 1).astype(jnp.int32)[:, None],
    )
    normed, tables = lax.optimization_barrier((normed, tables))
    weight_rows = gather_weight(qkv_weight)
    key_value_output = lax.dot_general(
        normed,
        weight_rows[query_length:],
        (((1,), (1,)), ((), ())),
        preferred_element_type=jnp.float32,
    )
    key_value_output = key_value_output + qkv_bias[None, query_length:]
    key_rows = apply_rotation(
        key_value_output[:, :key_length].reshape(token_rows, KEY_VALUE_HEADS, HEAD_SIZE),
        positions,
    ).astype(jnp.bfloat16)
    value_rows = key_value_output[:, key_length:].astype(jnp.bfloat16)
    window_output = jnp.stack([key_rows.reshape(token_rows, key_length), value_rows])
    received = send_rim(window_output, token_rows)
    prior = jnp.stack([earlier_keys, earlier_values])
    border_tokens = jnp.where(lax.axis_index("ctx") == 0, prior, received)
    padded_rows = jnp.concatenate([border_tokens, window_output], axis=1)
    return attend(normed, weight_rows, qkv_bias[None, :query_length], padded_rows, tables, sinks)


def solution(mesh):
    placed = (
        P(("dp", "ctx"), None),
        P(("dp", "ctx")),
        P(),
        P(None, "ctx"),
        P(),
        P(),
        P("dp", None),
        P("dp", None),
    )
    return jax.shard_map(
        on_device, mesh=mesh, in_specs=placed, out_specs=P(("dp", "ctx"), None), check_vma=False
    )
```

```python
import jax
import jax.numpy as jnp
from jax import lax
from jax.experimental import pallas as pl
from jax.experimental.pallas import tpu as pltpu
from jax.sharding import PartitionSpec as P

QUERY_HEADS = 32
KEY_VALUE_HEADS = 4
HEAD_SIZE = 64
WINDOW_TOKENS = 128


def shifted(value, axis, steps):
    count = lax.axis_size(axis)
    leading, last = (max(0, -steps), min(count, count - steps))
    return lax.ppermute(value, axis, [(source, source + steps) for source in range(leading, last)])


def apply_rotation(heads, positions):
    half = heads.shape[-1] // 2
    freq = 150000.0 ** (-(jnp.arange(half, dtype=jnp.float32) * 2.0 / heads.shape[-1]))
    angle = positions.astype(jnp.float32)[:, None] * freq[None, :]
    cosine = jnp.cos(angle)[:, None, :]
    sine = jnp.sin(angle)[:, None, :]
    first = heads[..., :half]
    second = heads[..., half:]
    return jnp.concatenate(
        [first * cosine - second * sine, second * cosine + first * sine], axis=-1
    )


def attend_head(query_rows, key_rows, value_rows, sink_row, visible):
    scores = jnp.einsum(
        "nrgd,nkd->ngrk", query_rows, key_rows, preferred_element_type=jnp.float32
    ) * HEAD_SIZE ** (-0.5)
    scores = jnp.where(visible[:, None], scores, -1e30)
    top = jnp.maximum(jnp.max(scores, axis=-1), sink_row[None, :, None])
    expo = jnp.exp(scores - top[..., None])
    total = jnp.sum(expo, axis=-1) + jnp.exp(sink_row[None, :, None] - top)
    probs = (expo / total[..., None]).astype(jnp.bfloat16)
    out = jnp.einsum("ngrk,nkd->nrgd", probs, value_rows, preferred_element_type=jnp.float32)
    return out.astype(jnp.bfloat16)


def attention_kernel(
    sinks_ref, limit_ref, cos_ref, sin_ref, normed_ref, weight_ref, bias_ref, k_ref, v_ref, out_ref
):
    group = pl.program_id(0)
    queries_all = lax.dot_general(
        normed_ref[...], weight_ref[...], (((1,), (1,)), ((), ())), preferred_element_type=jnp.float32
    )
    queries_all = queries_all + bias_ref[...]
    rows = queries_all.shape[0]
    query_group = queries_all.shape[1] // HEAD_SIZE
    half = HEAD_SIZE // 2
    lanes = cos_ref.shape[1]
    cosine = cos_ref[...]
    sine = sin_ref[...]
    lane = lax.broadcasted_iota(jnp.int32, (rows, lanes), 1)
    source = pltpu.roll(lane, half, 1)
    partner_lane = jnp.where(lane % HEAD_SIZE < half, lane + half, lane - half)
    take_first = source == partner_lane
    block = WINDOW_TOKENS
    query_index = lax.broadcasted_iota(jnp.int32, (block, 2 * block), 0)
    key_index = lax.broadcasted_iota(jnp.int32, (block, 2 * block), 1)
    rel = query_index - key_index + block
    visible = []
    for part in range(rows // block):
        limit = limit_ref[part * block : (part + 1) * block, :]
        visible.append((rel >= 0) & (rel <= limit))
    heads_per_chunk = lanes // HEAD_SIZE
    pick_first = group % 2 == 0
    window_keys = []
    window_values = []
    for part in range(rows // block):
        key_block = k_ref[part * block : part * block + 2 * block, :]
        value_block = v_ref[part * block : part * block + 2 * block, :]
        window_keys.append(jnp.where(pick_first, key_block[:, :HEAD_SIZE], key_block[:, HEAD_SIZE:]))
        window_values.append(jnp.where(pick_first, value_block[:, :HEAD_SIZE], value_block[:, HEAD_SIZE:]))
    for chunk in range(queries_all.shape[1] // lanes):
        x = queries_all[:, chunk * lanes : (chunk + 1) * lanes]
        first = pltpu.roll(x, half, 1)
        second = pltpu.roll(x, lanes - half, 1)
        partner = jnp.where(take_first, first, second)
        rotated = ((x * cosine + partner * sine) * HEAD_SIZE ** (-0.5)).astype(jnp.bfloat16)
        for inner in range(heads_per_chunk):
            head = chunk * heads_per_chunk + inner
            sink = sinks_ref[group * query_group + head]
            query_head = rotated[:, inner * HEAD_SIZE : (inner + 1) * HEAD_SIZE]
            for part in range(rows // block):
                queries = query_head[part * block : (part + 1) * block]
                keys = window_keys[part]
                values = window_values[part]
                scores = lax.dot_general(
                    queries, keys, (((1,), (1,)), ((), ())), preferred_element_type=jnp.float32
                )
                scores = jnp.where(visible[part], scores, -1e30)
                top = jnp.maximum(jnp.max(scores, axis=1, keepdims=True), sink)
                expo = jnp.exp(scores - top)
                total = jnp.sum(expo, axis=1, keepdims=True) + jnp.exp(sink - top)
                probs = (expo * (1.0 / total)).astype(jnp.bfloat16)
                out = jnp.dot(probs, values, preferred_element_type=jnp.float32)
                out_ref[part * block : (part + 1) * block, head * HEAD_SIZE : (head + 1) * HEAD_SIZE] = out.astype(
                    jnp.bfloat16
                )


def rotation_tables(positions, lanes):
    half = HEAD_SIZE // 2
    freq = 150000.0 ** (-(jnp.arange(half, dtype=jnp.float32) * 2.0 / HEAD_SIZE))
    repeats = lanes // half
    lane_freq = jnp.tile(freq, repeats)
    sign = jnp.tile(jnp.concatenate([-jnp.ones(half), jnp.ones(half)]).astype(jnp.float32), lanes // HEAD_SIZE)
    angle = positions.astype(jnp.float32)[:, None] * lane_freq[None, :]
    return jnp.cos(angle), sign[None, :] * jnp.sin(angle)


def attend(normed, weight_rows, query_bias, joined_rows, tables, sinks):
    token_rows = normed.shape[0]
    model_width = normed.shape[1]
    query_group = QUERY_HEADS // KEY_VALUE_HEADS
    group_width = query_group * HEAD_SIZE
    cos_table, sin_table, limit = tables
    lanes = cos_table.shape[1]
    key_rows = joined_rows.shape[1]
    return pl.pallas_call(
        attention_kernel,
        grid=(KEY_VALUE_HEADS,),
        in_specs=[
            pl.BlockSpec(memory_space=pltpu.SMEM),
            pl.BlockSpec((token_rows, 1), lambda g: (0, 0)),
            pl.BlockSpec((token_rows, lanes), lambda g: (0, 0)),
            pl.BlockSpec((token_rows, lanes), lambda g: (0, 0)),
            pl.BlockSpec((token_rows, model_width), lambda g: (0, 0)),
            pl.BlockSpec((group_width, model_width), lambda g: (g, 0)),
            pl.BlockSpec((1, group_width), lambda g: (0, g)),
            pl.BlockSpec((None, key_rows, 2 * HEAD_SIZE), lambda g: (0, 0, g // 2)),
            pl.BlockSpec((None, key_rows, 2 * HEAD_SIZE), lambda g: (1, 0, g // 2)),
        ],
        out_specs=pl.BlockSpec((token_rows, group_width), lambda g: (0, g)),
        out_shape=jax.ShapeDtypeStruct((token_rows, QUERY_HEADS * HEAD_SIZE), jnp.bfloat16),
    )(sinks, limit, cos_table, sin_table, normed, weight_rows, query_bias, joined_rows, joined_rows)


def send_rim(window_output, token_rows):
    return shifted(window_output[:, token_rows - WINDOW_TOKENS :], "ctx", 1)


def split_mixed(combined_output, positions, token_rows, query_length, key_length):
    key_rows = apply_rotation(
        combined_output[:, query_length : query_length + key_length].reshape(
            token_rows, KEY_VALUE_HEADS, HEAD_SIZE
        ),
        positions,
    ).astype(jnp.bfloat16)
    value_rows = combined_output[:, query_length + key_length :].astype(jnp.bfloat16)
    window_output = jnp.stack([key_rows.reshape(token_rows, key_length), value_rows])
    received = send_rim(window_output, token_rows)
    query_rows = apply_rotation(
        combined_output[:, :query_length].reshape(token_rows, QUERY_HEADS, HEAD_SIZE), positions
    ).astype(jnp.bfloat16)
    return (window_output, received, query_rows)


def gather_weight(qkv_weight):
    pairs = lax.axis_size("dp")
    columns = qkv_weight.shape[1]
    if columns % pairs:
        return lax.all_gather(qkv_weight.T, "ctx", axis=0, tiled=True)
    piece = columns // pairs
    own = lax.dynamic_slice_in_dim(qkv_weight, lax.axis_index("dp") * piece, piece, axis=1)
    return lax.all_gather(own.T, ("ctx", "dp"), axis=0, tiled=True)


def on_device(
    tokens, positions, norm_gain, qkv_weight, qkv_bias, sinks, earlier_keys, earlier_values
):
    token_rows = tokens.shape[0]
    query_group = QUERY_HEADS // KEY_VALUE_HEADS
    query_length = QUERY_HEADS * HEAD_SIZE
    key_length = KEY_VALUE_HEADS * HEAD_SIZE
    flat = tokens.astype(jnp.float32)
    scale = lax.rsqrt(jnp.mean(flat * flat, axis=-1, keepdims=True) + 1e-05)
    normed = (flat * scale * norm_gain[None, :]).astype(jnp.bfloat16)
    tables = rotation_tables(positions, 128) + (
        jnp.minimum(positions, WINDOW_TOKENS - 1).astype(jnp.int32)[:, None],
    )
    normed, tables = lax.optimization_barrier((normed, tables))
    weight_rows = gather_weight(qkv_weight)
    key_value_output = lax.dot_general(
        normed,
        weight_rows[query_length:],
        (((1,), (1,)), ((), ())),
        preferred_element_type=jnp.float32,
    )
    key_value_output = key_value_output + qkv_bias[None, query_length:]
    key_rows = apply_rotation(
        key_value_output[:, :key_length].reshape(token_rows, KEY_VALUE_HEADS, HEAD_SIZE),
        positions,
    ).astype(jnp.bfloat16)
    value_rows = key_value_output[:, key_length:].astype(jnp.bfloat16)
    window_output = jnp.stack([key_rows.reshape(token_rows, key_length), value_rows])
    received = send_rim(window_output, token_rows)
    prior = jnp.stack([earlier_keys, earlier_values])
    border_tokens = jnp.where(lax.axis_index("ctx") == 0, prior, received)
    padded_rows = jnp.concatenate([border_tokens, window_output], axis=1)
    return attend(normed, weight_rows, qkv_bias[None, :query_length], padded_rows, tables, sinks)


def solution(mesh):
    placed = (
        P(("dp", "ctx"), None),
        P(("dp", "ctx")),
        P(),
        P(None, "ctx"),
        P(),
        P(),
        P("dp", None),
        P("dp", None),
    )
    return jax.shard_map(
        on_device, mesh=mesh, in_specs=placed, out_specs=P(("dp", "ctx"), None), check_vma=False
    )
```

```python
import jax
import jax.numpy as jnp
from jax import lax
from jax.experimental import pallas as pl
from jax.experimental.pallas import tpu as pltpu
from jax.sharding import PartitionSpec as P

QUERY_HEADS = 32
KEY_VALUE_HEADS = 4
HEAD_SIZE = 64
WINDOW_TOKENS = 128


def shifted(value, axis, steps):
    count = lax.axis_size(axis)
    leading, last = (max(0, -steps), min(count, count - steps))
    return lax.ppermute(value, axis, [(source, source + steps) for source in range(leading, last)])


def apply_rotation(heads, positions):
    half = heads.shape[-1] // 2
    freq = 150000.0 ** (-(jnp.arange(half, dtype=jnp.float32) * 2.0 / heads.shape[-1]))
    angle = positions.astype(jnp.float32)[:, None] * freq[None, :]
    cosine = jnp.cos(angle)[:, None, :]
    sine = jnp.sin(angle)[:, None, :]
    first = heads[..., :half]
    second = heads[..., half:]
    return jnp.concatenate(
        [first * cosine - second * sine, second * cosine + first * sine], axis=-1
    )


def attend_head(query_rows, key_rows, value_rows, sink_row, visible):
    scores = jnp.einsum(
        "nrgd,nkd->ngrk", query_rows, key_rows, preferred_element_type=jnp.float32
    ) * HEAD_SIZE ** (-0.5)
    scores = jnp.where(visible[:, None], scores, -1e30)
    top = jnp.maximum(jnp.max(scores, axis=-1), sink_row[None, :, None])
    expo = jnp.exp(scores - top[..., None])
    total = jnp.sum(expo, axis=-1) + jnp.exp(sink_row[None, :, None] - top)
    probs = (expo / total[..., None]).astype(jnp.bfloat16)
    out = jnp.einsum("ngrk,nkd->nrgd", probs, value_rows, preferred_element_type=jnp.float32)
    return out.astype(jnp.bfloat16)


def attention_kernel(
    sinks_ref, limit_ref, cos_ref, sin_ref, normed_ref, weight_ref, bias_ref, k_ref, v_ref, out_ref
):
    group = pl.program_id(0)
    queries_all = lax.dot_general(
        normed_ref[...], weight_ref[...], (((1,), (1,)), ((), ())), preferred_element_type=jnp.float32
    )
    queries_all = queries_all + bias_ref[...]
    rows = queries_all.shape[0]
    query_group = queries_all.shape[1] // HEAD_SIZE
    half = HEAD_SIZE // 2
    lanes = cos_ref.shape[1]
    cosine = cos_ref[...]
    sine = sin_ref[...]
    lane = lax.broadcasted_iota(jnp.int32, (rows, lanes), 1)
    source = pltpu.roll(lane, half, 1)
    partner_lane = jnp.where(lane % HEAD_SIZE < half, lane + half, lane - half)
    take_first = source == partner_lane
    block = WINDOW_TOKENS
    query_index = lax.broadcasted_iota(jnp.int32, (block, 2 * block), 0)
    key_index = lax.broadcasted_iota(jnp.int32, (block, 2 * block), 1)
    rel = query_index - key_index + block
    visible = []
    for part in range(rows // block):
        limit = limit_ref[part * block : (part + 1) * block, :]
        visible.append((rel >= 0) & (rel <= limit))
    heads_per_chunk = lanes // HEAD_SIZE
    pick_first = group % 2 == 0
    window_keys = []
    window_values = []
    for part in range(rows // block):
        key_block = k_ref[part * block : part * block + 2 * block, :]
        value_block = v_ref[part * block : part * block + 2 * block, :]
        window_keys.append(jnp.where(pick_first, key_block[:, :HEAD_SIZE], key_block[:, HEAD_SIZE:]))
        window_values.append(jnp.where(pick_first, value_block[:, :HEAD_SIZE], value_block[:, HEAD_SIZE:]))
    for chunk in range(queries_all.shape[1] // lanes):
        x = queries_all[:, chunk * lanes : (chunk + 1) * lanes]
        first = pltpu.roll(x, half, 1)
        second = pltpu.roll(x, lanes - half, 1)
        partner = jnp.where(take_first, first, second)
        rotated = ((x * cosine + partner * sine) * HEAD_SIZE ** (-0.5)).astype(jnp.bfloat16)
        for inner in range(heads_per_chunk):
            head = chunk * heads_per_chunk + inner
            sink = sinks_ref[group * query_group + head]
            query_head = rotated[:, inner * HEAD_SIZE : (inner + 1) * HEAD_SIZE]
            for part in range(rows // block):
                queries = query_head[part * block : (part + 1) * block]
                keys = window_keys[part]
                values = window_values[part]
                scores = lax.dot_general(
                    queries, keys, (((1,), (1,)), ((), ())), preferred_element_type=jnp.float32
                )
                scores = jnp.where(visible[part], scores, -1e30)
                top = jnp.maximum(jnp.max(scores, axis=1, keepdims=True), sink)
                expo = jnp.exp(scores - top)
                total = jnp.sum(expo, axis=1, keepdims=True) + jnp.exp(sink - top)
                probs = (expo * (1.0 / total)).astype(jnp.bfloat16)
                out = jnp.dot(probs, values, preferred_element_type=jnp.float32)
                out_ref[part * block : (part + 1) * block, head * HEAD_SIZE : (head + 1) * HEAD_SIZE] = out.astype(
                    jnp.bfloat16
                )


def rotation_tables(positions, lanes):
    half = HEAD_SIZE // 2
    freq = 150000.0 ** (-(jnp.arange(half, dtype=jnp.float32) * 2.0 / HEAD_SIZE))
    repeats = lanes // half
    lane_freq = jnp.tile(freq, repeats)
    sign = jnp.tile(jnp.concatenate([-jnp.ones(half), jnp.ones(half)]).astype(jnp.float32), lanes // HEAD_SIZE)
    angle = positions.astype(jnp.float32)[:, None] * lane_freq[None, :]
    return jnp.cos(angle), sign[None, :] * jnp.sin(angle)


def attend(normed, weight_rows, query_bias, joined_rows, tables, sinks):
    token_rows = normed.shape[0]
    model_width = normed.shape[1]
    query_group = QUERY_HEADS // KEY_VALUE_HEADS
    group_width = query_group * HEAD_SIZE
    cos_table, sin_table, limit = tables
    lanes = cos_table.shape[1]
    key_rows = joined_rows.shape[1]
    return pl.pallas_call(
        attention_kernel,
        grid=(KEY_VALUE_HEADS,),
        in_specs=[
            pl.BlockSpec(memory_space=pltpu.SMEM),
            pl.BlockSpec((token_rows, 1), lambda g: (0, 0)),
            pl.BlockSpec((token_rows, lanes), lambda g: (0, 0)),
            pl.BlockSpec((token_rows, lanes), lambda g: (0, 0)),
            pl.BlockSpec((token_rows, model_width), lambda g: (0, 0)),
            pl.BlockSpec((group_width, model_width), lambda g: (g, 0)),
            pl.BlockSpec((1, group_width), lambda g: (0, g)),
            pl.BlockSpec((None, key_rows, 2 * HEAD_SIZE), lambda g: (0, 0, g // 2)),
            pl.BlockSpec((None, key_rows, 2 * HEAD_SIZE), lambda g: (1, 0, g // 2)),
        ],
        out_specs=pl.BlockSpec((token_rows, group_width), lambda g: (0, g)),
        out_shape=jax.ShapeDtypeStruct((token_rows, QUERY_HEADS * HEAD_SIZE), jnp.bfloat16),
    )(sinks, limit, cos_table, sin_table, normed, weight_rows, query_bias, joined_rows, joined_rows)


def send_rim(window_output, token_rows):
    return shifted(window_output[:, token_rows - WINDOW_TOKENS :], "ctx", 1)


def split_mixed(combined_output, positions, token_rows, query_length, key_length):
    key_rows = apply_rotation(
        combined_output[:, query_length : query_length + key_length].reshape(
            token_rows, KEY_VALUE_HEADS, HEAD_SIZE
        ),
        positions,
    ).astype(jnp.bfloat16)
    value_rows = combined_output[:, query_length + key_length :].astype(jnp.bfloat16)
    window_output = jnp.stack([key_rows.reshape(token_rows, key_length), value_rows])
    received = send_rim(window_output, token_rows)
    query_rows = apply_rotation(
        combined_output[:, :query_length].reshape(token_rows, QUERY_HEADS, HEAD_SIZE), positions
    ).astype(jnp.bfloat16)
    return (window_output, received, query_rows)


def gather_weight(qkv_weight):
    pairs = lax.axis_size("dp")
    columns = qkv_weight.shape[1]
    if columns % pairs:
        return lax.all_gather(qkv_weight.T, "ctx", axis=0, tiled=True)
    piece = columns // pairs
    own = lax.dynamic_slice_in_dim(qkv_weight, lax.axis_index("dp") * piece, piece, axis=1)
    return lax.all_gather(own.T, ("ctx", "dp"), axis=0, tiled=True)


def on_device(
    tokens, positions, norm_gain, qkv_weight, qkv_bias, sinks, earlier_keys, earlier_values
):
    token_rows = tokens.shape[0]
    query_group = QUERY_HEADS // KEY_VALUE_HEADS
    query_length = QUERY_HEADS * HEAD_SIZE
    key_length = KEY_VALUE_HEADS * HEAD_SIZE
    flat = tokens.astype(jnp.float32)
    scale = lax.rsqrt(jnp.mean(flat * flat, axis=-1, keepdims=True) + 1e-05)
    normed = (flat * scale * norm_gain[None, :]).astype(jnp.bfloat16)
    tables = rotation_tables(positions, 128) + (
        jnp.minimum(positions, WINDOW_TOKENS - 1).astype(jnp.int32)[:, None],
    )
    normed, tables = lax.optimization_barrier((normed, tables))
    weight_rows = gather_weight(qkv_weight)
    def key_value_rows(rows):
        output = lax.dot_general(
            normed[rows],
            weight_rows[query_length:],
            (((1,), (1,)), ((), ())),
            preferred_element_type=jnp.float32,
        )
        output = output + qkv_bias[None, query_length:]
        count = output.shape[0]
        keys = apply_rotation(
            output[:, :key_length].reshape(count, KEY_VALUE_HEADS, HEAD_SIZE), positions[rows]
        ).astype(jnp.bfloat16)
        values = output[:, key_length:].astype(jnp.bfloat16)
        return jnp.stack([keys.reshape(count, key_length), values])

    late_rows = key_value_rows(slice(token_rows - WINDOW_TOKENS, token_rows))
    received = shifted(late_rows, "ctx", 1)
    early_rows = key_value_rows(slice(0, token_rows - WINDOW_TOKENS))
    window_output = jnp.concatenate([early_rows, late_rows], axis=1)
    prior = jnp.stack([earlier_keys, earlier_values])
    border_tokens = jnp.where(lax.axis_index("ctx") == 0, prior, received)
    padded_rows = jnp.concatenate([border_tokens, window_output], axis=1)
    return attend(normed, weight_rows, qkv_bias[None, :query_length], padded_rows, tables, sinks)


def solution(mesh):
    placed = (
        P(("dp", "ctx"), None),
        P(("dp", "ctx")),
        P(),
        P(None, "ctx"),
        P(),
        P(),
        P("dp", None),
        P("dp", None),
    )
    return jax.shard_map(
        on_device, mesh=mesh, in_specs=placed, out_specs=P(("dp", "ctx"), None), check_vma=False
    )
```
